32 devices in a mesh: tm: 8 (over z, x), row: 4 (over y, core).
Axes of the slice: x: 2, y: 2, z: 4, core: 2. Of those that a mesh axis runs over, the one named last changes fastest.
Arguments:
- coupling: bfloat16 [8, 4096, 2048], P('tm', 'row'), as said below
- row_scale: float32 [8, 4096], P('tm', 'row'), may hold values from 0.1 to 10
- block_mask: int32 [8, 32, 16], P('tm', 'row'), may hold values 0 or 1
- link_map: int32 [8, 16], P('tm'), may hold values from 0 to 15, each once within a row
- tile_order: int32 [16], replicated, may hold values from 0 to 15, each once
- link_diag: float32 [8, 2048], P('tm'), may hold values from 0.1 to 1
Outputs:
- schur_rows: float32 [8, 2048, 2048], P('tm', 'row')
- chain_complement: float32 [8, 3, 128, 128], P('tm')
The draws below stay inside these ranges and needn't reach their ends.
Inputs may be any that keep to these rules, and one draw needn't show every extreme that they name: `coupling`: entries lie within 6 / sqrt(4096) of zero. Each row of link_map lists every linking block once. tile_order lists every linking block once.
All inputs are finite; a program needn't handle non-finite values. No bound on the sum of `block_mask` on one device may be relied on, other than what follows from the above.
Results may differ from the reference program's by a relative error of at most 0.0011.
Values may be sent and summed in bfloat16 or wider, within the bound.
No kernel may reach another device: no remote copies, remote signals or barrier semaphores. Data moves between devices by JAX's collectives and lax.ppermute only.
A program may use at most 128 MiB of HBM per device.

```python
import math
import jax
import jax.numpy as jnp
from jax import lax

L = 2048
BLK = 128
NB = 16
ROWS = 4096
TIMES = 8


def draw_coupling(key, part):
    factor_count = max(L // 32, 4)
    key_rows = jax.random.fold_in(key, 11)
    key_cols = jax.random.fold_in(key, 12)
    key_noise = jax.random.fold_in(key, 13)
    row_factors = jax.random.normal(key_rows, (TIMES, ROWS, factor_count), jnp.float32)
    col_factors = jax.random.normal(key_cols, (TIMES, factor_count, L), jnp.float32)
    noise_part = jax.random.normal(key_noise, (TIMES, ROWS, L), jnp.float32)
    common = jnp.einsum('trk,tkc->trc', row_factors, col_factors, precision=lax.Precision.HIGHEST)
    common = common * (1.0 / math.sqrt(factor_count))
    blended = math.sqrt(0.75) * common + 0.5 * noise_part
    blended = jnp.clip(blended, -6.0, 6.0) * (1.0 / math.sqrt(ROWS))
    return blended.astype(jnp.bfloat16)


def touch_ends(array, own_key, least, top_value):
    extent = array.shape
    place = [jax.random.randint(jax.random.fold_in(own_key, axis), (), 0, extent[axis]) for axis in range(len(extent))]
    array = array.at[tuple(place)].set(least)
    longest = extent.index(max(extent))
    place[longest] = (place[longest] + 1) % extent[longest]
    return array.at[tuple(place)].set(top_value)


def block_scale(rng, dims, split, smallest, top_value):
    def one(dim, blocks):
        draws = jax.random.uniform(jax.random.fold_in(jax.random.fold_in(rng, 6), dim), (blocks,), jnp.float32, smallest / len(split), top_value / len(split))
        return jnp.repeat(jnp.exp(draws), dims[dim] // blocks).reshape((-1,) + (1,) * (len(dims) - dim - 1))

    loudness = one(*split[0])
    for cut in split[1:]:
        loudness = loudness * one(*cut)
    return loudness


def setup_inputs(seed: int = 0) -> dict:
    keys = jax.random.split(jax.random.key(seed), 7)
    return {
        "coupling": draw_coupling(jax.random.fold_in(keys[6], 71), 0),
        "row_scale": jnp.clip(jnp.exp(math.log(10.0) - 4.6051702 * jax.random.uniform(keys[1], (TIMES, ROWS), jnp.float32) ** block_scale(keys[1], (TIMES, ROWS), ((0, 8), (1, 4)), -0.2, 0.2)), 0.1, 10.0),
        "block_mask": touch_ends((jax.random.randint(keys[2], (TIMES, ROWS // BLK, NB), 0, 2) < 1).astype(jnp.int32), jax.random.fold_in(keys[2], 1), 0, 1),
        "link_map": jax.vmap(lambda own: jax.random.permutation(own, NB))(jax.random.split(keys[3], TIMES)).reshape((TIMES, NB)).astype(jnp.int32),
        "tile_order": jax.random.permutation(keys[4], NB).astype(jnp.int32),
        "link_diag": jnp.clip(jnp.exp(math.log(1.0) - 2.3025851 * jax.random.uniform(keys[5], (TIMES, L), jnp.float32) ** block_scale(keys[5], (TIMES, L), ((0, 8),), -0.2, 0.2)), 0.1, 1.0),
    }


HIGHEST = lax.Precision.HIGHEST

def join_segments(earlier_seg, later_seg):
    top_one, cross_one, bottom_one, empty_one = earlier_seg
    top_two, cross_two, bottom_two, empty_two = later_seg
    both_empty = empty_one * empty_two
    middle = bottom_one + top_two
    middle = 0.5 * (middle + middle.T) + both_empty * jnp.eye(middle.shape[0], dtype=jnp.float32)
    factor = jnp.linalg.cholesky(middle)
    half_width = top_one.shape[0]
    solved = jax.scipy.linalg.cho_solve((factor, True), jnp.concatenate([cross_one.T, cross_two], axis=1))
    solve_one = solved[:, :half_width]
    solve_two = solved[:, half_width:]
    top_new = top_one - jnp.dot(cross_one, solve_one, precision=HIGHEST)
    cross_new = -jnp.dot(cross_one, solve_two, precision=HIGHEST)
    bottom_new = bottom_two - jnp.dot(cross_two.T, solve_two, precision=HIGHEST)
    first_empty = empty_one > 0.5
    second_empty = empty_two > 0.5
    top_out = jnp.where(first_empty, top_two, jnp.where(second_empty, top_one, top_new))
    cross_out = jnp.where(first_empty, cross_two, jnp.where(second_empty, cross_one, cross_new))
    bottom_out = jnp.where(first_empty, bottom_two, jnp.where(second_empty, bottom_one, bottom_new))
    return (top_out, cross_out, bottom_out, both_empty)

def schur_of_block(local_slab, row_weights, live_blocks, block_map, diagonal):
    slab_height = local_slab.shape[0]
    block_count = L // BLK
    masked = (local_slab.reshape(slab_height // BLK, BLK, block_count, BLK) * live_blocks.astype(jnp.bfloat16)[:, None, :, None]).reshape(slab_height, block_count, BLK)
    block_ids = jnp.arange(block_count, dtype=jnp.int32)
    source = jnp.sum(block_ids[None, :] * (block_map[None, :] == block_ids[:, None]).astype(jnp.int32), axis=1)
    global_cols = jnp.take(masked, source, axis=1).reshape(slab_height, L)
    scaled = (row_weights[:, None] * global_cols.astype(jnp.float32)).astype(jnp.bfloat16)
    gram_matrix = jnp.dot(global_cols.T.astype(jnp.float32), scaled.astype(jnp.float32), preferred_element_type=jnp.float32)
    return gram_matrix + jnp.diag(diagonal)

def reference(coupling, row_scale, block_mask, link_map, tile_order, link_diag):
    block_count = L // BLK

    def per_block(block_items):
        gram_matrix = schur_of_block(*block_items)
        ordered = jnp.take(gram_matrix.reshape(block_count, BLK, L), tile_order, axis=0).reshape(L, L)
        pieces = jnp.stack([gram_matrix[:BLK, :BLK], gram_matrix[:BLK, L - BLK:], gram_matrix[L - BLK:, L - BLK:]])
        return (ordered, pieces)
    schur_rows, segments = lax.map(per_block, (coupling, row_scale, block_mask, link_map, link_diag))
    zero_block = jnp.zeros((BLK, BLK), jnp.float32)
    running = (zero_block, zero_block, zero_block, jnp.ones((), jnp.float32))
    stacked = []
    for moment in range(TIMES):
        own_segment = (segments[moment, 0], segments[moment, 1], segments[moment, 2], jnp.zeros((), jnp.float32))
        running = join_segments(running, own_segment)
        stacked.append(jnp.stack(running[:3]))
    return (schur_rows, jnp.stack(stacked))
```

```python
import jax
import jax.numpy as jnp
from jax import lax
from jax.sharding import PartitionSpec as P

L = 2048
BLK = 128


HIGHEST = lax.Precision.HIGHEST


def join_segments(earlier_seg, later_seg):
    top_one, cross_one, bottom_one = earlier_seg
    top_two, cross_two, bottom_two = later_seg
    middle = bottom_one + top_two
    middle = 0.5 * (middle + middle.T)
    factor = jnp.linalg.cholesky(middle)
    half_width = top_one.shape[0]
    solved = jax.scipy.linalg.cho_solve(
        (factor, True), jnp.concatenate([cross_one.T, cross_two], axis=1)
    )
    solve_one = solved[:, :half_width]
    solve_two = solved[:, half_width:]
    top_new = top_one - jnp.dot(cross_one, solve_one, precision=HIGHEST)
    cross_new = -jnp.dot(cross_one, solve_two, precision=HIGHEST)
    bottom_new = bottom_two - jnp.dot(cross_two.T, solve_two, precision=HIGHEST)
    return (top_new, cross_new, bottom_new)


def contract_rows(left_cols, right_cols):
    return lax.dot_general(
        left_cols, right_cols, (((0,), (0,)), ((), ())), preferred_element_type=jnp.float32
    )


def local(coupling, row_scale, block_mask, link_map, tile_order, link_diag):
    local_slab = coupling[0]
    row_weights = row_scale[0]
    live_blocks = block_mask[0]
    block_map = link_map[0]
    diagonal = link_diag[0]
    slab_height = local_slab.shape[0]
    block_count = L // BLK
    owners = lax.axis_size("row")
    own_blocks = block_count // owners
    own_rows = own_blocks * BLK
    my_index = lax.axis_index("row")
    block_ids = jnp.arange(block_count, dtype=jnp.int32)
    source = jnp.sum(
        block_ids[None, :] * (block_map[None, :] == block_ids[:, None]).astype(jnp.int32), axis=1
    )

    def edge_cols(global_block):
        local_block = source[global_block]
        cols = lax.dynamic_slice_in_dim(local_slab, local_block * BLK, BLK, axis=1)
        live = lax.dynamic_index_in_dim(live_blocks, local_block, 1, False)
        cols = (cols.reshape(slab_height // BLK, BLK, BLK) * live.astype(jnp.bfloat16)[:, None, None])
        cols = cols.reshape(slab_height, BLK)
        weighted = (row_weights[:, None] * cols.astype(jnp.float32)).astype(jnp.bfloat16)
        return cols, weighted

    first_cols, first_scaled = edge_cols(0)
    final_cols, final_scaled = edge_cols(block_count - 1)
    part_pieces = jnp.stack(
        [
            contract_rows(first_cols, first_scaled),
            contract_rows(first_cols, final_scaled),
            contract_rows(final_cols, final_scaled),
        ]
    )
    summed = lax.psum(part_pieces, "row")
    eye = jnp.eye(BLK, dtype=jnp.float32)
    segment = (
        summed[0] + eye * diagonal[:BLK][None, :],
        summed[1],
        summed[2] + eye * diagonal[L - BLK :][None, :],
    )

    times = lax.axis_size("tm")
    position = lax.axis_index("tm")
    running = segment
    shift = 1
    while shift < times:
        pairs = [(src, src + shift) for src in range(times - shift)]
        earlier = tuple(lax.ppermute(piece, "tm", pairs) for piece in running)
        joined = join_segments(earlier, running)
        take = position >= shift
        running = tuple(jnp.where(take, new, old) for new, old in zip(joined, running))
        shift *= 2
    chain_out = jnp.stack(running)[None]

    masked = (
        local_slab.reshape(slab_height // BLK, BLK, block_count, BLK)
        * live_blocks.astype(jnp.bfloat16)[:, None, :, None]
    ).reshape(slab_height, block_count, BLK)
    global_cols = jnp.take(masked, source, axis=1).reshape(slab_height, L)
    my_blocks = lax.dynamic_slice_in_dim(tile_order, my_index * own_blocks, own_blocks)
    left_cols = jnp.take(masked, jnp.take(source, tile_order), axis=1).reshape(slab_height, L)
    scaled = (row_weights[:, None] * global_cols.astype(jnp.float32)).astype(jnp.bfloat16)
    owned = lax.psum_scatter(
        contract_rows(left_cols, scaled), "row", scatter_dimension=0, tiled=True
    )
    local_rows = jnp.arange(own_rows, dtype=jnp.int32)
    target = jnp.repeat(my_blocks, BLK) * BLK + local_rows % BLK
    column_ids = jnp.arange(L, dtype=jnp.int32)
    owned = owned + jnp.where(
        column_ids[None, :] == target[:, None], jnp.take(diagonal, target)[:, None], 0.0
    )
    return (owned[None], chain_out)


def solution(mesh):
    placed = (
        P("tm", "row", None),
        P("tm", "row"),
        P("tm", "row", None),
        P("tm", None),
        P(),
        P("tm", None),
    )
    return jax.shard_map(
        local,
        mesh=mesh,
        in_specs=placed,
        out_specs=(P("tm", "row", None), P("tm", None, None, None)),
        check_vma=False,
    )
```

```python
import jax
import jax.numpy as jnp
from jax import lax
from jax.sharding import PartitionSpec as P
from jax.experimental import pallas as pl
from jax.experimental.pallas import tpu as pltpu

L = 2048
BLK = 128


def gram_kernel(src_left, src_right, tile_ref, mask_ref, flag_ref, g_ref, w_ref, diag_ref,
                out_ref, s_ref, lt_ref):
    k = pl.program_id(0)
    row_blocks = g_ref.shape[0] // BLK
    col_blocks = g_ref.shape[1] // BLK

    @pl.when(k == 0)
    def _():
        def fill(j, carry):
            src = src_right[j]
            c0 = pl.multiple_of(src * BLK, BLK)
            d0 = pl.multiple_of(j * BLK, BLK)
            for rb in range(row_blocks):
                live = mask_ref[rb * col_blocks + src].astype(jnp.float32)
                vals = g_ref[rb * BLK:(rb + 1) * BLK, pl.ds(c0, BLK)].astype(jnp.float32)
                wts = w_ref[rb * BLK:(rb + 1) * BLK, :]
                s_ref[rb * BLK:(rb + 1) * BLK, pl.ds(d0, BLK)] = (wts * (vals * live)).astype(jnp.bfloat16)
            return carry
        lax.fori_loop(0, col_blocks, fill, 0)

    src = src_left[k]
    c0 = pl.multiple_of(src * BLK, BLK)
    for rb in range(row_blocks):
        live = mask_ref[rb * col_blocks + src].astype(jnp.float32)
        vals = g_ref[rb * BLK:(rb + 1) * BLK, pl.ds(c0, BLK)].astype(jnp.float32) * live
        lt_ref[:, rb * BLK:(rb + 1) * BLK] = vals.T.astype(jnp.bfloat16)
    out_ref[...] = jnp.dot(lt_ref[...], s_ref[...], preferred_element_type=jnp.float32)
    blk = tile_ref[k]
    e0 = pl.multiple_of(blk * BLK, BLK)
    rows = lax.broadcasted_iota(jnp.int32, (BLK, BLK), 0)
    cols = lax.broadcasted_iota(jnp.int32, (BLK, BLK), 1)
    dvals = diag_ref[pl.ds(blk, 1), :] * flag_ref[0].astype(jnp.float32)
    out_ref[:, pl.ds(e0, BLK)] += jnp.where(rows == cols, dvals, 0.0)


def gram_rows(slab, weights, live_blocks, src_left, src_right, tile_order, diagonal, flag):
    height = slab.shape[0]
    col_blocks = L // BLK
    grid_spec = pltpu.PrefetchScalarGridSpec(
        num_scalar_prefetch=5,
        grid=(col_blocks,),
        in_specs=[
            pl.BlockSpec((height, L), lambda k, *_: (0, 0)),
            pl.BlockSpec((height, 1), lambda k, *_: (0, 0)),
            pl.BlockSpec((col_blocks, BLK), lambda k, *_: (0, 0)),
        ],
        out_specs=pl.BlockSpec((BLK, L), lambda k, *_: (k, 0)),
        scratch_shapes=[pltpu.VMEM((height, L), jnp.bfloat16), pltpu.VMEM((BLK, height), jnp.bfloat16)],
    )
    return pl.pallas_call(
        gram_kernel,
        grid_spec=grid_spec,
        out_shape=jax.ShapeDtypeStruct((L, L), jnp.float32),
        compiler_params=pltpu.CompilerParams(vmem_limit_bytes=56 * 1024 * 1024),
    )(src_left, src_right, tile_order, live_blocks.reshape(-1), flag.reshape(1),
      slab, weights.reshape(height, 1), diagonal.reshape(col_blocks, BLK))


HIGHEST = lax.Precision.HIGHEST


def join_segments(earlier_seg, later_seg):
    top_one, cross_one, bottom_one = earlier_seg
    top_two, cross_two, bottom_two = later_seg
    middle = bottom_one + top_two
    middle = 0.5 * (middle + middle.T)
    factor = jnp.linalg.cholesky(middle)
    half_width = top_one.shape[0]
    solved = jax.scipy.linalg.cho_solve(
        (factor, True), jnp.concatenate([cross_one.T, cross_two], axis=1)
    )
    solve_one = solved[:, :half_width]
    solve_two = solved[:, half_width:]
    top_new = top_one - jnp.dot(cross_one, solve_one, precision=HIGHEST)
    cross_new = -jnp.dot(cross_one, solve_two, precision=HIGHEST)
    bottom_new = bottom_two - jnp.dot(cross_two.T, solve_two, precision=HIGHEST)
    return (top_new, cross_new, bottom_new)


def contract_rows(left_cols, right_cols):
    return lax.dot_general(
        left_cols, right_cols, (((0,), (0,)), ((), ())), preferred_element_type=jnp.float32
    )


def local(coupling, row_scale, block_mask, link_map, tile_order, link_diag):
    local_slab = coupling[0]
    row_weights = row_scale[0]
    live_blocks = block_mask[0]
    block_map = link_map[0]
    diagonal = link_diag[0]
    slab_height = local_slab.shape[0]
    block_count = L // BLK
    my_index = lax.axis_index("row")
    block_ids = jnp.arange(block_count, dtype=jnp.int32)
    source = jnp.sum(
        block_ids[None, :] * (block_map[None, :] == block_ids[:, None]).astype(jnp.int32), axis=1
    )

    def edge_cols(global_block):
        local_block = source[global_block]
        cols = lax.dynamic_slice_in_dim(local_slab, local_block * BLK, BLK, axis=1)
        live = lax.dynamic_index_in_dim(live_blocks, local_block, 1, False)
        cols = (cols.reshape(slab_height // BLK, BLK, BLK) * live.astype(jnp.bfloat16)[:, None, None])
        cols = cols.reshape(slab_height, BLK)
        weighted = (row_weights[:, None] * cols.astype(jnp.float32)).astype(jnp.bfloat16)
        return cols, weighted

    first_cols, first_scaled = edge_cols(0)
    final_cols, final_scaled = edge_cols(block_count - 1)
    part_pieces = jnp.stack(
        [
            contract_rows(first_cols, first_scaled),
            contract_rows(first_cols, final_scaled),
            contract_rows(final_cols, final_scaled),
        ]
    )
    summed = lax.psum(part_pieces, "row")
    eye = jnp.eye(BLK, dtype=jnp.float32)
    segment = (
        summed[0] + eye * diagonal[:BLK][None, :],
        summed[1],
        summed[2] + eye * diagonal[L - BLK :][None, :],
    )

    times = lax.axis_size("tm")
    position = lax.axis_index("tm")
    running = segment
    shift = 1
    while shift < times:
        pairs = [(src, src + shift) for src in range(times - shift)]
        moved = lax.ppermute(jnp.stack(running), "tm", pairs)
        earlier = (moved[0], moved[1], moved[2])
        joined = join_segments(earlier, running)
        take = position >= shift
        running = tuple(jnp.where(take, new, old) for new, old in zip(joined, running))
        shift *= 2
    chain_out = jnp.stack(running)[None]

    flag = (my_index == 0).astype(jnp.int32)
    partial = gram_rows(
        local_slab, row_weights, live_blocks, jnp.take(source, tile_order), source,
        tile_order, diagonal, flag,
    )
    owned = lax.psum_scatter(partial, "row", scatter_dimension=0, tiled=True)
    return (owned[None], chain_out)


def solution(mesh):
    placed = (
        P("tm", "row", None),
        P("tm", "row"),
        P("tm", "row", None),
        P("tm", None),
        P(),
        P("tm", None),
    )
    return jax.shard_map(
        local,
        mesh=mesh,
        in_specs=placed,
        out_specs=(P("tm", "row", None), P("tm", None, None, None)),
        check_vma=False,
    )
```

```python
import jax
import jax.numpy as jnp
from jax import lax
from jax.sharding import PartitionSpec as P
from jax.experimental import pallas as pl
from jax.experimental.pallas import tpu as pltpu

L = 2048
BLK = 128


def contrib_kernel(src_left, src_right, tile_ref, mask_ref, flag_ref, g_ref, w_ref, diag_ref, *rest):
    if len(rest) == 4:
        acc_ref, out_ref, s_ref, lt_ref = rest
    else:
        acc_ref = None
        out_ref, s_ref, lt_ref = rest
    k = pl.program_id(0)
    row_blocks = g_ref.shape[0] // BLK
    col_blocks = g_ref.shape[1] // BLK

    @pl.when(k == 0)
    def _():
        def fill(j, carry):
            src = src_right[j]
            c0 = pl.multiple_of(src * BLK, BLK)
            d0 = pl.multiple_of(j * BLK, BLK)
            for rb in range(row_blocks):
                live = mask_ref[rb * col_blocks + src].astype(jnp.float32)
                vals = g_ref[rb * BLK:(rb + 1) * BLK, pl.ds(c0, BLK)].astype(jnp.float32)
                wts = w_ref[rb * BLK:(rb + 1) * BLK, :]
                s_ref[rb * BLK:(rb + 1) * BLK, pl.ds(d0, BLK)] = (wts * (vals * live)).astype(jnp.bfloat16)
            return carry
        lax.fori_loop(0, col_blocks, fill, 0)

    src = src_left[k]
    c0 = pl.multiple_of(src * BLK, BLK)
    for rb in range(row_blocks):
        live = mask_ref[rb * col_blocks + src].astype(jnp.float32)
        vals = g_ref[rb * BLK:(rb + 1) * BLK, pl.ds(c0, BLK)].astype(jnp.float32) * live
        lt_ref[:, rb * BLK:(rb + 1) * BLK] = vals.T.astype(jnp.bfloat16)
    term = jnp.dot(lt_ref[...], s_ref[...], preferred_element_type=jnp.float32)
    if acc_ref is None:
        out_ref[...] = term
        blk = tile_ref[k]
        e0 = pl.multiple_of(blk * BLK, BLK)
        rows = lax.broadcasted_iota(jnp.int32, (BLK, BLK), 0)
        cols = lax.broadcasted_iota(jnp.int32, (BLK, BLK), 1)
        dvals = diag_ref[pl.ds(blk, 1), :] * flag_ref[0].astype(jnp.float32)
        out_ref[:, pl.ds(e0, BLK)] += jnp.where(rows == cols, dvals, 0.0)
    else:
        out_ref[...] = acc_ref[...] + term


def gram_contrib(slab, weights, live_blocks, src_left, src_right, own_tiles, diagonal, acc=None):
    height = slab.shape[0]
    col_blocks = L // BLK
    out_blocks = src_left.shape[0]
    in_specs = [
        pl.BlockSpec((height, L), lambda k, *_: (0, 0)),
        pl.BlockSpec((height, 1), lambda k, *_: (0, 0)),
        pl.BlockSpec((col_blocks, BLK), lambda k, *_: (0, 0)),
    ]
    operands = [slab, weights.reshape(height, 1), diagonal.reshape(col_blocks, BLK)]
    aliases = {}
    if acc is not None:
        in_specs.append(pl.BlockSpec((BLK, L), lambda k, *_: (k, 0)))
        operands.append(acc)
        aliases = {8: 0}
    grid_spec = pltpu.PrefetchScalarGridSpec(
        num_scalar_prefetch=5,
        grid=(out_blocks,),
        in_specs=in_specs,
        out_specs=pl.BlockSpec((BLK, L), lambda k, *_: (k, 0)),
        scratch_shapes=[pltpu.VMEM((height, L), jnp.bfloat16), pltpu.VMEM((BLK, height), jnp.bfloat16)],
    )
    return pl.pallas_call(
        contrib_kernel,
        grid_spec=grid_spec,
        out_shape=jax.ShapeDtypeStruct((out_blocks * BLK, L), jnp.float32),
        input_output_aliases=aliases,
        compiler_params=pltpu.CompilerParams(vmem_limit_bytes=56 * 1024 * 1024),
    )(src_left, src_right, own_tiles, live_blocks.reshape(-1), jnp.ones((1,), jnp.int32), *operands)


HIGHEST = lax.Precision.HIGHEST


def join_segments(earlier_seg, later_seg):
    top_one, cross_one, bottom_one = earlier_seg
    top_two, cross_two, bottom_two = later_seg
    middle = bottom_one + top_two
    middle = 0.5 * (middle + middle.T)
    factor = jnp.linalg.cholesky(middle)
    half_width = top_one.shape[0]
    solved = jax.scipy.linalg.cho_solve(
        (factor, True), jnp.concatenate([cross_one.T, cross_two], axis=1)
    )
    solve_one = solved[:, :half_width]
    solve_two = solved[:, half_width:]
    top_new = top_one - jnp.dot(cross_one, solve_one, precision=HIGHEST)
    cross_new = -jnp.dot(cross_one, solve_two, precision=HIGHEST)
    bottom_new = bottom_two - jnp.dot(cross_two.T, solve_two, precision=HIGHEST)
    return (top_new, cross_new, bottom_new)


def contract_rows(left_cols, right_cols):
    return lax.dot_general(
        left_cols, right_cols, (((0,), (0,)), ((), ())), preferred_element_type=jnp.float32
    )


def local(coupling, row_scale, block_mask, link_map, tile_order, link_diag):
    local_slab = coupling[0]
    row_weights = row_scale[0]
    live_blocks = block_mask[0]
    block_map = link_map[0]
    diagonal = link_diag[0]
    slab_height = local_slab.shape[0]
    block_count = L // BLK
    my_index = lax.axis_index("row")
    block_ids = jnp.arange(block_count, dtype=jnp.int32)
    source = jnp.sum(
        block_ids[None, :] * (block_map[None, :] == block_ids[:, None]).astype(jnp.int32), axis=1
    )

    def edge_cols(global_block):
        local_block = source[global_block]
        cols = lax.dynamic_slice_in_dim(local_slab, local_block * BLK, BLK, axis=1)
        live = lax.dynamic_index_in_dim(live_blocks, local_block, 1, False)
        cols = (cols.reshape(slab_height // BLK, BLK, BLK) * live.astype(jnp.bfloat16)[:, None, None])
        cols = cols.reshape(slab_height, BLK)
        weighted = (row_weights[:, None] * cols.astype(jnp.float32)).astype(jnp.bfloat16)
        return cols, weighted

    first_cols, first_scaled = edge_cols(0)
    final_cols, final_scaled = edge_cols(block_count - 1)
    part_pieces = jnp.stack(
        [
            contract_rows(first_cols, first_scaled),
            contract_rows(first_cols, final_scaled),
            contract_rows(final_cols, final_scaled),
        ]
    )
    summed = lax.psum(part_pieces, "row")
    eye = jnp.eye(BLK, dtype=jnp.float32)
    segment = (
        summed[0] + eye * diagonal[:BLK][None, :],
        summed[1],
        summed[2] + eye * diagonal[L - BLK :][None, :],
    )

    times = lax.axis_size("tm")
    position = lax.axis_index("tm")
    running = segment
    shift = 1
    while shift < times:
        pairs = [(src, src + shift) for src in range(times - shift)]
        moved = lax.ppermute(jnp.stack(running), "tm", pairs)
        earlier = (moved[0], moved[1], moved[2])
        joined = join_segments(earlier, running)
        take = position >= shift
        running = tuple(jnp.where(take, new, old) for new, old in zip(joined, running))
        shift *= 2
    chain_out = jnp.stack(running)[None]

    owners = lax.axis_size("row")
    own_blocks = block_count // owners
    own_tiles = lax.dynamic_slice_in_dim(tile_order, my_index * own_blocks, own_blocks)
    left_src = jnp.take(source, own_tiles)
    every_weight = lax.all_gather(row_weights, "row", axis=0, tiled=False)
    every_mask = lax.all_gather(live_blocks, "row", axis=0, tiled=False)
    peers = []
    for step in range(1, owners):
        pairs = [(src, src ^ step) for src in range(owners)]
        peers.append((lax.ppermute(local_slab, "row", pairs), my_index ^ step))
    owned = gram_contrib(
        local_slab, row_weights, live_blocks, left_src, source, own_tiles, diagonal
    )
    for slab, where_from in peers:
        owned = gram_contrib(
            slab,
            lax.dynamic_index_in_dim(every_weight, where_from, 0, False),
            lax.dynamic_index_in_dim(every_mask, where_from, 0, False),
            left_src, source, own_tiles, diagonal, owned,
        )
    return (owned[None], chain_out)


def solution(mesh):
    placed = (
        P("tm", "row", None),
        P("tm", "row"),
        P("tm", "row", None),
        P("tm", None),
        P(),
        P("tm", None),
    )
    return jax.shard_map(
        local,
        mesh=mesh,
        in_specs=placed,
        out_specs=(P("tm", "row", None), P("tm", None, None, None)),
        check_vma=False,
    )
```

```python
import jax
import jax.numpy as jnp
from jax import lax
from jax.sharding import PartitionSpec as P
from jax.experimental import pallas as pl
from jax.experimental.pallas import tpu as pltpu

L = 2048
BLK = 128


def contrib_kernel(src_left, src_right, tile_ref, mask_ref, flag_ref, g_ref, w_ref, diag_ref, *rest):
    if len(rest) == 4:
        acc_ref, out_ref, s_ref, lt_ref = rest
    else:
        acc_ref = None
        out_ref, s_ref, lt_ref = rest
    k = pl.program_id(0)
    row_blocks = g_ref.shape[0] // BLK
    col_blocks = g_ref.shape[1] // BLK

    @pl.when(k == 0)
    def _():
        def fill(j, carry):
            src = src_right[j]
            c0 = pl.multiple_of(src * BLK, BLK)
            d0 = pl.multiple_of(j * BLK, BLK)
            for rb in range(row_blocks):
                live = mask_ref[rb * col_blocks + src].astype(jnp.float32)
                vals = g_ref[rb * BLK:(rb + 1) * BLK, pl.ds(c0, BLK)].astype(jnp.float32)
                wts = w_ref[rb * BLK:(rb + 1) * BLK, :]
                s_ref[rb * BLK:(rb + 1) * BLK, pl.ds(d0, BLK)] = (wts * (vals * live)).astype(jnp.bfloat16)
            return carry
        lax.fori_loop(0, col_blocks, fill, 0)

    src = src_left[k]
    c0 = pl.multiple_of(src * BLK, BLK)
    for rb in range(row_blocks):
        live = mask_ref[rb * col_blocks + src].astype(jnp.float32)
        vals = g_ref[rb * BLK:(rb + 1) * BLK, pl.ds(c0, BLK)].astype(jnp.float32) * live
        lt_ref[:, rb * BLK:(rb + 1) * BLK] = vals.T.astype(jnp.bfloat16)
    term = jnp.dot(lt_ref[...], s_ref[...], preferred_element_type=jnp.float32)
    if acc_ref is None:
        out_ref[...] = term
        blk = tile_ref[k]
        e0 = pl.multiple_of(blk * BLK, BLK)
        rows = lax.broadcasted_iota(jnp.int32, (BLK, BLK), 0)
        cols = lax.broadcasted_iota(jnp.int32, (BLK, BLK), 1)
        dvals = diag_ref[pl.ds(blk, 1), :] * flag_ref[0].astype(jnp.float32)
        out_ref[:, pl.ds(e0, BLK)] += jnp.where(rows == cols, dvals, 0.0)
    else:
        out_ref[...] = acc_ref[...] + term


def gram_contrib(slab, weights, live_blocks, src_left, src_right, own_tiles, diagonal, acc=None):
    height = slab.shape[0]
    col_blocks = L // BLK
    out_blocks = src_left.shape[0]
    in_specs = [
        pl.BlockSpec((height, L), lambda k, *_: (0, 0)),
        pl.BlockSpec((height, 1), lambda k, *_: (0, 0)),
        pl.BlockSpec((col_blocks, BLK), lambda k, *_: (0, 0)),
    ]
    operands = [slab, weights.reshape(height, 1), diagonal.reshape(col_blocks, BLK)]
    aliases = {}
    if acc is not None:
        in_specs.append(pl.BlockSpec((BLK, L), lambda k, *_: (k, 0)))
        operands.append(acc)
        aliases = {8: 0}
    grid_spec = pltpu.PrefetchScalarGridSpec(
        num_scalar_prefetch=5,
        grid=(out_blocks,),
        in_specs=in_specs,
        out_specs=pl.BlockSpec((BLK, L), lambda k, *_: (k, 0)),
        scratch_shapes=[pltpu.VMEM((height, L), jnp.bfloat16), pltpu.VMEM((BLK, height), jnp.bfloat16)],
    )
    return pl.pallas_call(
        contrib_kernel,
        grid_spec=grid_spec,
        out_shape=jax.ShapeDtypeStruct((out_blocks * BLK, L), jnp.float32),
        input_output_aliases=aliases,
        compiler_params=pltpu.CompilerParams(vmem_limit_bytes=56 * 1024 * 1024),
    )(src_left, src_right, own_tiles, live_blocks.reshape(-1), jnp.ones((1,), jnp.int32), *operands)


HIGHEST = lax.Precision.HIGHEST


def join_segments(earlier_seg, later_seg):
    top_one, cross_one, bottom_one = earlier_seg
    top_two, cross_two, bottom_two = later_seg
    middle = bottom_one + top_two
    middle = 0.5 * (middle + middle.T)
    factor = jnp.linalg.cholesky(middle)
    half_width = top_one.shape[0]
    solved = jax.scipy.linalg.cho_solve(
        (factor, True), jnp.concatenate([cross_one.T, cross_two], axis=1)
    )
    solve_one = solved[:, :half_width]
    solve_two = solved[:, half_width:]
    top_new = top_one - jnp.dot(cross_one, solve_one, precision=HIGHEST)
    cross_new = -jnp.dot(cross_one, solve_two, precision=HIGHEST)
    bottom_new = bottom_two - jnp.dot(cross_two.T, solve_two, precision=HIGHEST)
    return (top_new, cross_new, bottom_new)


def contract_rows(left_cols, right_cols):
    return lax.dot_general(
        left_cols, right_cols, (((0,), (0,)), ((), ())), preferred_element_type=jnp.float32
    )


def local(coupling, row_scale, block_mask, link_map, tile_order, link_diag):
    local_slab = coupling[0]
    row_weights = row_scale[0]
    live_blocks = block_mask[0]
    block_map = link_map[0]
    diagonal = link_diag[0]
    slab_height = local_slab.shape[0]
    block_count = L // BLK
    my_index = lax.axis_index("row")
    block_ids = jnp.arange(block_count, dtype=jnp.int32)
    source = jnp.sum(
        block_ids[None, :] * (block_map[None, :] == block_ids[:, None]).astype(jnp.int32), axis=1
    )

    def edge_cols(global_block):
        local_block = source[global_block]
        cols = lax.dynamic_slice_in_dim(local_slab, local_block * BLK, BLK, axis=1)
        live = lax.dynamic_index_in_dim(live_blocks, local_block, 1, False)
        cols = (cols.reshape(slab_height // BLK, BLK, BLK) * live.astype(jnp.bfloat16)[:, None, None])
        cols = cols.reshape(slab_height, BLK)
        weighted = (row_weights[:, None] * cols.astype(jnp.float32)).astype(jnp.bfloat16)
        return cols, weighted

    first_cols, first_scaled = edge_cols(0)
    final_cols, final_scaled = edge_cols(block_count - 1)
    part_pieces = jnp.stack(
        [
            contract_rows(first_cols, first_scaled),
            contract_rows(first_cols, final_scaled),
            contract_rows(final_cols, final_scaled),
        ]
    )
    summed = lax.psum(part_pieces, "row")
    eye = jnp.eye(BLK, dtype=jnp.float32)
    segment = (
        summed[0] + eye * diagonal[:BLK][None, :],
        summed[1],
        summed[2] + eye * diagonal[L - BLK :][None, :],
    )

    times = lax.axis_size("tm")
    position = lax.axis_index("tm")
    running = segment
    shift = 1
    while shift < times:
        pairs = [(src, src + shift) for src in range(times - shift)]
        moved = lax.ppermute(jnp.stack(running), "tm", pairs)
        earlier = (moved[0], moved[1], moved[2])
        joined = join_segments(earlier, running)
        take = position >= shift
        running = tuple(jnp.where(take, new, old) for new, old in zip(joined, running))
        shift *= 2
    chain_out = jnp.stack(running)[None]

    owners = lax.axis_size("row")
    own_blocks = block_count // owners
    own_tiles = lax.dynamic_slice_in_dim(tile_order, my_index * own_blocks, own_blocks)
    left_src = jnp.take(source, own_tiles)
    packed_side = jnp.concatenate(
        [row_weights, live_blocks.reshape(-1).astype(jnp.float32)]
    )

    def unpack_side(side, chunk, chunks):
        rows = slab_height // chunks
        weights = lax.slice_in_dim(side, chunk * rows, (chunk + 1) * rows)
        live = side[slab_height:].reshape(slab_height // BLK, block_count).astype(jnp.int32)
        live = lax.slice_in_dim(live, chunk * (rows // BLK), (chunk + 1) * (rows // BLK))
        return weights, live

    def exchange(value, step):
        return lax.ppermute(value, "row", [(src, src ^ step) for src in range(owners)])

    chunks = 2
    chunk_rows = slab_height // chunks
    own_slabs = [lax.slice_in_dim(local_slab, c * chunk_rows, (c + 1) * chunk_rows) for c in range(chunks)]
    if owners == 4:
        neighbour = (exchange(local_slab, 1), exchange(packed_side, 1), 1)
        across_side = exchange(packed_side, 2)
        across = [exchange(piece, 2) for piece in own_slabs]
        forwarded = [exchange(piece, 1) for piece in across]
        forwarded_side = exchange(across_side, 1)
        arrivals = [neighbour]
        arrivals += [(piece, across_side, c, chunks) for c, piece in enumerate(across)]
        arrivals += [(piece, forwarded_side, c, chunks) for c, piece in enumerate(forwarded)]
    else:
        arrivals = [
            (exchange(local_slab, step), exchange(packed_side, step), 0, 1)
            for step in range(1, owners)
        ]
    owned = gram_contrib(
        local_slab, row_weights, live_blocks, left_src, source, own_tiles, diagonal
    )
    for arrival in arrivals:
        if len(arrival) == 3:
            slab, side, _ = arrival
            weights, live = unpack_side(side, 0, 1)
        else:
            slab, side, chunk, count = arrival
            weights, live = unpack_side(side, chunk, count)
        owned = gram_contrib(
            slab, weights, live, left_src, source, own_tiles, diagonal, owned,
        )
    return (owned[None], chain_out)


def solution(mesh):
    placed = (
        P("tm", "row", None),
        P("tm", "row"),
        P("tm", "row", None),
        P("tm", None),
        P(),
        P("tm", None),
    )
    return jax.shard_map(
        local,
        mesh=mesh,
        in_specs=placed,
        out_specs=(P("tm", "row", None), P("tm", None, None, None)),
        check_vma=False,
    )
```

```python
import jax
import jax.numpy as jnp
from jax import lax
from jax.sharding import PartitionSpec as P
from jax.experimental import pallas as pl
from jax.experimental.pallas import tpu as pltpu

L = 2048
BLK = 128


def gram_kernel(src_left, src_right, tile_ref, mask_ref, flag_ref, g_ref, w_ref, diag_ref,
                out_ref, s_ref, lt_ref):
    k = pl.program_id(0)
    row_blocks = g_ref.shape[0] // BLK
    col_blocks = g_ref.shape[1] // BLK

    @pl.when(k == 0)
    def _():
        def fill(j, carry):
            src = src_right[j]
            c0 = pl.multiple_of(src * BLK, BLK)
            d0 = pl.multiple_of(j * BLK, BLK)
            for rb in range(row_blocks):
                live = mask_ref[rb * col_blocks + src].astype(jnp.float32)
                vals = g_ref[rb * BLK:(rb + 1) * BLK, pl.ds(c0, BLK)].astype(jnp.float32)
                wts = w_ref[rb * BLK:(rb + 1) * BLK, :]
                s_ref[rb * BLK:(rb + 1) * BLK, pl.ds(d0, BLK)] = (wts * (vals * live)).astype(jnp.bfloat16)
            return carry
        lax.fori_loop(0, col_blocks, fill, 0)

    src = src_left[k]
    c0 = pl.multiple_of(src * BLK, BLK)
    for rb in range(row_blocks):
        live = mask_ref[rb * col_blocks + src].astype(jnp.float32)
        vals = g_ref[rb * BLK:(rb + 1) * BLK, pl.ds(c0, BLK)].astype(jnp.float32) * live
        lt_ref[:, rb * BLK:(rb + 1) * BLK] = vals.T.astype(jnp.bfloat16)
    out_ref[...] = jnp.dot(lt_ref[...], s_ref[...], preferred_element_type=jnp.float32)
    blk = tile_ref[k]
    e0 = pl.multiple_of(blk * BLK, BLK)
    rows = lax.broadcasted_iota(jnp.int32, (BLK, BLK), 0)
    cols = lax.broadcasted_iota(jnp.int32, (BLK, BLK), 1)
    dvals = diag_ref[pl.ds(blk, 1), :] * flag_ref[0].astype(jnp.float32)
    out_ref[:, pl.ds(e0, BLK)] += jnp.where(rows == cols, dvals, 0.0)


def gram_rows(slab, weights, live_blocks, src_left, src_right, tile_order, diagonal, flag, group):
    height = slab.shape[0]
    col_blocks = L // BLK
    grid_spec = pltpu.PrefetchScalarGridSpec(
        num_scalar_prefetch=5,
        grid=(col_blocks,),
        in_specs=[
            pl.BlockSpec((height, L), lambda k, *_: (0, 0)),
            pl.BlockSpec((height, 1), lambda k, *_: (0, 0)),
            pl.BlockSpec((col_blocks, BLK), lambda k, *_: (0, 0)),
        ],
        out_specs=pl.BlockSpec((None, BLK, L), lambda k, *_: (k // group, k % group, 0)),
        scratch_shapes=[pltpu.VMEM((height, L), jnp.bfloat16), pltpu.VMEM((BLK, height), jnp.bfloat16)],
    )
    return pl.pallas_call(
        gram_kernel,
        grid_spec=grid_spec,
        out_shape=jax.ShapeDtypeStruct((col_blocks // group, group * BLK, L), jnp.float32),
        compiler_params=pltpu.CompilerParams(vmem_limit_bytes=56 * 1024 * 1024),
    )(src_left, src_right, tile_order, live_blocks.reshape(-1), flag.reshape(1),
      slab, weights.reshape(height, 1), diagonal.reshape(col_blocks, BLK))


HIGHEST = lax.Precision.HIGHEST


def join_segments(earlier_seg, later_seg):
    top_one, cross_one, bottom_one = earlier_seg
    top_two, cross_two, bottom_two = later_seg
    middle = bottom_one + top_two
    middle = 0.5 * (middle + middle.T)
    factor = jnp.linalg.cholesky(middle)
    half_width = top_one.shape[0]
    solved = lax.linalg.triangular_solve(
        factor, jnp.concatenate([cross_one.T, cross_two], axis=1), left_side=True, lower=True
    )
    solve_one = solved[:, :half_width]
    solve_two = solved[:, half_width:]
    top_new = top_one - jnp.dot(solve_one.T, solve_one, precision=HIGHEST)
    cross_new = -jnp.dot(solve_one.T, solve_two, precision=HIGHEST)
    bottom_new = bottom_two - jnp.dot(solve_two.T, solve_two, precision=HIGHEST)
    return (top_new, cross_new, bottom_new)


def contract_rows(left_cols, right_cols):
    return lax.dot_general(
        left_cols, right_cols, (((0,), (0,)), ((), ())), preferred_element_type=jnp.float32
    )


def local(coupling, row_scale, block_mask, link_map, tile_order, link_diag):
    local_slab = coupling[0]
    row_weights = row_scale[0]
    live_blocks = block_mask[0]
    block_map = link_map[0]
    diagonal = link_diag[0]
    slab_height = local_slab.shape[0]
    block_count = L // BLK
    my_index = lax.axis_index("row")
    block_ids = jnp.arange(block_count, dtype=jnp.int32)
    source = jnp.sum(
        block_ids[None, :] * (block_map[None, :] == block_ids[:, None]).astype(jnp.int32), axis=1
    )

    def edge_cols(global_block):
        local_block = source[global_block]
        cols = lax.dynamic_slice_in_dim(local_slab, local_block * BLK, BLK, axis=1)
        live = lax.dynamic_index_in_dim(live_blocks, local_block, 1, False)
        cols = (cols.reshape(slab_height // BLK, BLK, BLK) * live.astype(jnp.bfloat16)[:, None, None])
        cols = cols.reshape(slab_height, BLK)
        weighted = (row_weights[:, None] * cols.astype(jnp.float32)).astype(jnp.bfloat16)
        return cols, weighted

    first_cols, first_scaled = edge_cols(0)
    final_cols, final_scaled = edge_cols(block_count - 1)
    part_pieces = jnp.stack(
        [
            contract_rows(first_cols, first_scaled),
            contract_rows(first_cols, final_scaled),
            contract_rows(final_cols, final_scaled),
        ]
    )
    summed = lax.psum(part_pieces, "row")
    eye = jnp.eye(BLK, dtype=jnp.float32)
    segment = (
        summed[0] + eye * diagonal[:BLK][None, :],
        summed[1],
        summed[2] + eye * diagonal[L - BLK :][None, :],
    )

    times = lax.axis_size("tm")
    position = lax.axis_index("tm")
    running = segment
    shift = 1
    while shift < times:
        pairs = [(src, src + shift) for src in range(times - shift)]
        moved = lax.ppermute(jnp.stack(running), "tm", pairs)
        earlier = (moved[0], moved[1], moved[2])
        joined = join_segments(earlier, running)
        take = position >= shift
        running = tuple(jnp.where(take, new, old) for new, old in zip(joined, running))
        shift *= 2
    chain_out = jnp.stack(running)[None]

    flag = (my_index == 0).astype(jnp.int32)
    owners = lax.axis_size("row")
    own_blocks = block_count // owners
    if owners == 4:
        order = jnp.concatenate(
            [lax.dynamic_slice_in_dim(tile_order, (my_index ^ q) * own_blocks, own_blocks) for q in range(owners)]
        )
    else:
        order = tile_order
    partial = gram_rows(
        local_slab, row_weights, live_blocks, jnp.take(source, order), source,
        order, diagonal, flag, own_blocks,
    )
    if owners == 4:
        def exchange(value, step):
            return lax.ppermute(value, "row", [(src, src ^ step) for src in range(owners)])

        from_partner = exchange(partial[1], 1)
        for_across = exchange(partial[3], 1)
        from_across = exchange(partial[2] + for_across, 2)
        owned = partial[0] + from_partner + from_across
    else:
        owned = lax.psum_scatter(
            partial.reshape(L, L), "row", scatter_dimension=0, tiled=True
        )
    return (owned[None], chain_out)


def solution(mesh):
    placed = (
        P("tm", "row", None),
        P("tm", "row"),
        P("tm", "row", None),
        P("tm", None),
        P(),
        P("tm", None),
    )
    return jax.shard_map(
        local,
        mesh=mesh,
        in_specs=placed,
        out_specs=(P("tm", "row", None), P("tm", None, None, None)),
        check_vma=False,
    )
```

```python
import jax
import jax.numpy as jnp
from jax import lax
from jax.sharding import PartitionSpec as P
from jax.experimental import pallas as pl
from jax.experimental.pallas import tpu as pltpu

L = 2048
BLK = 128


def gram_kernel(src_left, src_right, tile_ref, mask_ref, flag_ref, g_ref, w_ref, diag_ref,
                out_ref, s_ref, lt_ref):
    k = pl.program_id(0)
    row_blocks = g_ref.shape[0] // BLK
    col_blocks = g_ref.shape[1] // BLK

    @pl.when(k == 0)
    def _():
        def fill(j, carry):
            src = src_right[j]
            c0 = pl.multiple_of(src * BLK, BLK)
            d0 = pl.multiple_of(j * BLK, BLK)
            for rb in range(row_blocks):
                live = mask_ref[rb * col_blocks + src].astype(jnp.float32)
                vals = g_ref[rb * BLK:(rb + 1) * BLK, pl.ds(c0, BLK)].astype(jnp.float32)
                wts = w_ref[rb * BLK:(rb + 1) * BLK, :]
                s_ref[rb * BLK:(rb + 1) * BLK, pl.ds(d0, BLK)] = (wts * (vals * live)).astype(jnp.bfloat16)
            return carry
        lax.fori_loop(0, col_blocks, fill, 0)

    src = src_left[k]
    c0 = pl.multiple_of(src * BLK, BLK)
    for rb in range(row_blocks):
        live = mask_ref[rb * col_blocks + src].astype(jnp.float32)
        vals = g_ref[rb * BLK:(rb + 1) * BLK, pl.ds(c0, BLK)].astype(jnp.float32) * live
        lt_ref[:, rb * BLK:(rb + 1) * BLK] = vals.T.astype(jnp.bfloat16)
    out_ref[...] = jnp.dot(lt_ref[...], s_ref[...], preferred_element_type=jnp.float32)
    blk = tile_ref[k]
    e0 = pl.multiple_of(blk * BLK, BLK)
    rows = lax.broadcasted_iota(jnp.int32, (BLK, BLK), 0)
    cols = lax.broadcasted_iota(jnp.int32, (BLK, BLK), 1)
    dvals = diag_ref[pl.ds(blk, 1), :] * flag_ref[0].astype(jnp.float32)
    out_ref[:, pl.ds(e0, BLK)] += jnp.where(rows == cols, dvals, 0.0)


def gram_rows(slab, weights, live_blocks, src_left, src_right, tile_order, diagonal, flag, group):
    height = slab.shape[0]
    col_blocks = L // BLK
    grid_spec = pltpu.PrefetchScalarGridSpec(
        num_scalar_prefetch=5,
        grid=(col_blocks,),
        in_specs=[
            pl.BlockSpec((height, L), lambda k, *_: (0, 0)),
            pl.BlockSpec((height, 1), lambda k, *_: (0, 0)),
            pl.BlockSpec((col_blocks, BLK), lambda k, *_: (0, 0)),
        ],
        out_specs=pl.BlockSpec((None, BLK, L), lambda k, *_: (k // group, k % group, 0)),
        scratch_shapes=[pltpu.VMEM((height, L), jnp.bfloat16), pltpu.VMEM((BLK, height), jnp.bfloat16)],
    )
    return pl.pallas_call(
        gram_kernel,
        grid_spec=grid_spec,
        out_shape=jax.ShapeDtypeStruct((col_blocks // group, group * BLK, L), jnp.float32),
        compiler_params=pltpu.CompilerParams(vmem_limit_bytes=56 * 1024 * 1024),
    )(src_left, src_right, tile_order, live_blocks.reshape(-1), flag.reshape(1),
      slab, weights.reshape(height, 1), diagonal.reshape(col_blocks, BLK))


HIGHEST = lax.Precision.HIGHEST


def join_segments(earlier_seg, later_seg):
    top_one, cross_one, bottom_one = earlier_seg
    top_two, cross_two, bottom_two = later_seg
    middle = bottom_one + top_two
    middle = 0.5 * (middle + middle.T)
    factor = jnp.linalg.cholesky(middle)
    half_width = top_one.shape[0]
    solved = lax.linalg.triangular_solve(
        factor, jnp.concatenate([cross_one.T, cross_two], axis=1), left_side=True, lower=True
    )
    solve_one = solved[:, :half_width]
    solve_two = solved[:, half_width:]
    top_new = top_one - jnp.dot(solve_one.T, solve_one, precision=HIGHEST)
    cross_new = -jnp.dot(solve_one.T, solve_two, precision=HIGHEST)
    bottom_new = bottom_two - jnp.dot(solve_two.T, solve_two, precision=HIGHEST)
    return (top_new, cross_new, bottom_new)


def contract_rows(left_cols, right_cols):
    return lax.dot_general(
        left_cols, right_cols, (((0,), (0,)), ((), ())), preferred_element_type=jnp.float32
    )


def local(coupling, row_scale, block_mask, link_map, tile_order, link_diag):
    local_slab = coupling[0]
    row_weights = row_scale[0]
    live_blocks = block_mask[0]
    block_map = link_map[0]
    diagonal = link_diag[0]
    slab_height = local_slab.shape[0]
    block_count = L // BLK
    my_index = lax.axis_index("row")
    block_ids = jnp.arange(block_count, dtype=jnp.int32)
    source = jnp.sum(
        block_ids[None, :] * (block_map[None, :] == block_ids[:, None]).astype(jnp.int32), axis=1
    )

    def edge_cols(global_block):
        local_block = source[global_block]
        cols = lax.dynamic_slice_in_dim(local_slab, local_block * BLK, BLK, axis=1)
        live = lax.dynamic_index_in_dim(live_blocks, local_block, 1, False)
        cols = (cols.reshape(slab_height // BLK, BLK, BLK) * live.astype(jnp.bfloat16)[:, None, None])
        cols = cols.reshape(slab_height, BLK)
        weighted = (row_weights[:, None] * cols.astype(jnp.float32)).astype(jnp.bfloat16)
        return cols, weighted

    first_cols, first_scaled = edge_cols(0)
    final_cols, final_scaled = edge_cols(block_count - 1)
    part_pieces = jnp.stack(
        [
            contract_rows(first_cols, first_scaled),
            contract_rows(first_cols, final_scaled),
            contract_rows(final_cols, final_scaled),
        ]
    )
    owners = lax.axis_size("row")
    own_blocks = block_count // owners

    def exchange(value, step):
        return lax.ppermute(value, "row", [(src, src ^ step) for src in range(owners)])

    kernel_slab, part_pieces = lax.optimization_barrier((local_slab, part_pieces))
    if owners & (owners - 1) == 0:
        summed = part_pieces
        step = 1
        while step < owners:
            summed = summed + exchange(summed, step)
            step *= 2
    else:
        summed = lax.psum(part_pieces, "row")
    eye = jnp.eye(BLK, dtype=jnp.float32)
    segment = jnp.stack([
        summed[0] + eye * diagonal[:BLK][None, :],
        summed[1],
        summed[2] + eye * diagonal[L - BLK :][None, :],
    ])

    flag = (my_index == 0).astype(jnp.int32)
    if owners == 4:
        order = jnp.concatenate(
            [lax.dynamic_slice_in_dim(tile_order, (my_index ^ q) * own_blocks, own_blocks) for q in range(owners)]
        )
    else:
        order = tile_order
    partial = gram_rows(
        kernel_slab, row_weights, live_blocks, jnp.take(source, order), source,
        order, diagonal, flag, own_blocks,
    )
    if owners == 4:
        for_across = exchange(partial[3], 1)
        to_across = partial[2] + for_across
        to_across, segment = lax.optimization_barrier((to_across, segment))
        from_across = exchange(to_across, 2)
        from_partner = exchange(partial[1], 1)
    else:
        owned = lax.psum_scatter(
            partial.reshape(L, L), "row", scatter_dimension=0, tiled=True
        )

    times = lax.axis_size("tm")
    position = lax.axis_index("tm")
    running = (segment[0], segment[1], segment[2])
    shift = 1
    while shift < times:
        pairs = [(src, src + shift) for src in range(times - shift)]
        moved = lax.ppermute(jnp.stack(running), "tm", pairs)
        earlier = (moved[0], moved[1], moved[2])
        joined = join_segments(earlier, running)
        take = position >= shift
        running = tuple(jnp.where(take, new, old) for new, old in zip(joined, running))
        shift *= 2
    chain_out = jnp.stack(running)[None]
    if owners == 4:
        owned = partial[0] + from_partner + from_across
    return (owned[None], chain_out)


def solution(mesh):
    placed = (
        P("tm", "row", None),
        P("tm", "row"),
        P("tm", "row", None),
        P("tm", None),
        P(),
        P("tm", None),
    )
    return jax.shard_map(
        local,
        mesh=mesh,
        in_specs=placed,
        out_specs=(P("tm", "row", None), P("tm", None, None, None)),
        check_vma=False,
    )
```

```python
import jax
import jax.numpy as jnp
from jax import lax
from jax.sharding import PartitionSpec as P
from jax.experimental import pallas as pl
from jax.experimental.pallas import tpu as pltpu

L = 2048
BLK = 128


def gram_kernel(src_left, src_right, tile_ref, mask_ref, flag_ref, g_ref, w_ref, diag_ref, *rest):
    if len(rest) == 4:
        acc_ref, out_ref, s_ref, lt_ref = rest
    else:
        acc_ref = None
        out_ref, s_ref, lt_ref = rest
    k = pl.program_id(0)
    row_blocks = g_ref.shape[0] // BLK
    col_blocks = g_ref.shape[1] // BLK

    @pl.when(k == 0)
    def _():
        def fill(j, carry):
            src = src_right[j]
            c0 = pl.multiple_of(src * BLK, BLK)
            d0 = pl.multiple_of(j * BLK, BLK)
            for rb in range(row_blocks):
                live = mask_ref[rb * col_blocks + src].astype(jnp.float32)
                vals = g_ref[rb * BLK:(rb + 1) * BLK, pl.ds(c0, BLK)].astype(jnp.float32)
                wts = w_ref[rb * BLK:(rb + 1) * BLK, :]
                s_ref[rb * BLK:(rb + 1) * BLK, pl.ds(d0, BLK)] = (wts * (vals * live)).astype(jnp.bfloat16)
            return carry
        lax.fori_loop(0, col_blocks, fill, 0)

    src = src_left[k]
    c0 = pl.multiple_of(src * BLK, BLK)
    for rb in range(row_blocks):
        live = mask_ref[rb * col_blocks + src].astype(jnp.float32)
        vals = g_ref[rb * BLK:(rb + 1) * BLK, pl.ds(c0, BLK)].astype(jnp.float32) * live
        lt_ref[:, rb * BLK:(rb + 1) * BLK] = vals.T.astype(jnp.bfloat16)
    term = jnp.dot(lt_ref[...], s_ref[...], preferred_element_type=jnp.float32)
    if acc_ref is None:
        out_ref[...] = term
        blk = tile_ref[k]
        e0 = pl.multiple_of(blk * BLK, BLK)
        rows = lax.broadcasted_iota(jnp.int32, (BLK, BLK), 0)
        cols = lax.broadcasted_iota(jnp.int32, (BLK, BLK), 1)
        dvals = diag_ref[pl.ds(blk, 1), :] * flag_ref[k].astype(jnp.float32)
        out_ref[:, pl.ds(e0, BLK)] += jnp.where(rows == cols, dvals, 0.0)
    else:
        out_ref[...] = acc_ref[...] + term


def gram_rows(slab, weights, live_blocks, src_left, src_right, out_tiles, diagonal, flags, group, acc=None):
    height = slab.shape[0]
    col_blocks = L // BLK
    out_blocks = src_left.shape[0]
    in_specs = [
        pl.BlockSpec((height, L), lambda k, *_: (0, 0)),
        pl.BlockSpec((height, 1), lambda k, *_: (0, 0)),
        pl.BlockSpec((col_blocks, BLK), lambda k, *_: (0, 0)),
    ]
    operands = [slab, weights.reshape(height, 1), diagonal.reshape(col_blocks, BLK)]
    aliases = {}
    out_spec = pl.BlockSpec((None, BLK, L), lambda k, *_: (k // group, k % group, 0))
    if acc is not None:
        in_specs.append(out_spec)
        operands.append(acc)
        aliases = {8: 0}
    grid_spec = pltpu.PrefetchScalarGridSpec(
        num_scalar_prefetch=5,
        grid=(out_blocks,),
        in_specs=in_specs,
        out_specs=out_spec,
        scratch_shapes=[pltpu.VMEM((height, L), jnp.bfloat16), pltpu.VMEM((BLK, height), jnp.bfloat16)],
    )
    return pl.pallas_call(
        gram_kernel,
        grid_spec=grid_spec,
        out_shape=jax.ShapeDtypeStruct((out_blocks // group, group * BLK, L), jnp.float32),
        input_output_aliases=aliases,
        compiler_params=pltpu.CompilerParams(vmem_limit_bytes=56 * 1024 * 1024),
    )(src_left, src_right, out_tiles, live_blocks.reshape(-1), flags, *operands)


HIGHEST = lax.Precision.HIGHEST


def join_segments(earlier_seg, later_seg):
    top_one, cross_one, bottom_one = earlier_seg
    top_two, cross_two, bottom_two = later_seg
    middle = bottom_one + top_two
    middle = 0.5 * (middle + middle.T)
    factor = jnp.linalg.cholesky(middle)
    half_width = top_one.shape[0]
    solved = lax.linalg.triangular_solve(
        factor, jnp.concatenate([cross_one.T, cross_two], axis=1), left_side=True, lower=True
    )
    solve_one = solved[:, :half_width]
    solve_two = solved[:, half_width:]
    top_new = top_one - jnp.dot(solve_one.T, solve_one, precision=HIGHEST)
    cross_new = -jnp.dot(solve_one.T, solve_two, precision=HIGHEST)
    bottom_new = bottom_two - jnp.dot(solve_two.T, solve_two, precision=HIGHEST)
    return (top_new, cross_new, bottom_new)


def contract_rows(left_cols, right_cols):
    return lax.dot_general(
        left_cols, right_cols, (((0,), (0,)), ((), ())), preferred_element_type=jnp.float32
    )


def local(coupling, row_scale, block_mask, link_map, tile_order, link_diag):
    local_slab = coupling[0]
    row_weights = row_scale[0]
    live_blocks = block_mask[0]
    block_map = link_map[0]
    diagonal = link_diag[0]
    slab_height = local_slab.shape[0]
    block_count = L // BLK
    my_index = lax.axis_index("row")
    block_ids = jnp.arange(block_count, dtype=jnp.int32)
    source = jnp.sum(
        block_ids[None, :] * (block_map[None, :] == block_ids[:, None]).astype(jnp.int32), axis=1
    )

    def edge_cols(global_block):
        local_block = source[global_block]
        cols = lax.dynamic_slice_in_dim(local_slab, local_block * BLK, BLK, axis=1)
        live = lax.dynamic_index_in_dim(live_blocks, local_block, 1, False)
        cols = (cols.reshape(slab_height // BLK, BLK, BLK) * live.astype(jnp.bfloat16)[:, None, None])
        cols = cols.reshape(slab_height, BLK)
        weighted = (row_weights[:, None] * cols.astype(jnp.float32)).astype(jnp.bfloat16)
        return cols, weighted

    first_cols, first_scaled = edge_cols(0)
    final_cols, final_scaled = edge_cols(block_count - 1)
    part_pieces = jnp.stack(
        [
            contract_rows(first_cols, first_scaled),
            contract_rows(first_cols, final_scaled),
            contract_rows(final_cols, final_scaled),
        ]
    )
    owners = lax.axis_size("row")
    own_blocks = block_count // owners

    def exchange(value, step):
        return lax.ppermute(value, "row", [(src, src ^ step) for src in range(owners)])

    kernel_slab, part_pieces = lax.optimization_barrier((local_slab, part_pieces))
    if owners & (owners - 1) == 0:
        summed = part_pieces
        step = 1
        while step < owners:
            summed = summed + exchange(summed, step)
            step *= 2
    else:
        summed = lax.psum(part_pieces, "row")
    eye = jnp.eye(BLK, dtype=jnp.float32)
    segment = jnp.stack([
        summed[0] + eye * diagonal[:BLK][None, :],
        summed[1],
        summed[2] + eye * diagonal[L - BLK :][None, :],
    ])

    if owners == 4:
        packed_side = jnp.concatenate([row_weights, live_blocks.reshape(-1).astype(jnp.float32)])
        across_slab = exchange(local_slab, 2)
        across_side = exchange(packed_side, 2)
        across_weights = across_side[:slab_height]
        across_live = across_side[slab_height:].reshape(live_blocks.shape).astype(jnp.int32)
        order = jnp.concatenate(
            [lax.dynamic_slice_in_dim(tile_order, (my_index ^ q) * own_blocks, own_blocks) for q in range(2)]
        )
        flags = (jnp.arange(2 * own_blocks) < own_blocks).astype(jnp.int32)
        left_src = jnp.take(source, order)
        partial = gram_rows(
            kernel_slab, row_weights, live_blocks, left_src, source, order, diagonal, flags, own_blocks,
        )
        partial = gram_rows(
            across_slab, across_weights, across_live, left_src, source, order, diagonal, flags,
            own_blocks, partial,
        )
        owned = partial[0] + exchange(partial[1], 1)
    else:
        flags = jnp.full((block_count,), (my_index == 0).astype(jnp.int32))
        partial = gram_rows(
            kernel_slab, row_weights, live_blocks, jnp.take(source, tile_order), source,
            tile_order, diagonal, flags, own_blocks,
        )
        owned = lax.psum_scatter(
            partial.reshape(L, L), "row", scatter_dimension=0, tiled=True
        )

    times = lax.axis_size("tm")
    position = lax.axis_index("tm")
    running = (segment[0], segment[1], segment[2])
    shift = 1
    while shift < times:
        pairs = [(src, src + shift) for src in range(times - shift)]
        moved = lax.ppermute(jnp.stack(running), "tm", pairs)
        earlier = (moved[0], moved[1], moved[2])
        joined = join_segments(earlier, running)
        take = position >= shift
        running = tuple(jnp.where(take, new, old) for new, old in zip(joined, running))
        shift *= 2
    chain_out = jnp.stack(running)[None]
    return (owned[None], chain_out)


def solution(mesh):
    placed = (
        P("tm", "row", None),
        P("tm", "row"),
        P("tm", "row", None),
        P("tm", None),
        P(),
        P("tm", None),
    )
    return jax.shard_map(
        local,
        mesh=mesh,
        in_specs=placed,
        out_specs=(P("tm", "row", None), P("tm", None, None, None)),
        check_vma=False,
    )
```

```python
import jax
import jax.numpy as jnp
from jax import lax
from jax.sharding import PartitionSpec as P
from jax.experimental import pallas as pl
from jax.experimental.pallas import tpu as pltpu

L = 2048
BLK = 128


def gram_kernel(src_left, src_right, tile_ref, mask_ref, flag_ref, g_ref, w_ref, diag_ref, *rest):
    if len(rest) == 4:
        acc_ref, out_ref, s_ref, lt_ref = rest
    else:
        acc_ref = None
        out_ref, s_ref, lt_ref = rest
    k = pl.program_id(0)
    row_blocks = g_ref.shape[0] // BLK
    col_blocks = g_ref.shape[1] // BLK

    @pl.when(k == 0)
    def _():
        def fill(j, carry):
            src = src_right[j]
            c0 = pl.multiple_of(src * BLK, BLK)
            d0 = pl.multiple_of(j * BLK, BLK)
            for rb in range(row_blocks):
                live = mask_ref[rb * col_blocks + src].astype(jnp.float32)
                vals = g_ref[rb * BLK:(rb + 1) * BLK, pl.ds(c0, BLK)].astype(jnp.float32)
                wts = w_ref[rb * BLK:(rb + 1) * BLK, :]
                s_ref[rb * BLK:(rb + 1) * BLK, pl.ds(d0, BLK)] = (wts * (vals * live)).astype(jnp.bfloat16)
            return carry
        lax.fori_loop(0, col_blocks, fill, 0)

    src = src_left[k]
    c0 = pl.multiple_of(src * BLK, BLK)
    for rb in range(row_blocks):
        live = mask_ref[rb * col_blocks + src].astype(jnp.float32)
        vals = g_ref[rb * BLK:(rb + 1) * BLK, pl.ds(c0, BLK)].astype(jnp.float32) * live
        lt_ref[:, rb * BLK:(rb + 1) * BLK] = vals.T.astype(jnp.bfloat16)
    term = jnp.dot(lt_ref[...], s_ref[...], preferred_element_type=jnp.float32)
    if acc_ref is None:
        out_ref[...] = term
        blk = tile_ref[k]
        e0 = pl.multiple_of(blk * BLK, BLK)
        rows = lax.broadcasted_iota(jnp.int32, (BLK, BLK), 0)
        cols = lax.broadcasted_iota(jnp.int32, (BLK, BLK), 1)
        dvals = diag_ref[pl.ds(blk, 1), :] * flag_ref[k].astype(jnp.float32)
        out_ref[:, pl.ds(e0, BLK)] += jnp.where(rows == cols, dvals, 0.0)
    else:
        out_ref[...] = acc_ref[...] + term


def gram_rows(slab, weights, live_blocks, src_left, src_right, out_tiles, diagonal, flags, group, acc=None):
    height = slab.shape[0]
    col_blocks = L // BLK
    out_blocks = src_left.shape[0]
    in_specs = [
        pl.BlockSpec((height, L), lambda k, *_: (0, 0)),
        pl.BlockSpec((height, 1), lambda k, *_: (0, 0)),
        pl.BlockSpec((col_blocks, BLK), lambda k, *_: (0, 0)),
    ]
    operands = [slab, weights.reshape(height, 1), diagonal.reshape(col_blocks, BLK)]
    aliases = {}
    out_spec = pl.BlockSpec((None, BLK, L), lambda k, *_: (k // group, k % group, 0))
    if acc is not None:
        in_specs.append(out_spec)
        operands.append(acc)
        aliases = {8: 0}
    grid_spec = pltpu.PrefetchScalarGridSpec(
        num_scalar_prefetch=5,
        grid=(out_blocks,),
        in_specs=in_specs,
        out_specs=out_spec,
        scratch_shapes=[pltpu.VMEM((height, L), jnp.bfloat16), pltpu.VMEM((BLK, height), jnp.bfloat16)],
    )
    return pl.pallas_call(
        gram_kernel,
        grid_spec=grid_spec,
        out_shape=jax.ShapeDtypeStruct((out_blocks // group, group * BLK, L), jnp.float32),
        input_output_aliases=aliases,
        compiler_params=pltpu.CompilerParams(vmem_limit_bytes=56 * 1024 * 1024),
    )(src_left, src_right, out_tiles, live_blocks.reshape(-1), flags, *operands)


HIGHEST = lax.Precision.HIGHEST


def join_segments(earlier_seg, later_seg):
    top_one, cross_one, bottom_one = earlier_seg
    top_two, cross_two, bottom_two = later_seg
    middle = bottom_one + top_two
    middle = 0.5 * (middle + middle.T)
    factor = jnp.linalg.cholesky(middle)
    half_width = top_one.shape[0]
    solved = lax.linalg.triangular_solve(
        factor, jnp.concatenate([cross_one.T, cross_two], axis=1), left_side=True, lower=True
    )
    solve_one = solved[:, :half_width]
    solve_two = solved[:, half_width:]
    top_new = top_one - jnp.dot(solve_one.T, solve_one, precision=HIGHEST)
    cross_new = -jnp.dot(solve_one.T, solve_two, precision=HIGHEST)
    bottom_new = bottom_two - jnp.dot(solve_two.T, solve_two, precision=HIGHEST)
    return (top_new, cross_new, bottom_new)


def contract_rows(left_cols, right_cols):
    return lax.dot_general(
        left_cols, right_cols, (((0,), (0,)), ((), ())), preferred_element_type=jnp.float32
    )


def local(coupling, row_scale, block_mask, link_map, tile_order, link_diag):
    local_slab = coupling[0]
    row_weights = row_scale[0]
    live_blocks = block_mask[0]
    block_map = link_map[0]
    diagonal = link_diag[0]
    slab_height = local_slab.shape[0]
    block_count = L // BLK
    my_index = lax.axis_index("row")
    block_ids = jnp.arange(block_count, dtype=jnp.int32)
    source = jnp.sum(
        block_ids[None, :] * (block_map[None, :] == block_ids[:, None]).astype(jnp.int32), axis=1
    )

    def edge_cols(global_block):
        local_block = source[global_block]
        cols = lax.dynamic_slice_in_dim(local_slab, local_block * BLK, BLK, axis=1)
        live = lax.dynamic_index_in_dim(live_blocks, local_block, 1, False)
        cols = (cols.reshape(slab_height // BLK, BLK, BLK) * live.astype(jnp.bfloat16)[:, None, None])
        cols = cols.reshape(slab_height, BLK)
        weighted = (row_weights[:, None] * cols.astype(jnp.float32)).astype(jnp.bfloat16)
        return cols, weighted

    first_cols, first_scaled = edge_cols(0)
    final_cols, final_scaled = edge_cols(block_count - 1)
    part_pieces = jnp.stack(
        [
            contract_rows(first_cols, first_scaled),
            contract_rows(first_cols, final_scaled),
            contract_rows(final_cols, final_scaled),
        ]
    )
    owners = lax.axis_size("row")
    own_blocks = block_count // owners

    def exchange(value, step):
        return lax.ppermute(value, "row", [(src, src ^ step) for src in range(owners)])

    kernel_slab, part_pieces = lax.optimization_barrier((local_slab, part_pieces))
    summed = lax.psum(part_pieces, "row")
    eye = jnp.eye(BLK, dtype=jnp.float32)
    segment = jnp.stack([
        summed[0] + eye * diagonal[:BLK][None, :],
        summed[1],
        summed[2] + eye * diagonal[L - BLK :][None, :],
    ])

    if owners == 4:
        packed_side = jnp.concatenate([row_weights, live_blocks.reshape(-1).astype(jnp.float32)])
        across_slab = exchange(local_slab, 2)
        across_side = exchange(packed_side, 2)
        across_weights = across_side[:slab_height]
        across_live = across_side[slab_height:].reshape(live_blocks.shape).astype(jnp.int32)
        order = jnp.concatenate(
            [lax.dynamic_slice_in_dim(tile_order, (my_index ^ q) * own_blocks, own_blocks) for q in range(2)]
        )
        flags = (jnp.arange(2 * own_blocks) < own_blocks).astype(jnp.int32)
        left_src = jnp.take(source, order)
        partial = gram_rows(
            kernel_slab, row_weights, live_blocks, left_src, source, order, diagonal, flags, own_blocks,
        )
        partial, segment = lax.optimization_barrier((partial, segment))
        partial = gram_rows(
            across_slab, across_weights, across_live, left_src, source, order, diagonal, flags,
            own_blocks, partial,
        )
        owned = partial[0] + exchange(partial[1], 1)
    else:
        flags = jnp.full((block_count,), (my_index == 0).astype(jnp.int32))
        partial = gram_rows(
            kernel_slab, row_weights, live_blocks, jnp.take(source, tile_order), source,
            tile_order, diagonal, flags, own_blocks,
        )
        owned = lax.psum_scatter(
            partial.reshape(L, L), "row", scatter_dimension=0, tiled=True
        )

    times = lax.axis_size("tm")
    position = lax.axis_index("tm")
    running = (segment[0], segment[1], segment[2])
    shift = 1
    while shift < times:
        pairs = [(src, src + shift) for src in range(times - shift)]
        moved = lax.ppermute(jnp.stack(running), "tm", pairs)
        earlier = (moved[0], moved[1], moved[2])
        joined = join_segments(earlier, running)
        take = position >= shift
        running = tuple(jnp.where(take, new, old) for new, old in zip(joined, running))
        shift *= 2
    chain_out = jnp.stack(running)[None]
    return (owned[None], chain_out)


def solution(mesh):
    placed = (
        P("tm", "row", None),
        P("tm", "row"),
        P("tm", "row", None),
        P("tm", None),
        P(),
        P("tm", None),
    )
    return jax.shard_map(
        local,
        mesh=mesh,
        in_specs=placed,
        out_specs=(P("tm", "row", None), P("tm", None, None, None)),
        check_vma=False,
    )
```

```python
import jax
import jax.numpy as jnp
from jax import lax
from jax.sharding import PartitionSpec as P
from jax.experimental import pallas as pl
from jax.experimental.pallas import tpu as pltpu

L = 2048
BLK = 128


def gram_kernel(src_left, src_right, tile_ref, mask_ref, flag_ref, g_ref, w_ref, diag_ref, *rest):
    if len(rest) == 4:
        acc_ref, out_ref, s_ref, lt_ref = rest
    else:
        acc_ref = None
        out_ref, s_ref, lt_ref = rest
    k = pl.program_id(0)
    row_blocks = g_ref.shape[0] // BLK
    col_blocks = g_ref.shape[1] // BLK

    @pl.when(k == 0)
    def _():
        def fill(j, carry):
            src = src_right[j]
            c0 = pl.multiple_of(src * BLK, BLK)
            d0 = pl.multiple_of(j * BLK, BLK)
            for rb in range(row_blocks):
                live = mask_ref[rb * col_blocks + src].astype(jnp.float32)
                vals = g_ref[rb * BLK:(rb + 1) * BLK, pl.ds(c0, BLK)].astype(jnp.float32)
                wts = w_ref[rb * BLK:(rb + 1) * BLK, :]
                s_ref[rb * BLK:(rb + 1) * BLK, pl.ds(d0, BLK)] = (wts * (vals * live)).astype(jnp.bfloat16)
            return carry
        lax.fori_loop(0, col_blocks, fill, 0)

    src = src_left[k]
    c0 = pl.multiple_of(src * BLK, BLK)
    for rb in range(row_blocks):
        live = mask_ref[rb * col_blocks + src].astype(jnp.float32)
        vals = g_ref[rb * BLK:(rb + 1) * BLK, pl.ds(c0, BLK)].astype(jnp.float32) * live
        lt_ref[:, rb * BLK:(rb + 1) * BLK] = vals.T.astype(jnp.bfloat16)
    term = jnp.dot(lt_ref[...], s_ref[...], preferred_element_type=jnp.float32)
    if acc_ref is None:
        out_ref[...] = term
        blk = tile_ref[k]
        e0 = pl.multiple_of(blk * BLK, BLK)
        rows = lax.broadcasted_iota(jnp.int32, (BLK, BLK), 0)
        cols = lax.broadcasted_iota(jnp.int32, (BLK, BLK), 1)
        dvals = diag_ref[pl.ds(blk, 1), :] * flag_ref[k].astype(jnp.float32)
        out_ref[:, pl.ds(e0, BLK)] += jnp.where(rows == cols, dvals, 0.0)
    else:
        out_ref[...] = acc_ref[...] + term


def gram_rows(slab, weights, live_blocks, src_left, src_right, out_tiles, diagonal, flags, group, acc=None):
    height = slab.shape[0]
    col_blocks = L // BLK
    out_blocks = src_left.shape[0]
    in_specs = [
        pl.BlockSpec((height, L), lambda k, *_: (0, 0)),
        pl.BlockSpec((height, 1), lambda k, *_: (0, 0)),
        pl.BlockSpec((col_blocks, BLK), lambda k, *_: (0, 0)),
    ]
    operands = [slab, weights.reshape(height, 1), diagonal.reshape(col_blocks, BLK)]
    aliases = {}
    out_spec = pl.BlockSpec((None, BLK, L), lambda k, *_: (k // group, k % group, 0))
    if acc is not None:
        in_specs.append(out_spec)
        operands.append(acc)
        aliases = {8: 0}
    grid_spec = pltpu.PrefetchScalarGridSpec(
        num_scalar_prefetch=5,
        grid=(out_blocks,),
        in_specs=in_specs,
        out_specs=out_spec,
        scratch_shapes=[pltpu.VMEM((height, L), jnp.bfloat16), pltpu.VMEM((BLK, height), jnp.bfloat16)],
    )
    return pl.pallas_call(
        gram_kernel,
        grid_spec=grid_spec,
        out_shape=jax.ShapeDtypeStruct((out_blocks // group, group * BLK, L), jnp.float32),
        input_output_aliases=aliases,
        compiler_params=pltpu.CompilerParams(vmem_limit_bytes=56 * 1024 * 1024),
    )(src_left, src_right, out_tiles, live_blocks.reshape(-1), flags, *operands)


HIGHEST = lax.Precision.HIGHEST


def join_segments(earlier_seg, later_seg):
    top_one, cross_one, bottom_one = earlier_seg
    top_two, cross_two, bottom_two = later_seg
    middle = bottom_one + top_two
    middle = 0.5 * (middle + middle.T)
    factor = jnp.linalg.cholesky(middle)
    half_width = top_one.shape[0]
    solved = lax.linalg.triangular_solve(
        factor, jnp.concatenate([cross_one.T, cross_two], axis=1), left_side=True, lower=True
    )
    solve_one = solved[:, :half_width]
    solve_two = solved[:, half_width:]
    top_new = top_one - jnp.dot(solve_one.T, solve_one, precision=HIGHEST)
    cross_new = -jnp.dot(solve_one.T, solve_two, precision=HIGHEST)
    bottom_new = bottom_two - jnp.dot(solve_two.T, solve_two, precision=HIGHEST)
    return (top_new, cross_new, bottom_new)


def contract_rows(left_cols, right_cols):
    return lax.dot_general(
        left_cols, right_cols, (((0,), (0,)), ((), ())), preferred_element_type=jnp.float32
    )


def local(coupling, row_scale, block_mask, link_map, tile_order, link_diag):
    local_slab = coupling[0]
    row_weights = row_scale[0]
    live_blocks = block_mask[0]
    block_map = link_map[0]
    diagonal = link_diag[0]
    slab_height = local_slab.shape[0]
    block_count = L // BLK
    my_index = lax.axis_index("row")
    block_ids = jnp.arange(block_count, dtype=jnp.int32)
    source = jnp.sum(
        block_ids[None, :] * (block_map[None, :] == block_ids[:, None]).astype(jnp.int32), axis=1
    )

    def edge_cols(global_block):
        local_block = source[global_block]
        cols = lax.dynamic_slice_in_dim(local_slab, local_block * BLK, BLK, axis=1)
        live = lax.dynamic_index_in_dim(live_blocks, local_block, 1, False)
        cols = (cols.reshape(slab_height // BLK, BLK, BLK) * live.astype(jnp.bfloat16)[:, None, None])
        cols = cols.reshape(slab_height, BLK)
        weighted = (row_weights[:, None] * cols.astype(jnp.float32)).astype(jnp.bfloat16)
        return cols, weighted

    first_cols, first_scaled = edge_cols(0)
    final_cols, final_scaled = edge_cols(block_count - 1)
    part_pieces = jnp.stack(
        [
            contract_rows(first_cols, first_scaled),
            contract_rows(first_cols, final_scaled),
            contract_rows(final_cols, final_scaled),
        ]
    )
    owners = lax.axis_size("row")
    own_blocks = block_count // owners

    def exchange(value, step):
        return lax.ppermute(value, "row", [(src, src ^ step) for src in range(owners)])

    kernel_slab, part_pieces = lax.optimization_barrier((local_slab, part_pieces))
    packed_side = jnp.concatenate([row_weights, live_blocks.reshape(-1).astype(jnp.float32)])
    side_slots = jnp.zeros((owners, packed_side.shape[0]), jnp.float32)
    side_slots = lax.dynamic_update_index_in_dim(side_slots, packed_side, my_index, 0)
    piece_count = part_pieces.size
    summed_all = lax.psum(jnp.concatenate([part_pieces.reshape(-1), side_slots.reshape(-1)]), "row")
    summed = summed_all[:piece_count].reshape(part_pieces.shape)
    every_side = summed_all[piece_count:].reshape(side_slots.shape)
    eye = jnp.eye(BLK, dtype=jnp.float32)
    segment = jnp.stack([
        summed[0] + eye * diagonal[:BLK][None, :],
        summed[1],
        summed[2] + eye * diagonal[L - BLK :][None, :],
    ])

    if owners == 4:
        across_slab = exchange(local_slab, 2)
        across_side = lax.dynamic_index_in_dim(every_side, my_index ^ 2, 0, False)
        across_weights = across_side[:slab_height]
        across_live = across_side[slab_height:].reshape(live_blocks.shape).astype(jnp.int32)
        order = jnp.concatenate(
            [lax.dynamic_slice_in_dim(tile_order, (my_index ^ q) * own_blocks, own_blocks) for q in range(2)]
        )
        flags = (jnp.arange(2 * own_blocks) < own_blocks).astype(jnp.int32)
        left_src = jnp.take(source, order)
        partial = gram_rows(
            kernel_slab, row_weights, live_blocks, left_src, source, order, diagonal, flags, own_blocks,
        )
        partial, segment = lax.optimization_barrier((partial, segment))
        partial = gram_rows(
            across_slab, across_weights, across_live, left_src, source, order, diagonal, flags,
            own_blocks, partial,
        )
        owned = partial[0] + exchange(partial[1], 1)
    else:
        flags = jnp.full((block_count,), (my_index == 0).astype(jnp.int32))
        partial = gram_rows(
            kernel_slab, row_weights, live_blocks, jnp.take(source, tile_order), source,
            tile_order, diagonal, flags, own_blocks,
        )
        owned = lax.psum_scatter(
            partial.reshape(L, L), "row", scatter_dimension=0, tiled=True
        )

    times = lax.axis_size("tm")
    position = lax.axis_index("tm")
    running = (segment[0], segment[1], segment[2])
    shift = 1
    while shift < times:
        pairs = [(src, src + shift) for src in range(times - shift)]
        moved = lax.ppermute(jnp.stack(running), "tm", pairs)
        earlier = (moved[0], moved[1], moved[2])
        joined = join_segments(earlier, running)
        take = position >= shift
        running = tuple(jnp.where(take, new, old) for new, old in zip(joined, running))
        shift *= 2
    chain_out = jnp.stack(running)[None]
    return (owned[None], chain_out)


def solution(mesh):
    placed = (
        P("tm", "row", None),
        P("tm", "row"),
        P("tm", "row", None),
        P("tm", None),
        P(),
        P("tm", None),
    )
    return jax.shard_map(
        local,
        mesh=mesh,
        in_specs=placed,
        out_specs=(P("tm", "row", None), P("tm", None, None, None)),
        check_vma=False,
    )
```

```python
import jax
import jax.numpy as jnp
from jax import lax
from jax.sharding import PartitionSpec as P
from jax.experimental import pallas as pl
from jax.experimental.pallas import tpu as pltpu

L = 2048
BLK = 128


def gram_kernel(src_left, src_right, tile_ref, mask_ref, flag_ref, g_ref, w_ref, diag_ref, *rest):
    if len(rest) == 4:
        acc_ref, out_ref, s_ref, lt_ref = rest
    else:
        acc_ref = None
        out_ref, s_ref, lt_ref = rest
    k = pl.program_id(0)
    row_blocks = g_ref.shape[0] // BLK
    col_blocks = g_ref.shape[1] // BLK

    @pl.when(k == 0)
    def _():
        def fill(j, carry):
            src = src_right[j]
            c0 = pl.multiple_of(src * BLK, BLK)
            d0 = pl.multiple_of(j * BLK, BLK)
            for rb in range(row_blocks):
                live = mask_ref[rb * col_blocks + src].astype(jnp.float32)
                vals = g_ref[rb * BLK:(rb + 1) * BLK, pl.ds(c0, BLK)].astype(jnp.float32)
                wts = w_ref[rb * BLK:(rb + 1) * BLK, :]
                s_ref[rb * BLK:(rb + 1) * BLK, pl.ds(d0, BLK)] = (wts * (vals * live)).astype(jnp.bfloat16)
            return carry
        lax.fori_loop(0, col_blocks, fill, 0)

    src = src_left[k]
    c0 = pl.multiple_of(src * BLK, BLK)
    for rb in range(row_blocks):
        live = mask_ref[rb * col_blocks + src].astype(jnp.float32)
        vals = g_ref[rb * BLK:(rb + 1) * BLK, pl.ds(c0, BLK)].astype(jnp.float32) * live
        lt_ref[:, rb * BLK:(rb + 1) * BLK] = vals.T.astype(jnp.bfloat16)
    term = jnp.dot(lt_ref[...], s_ref[...], preferred_element_type=jnp.float32)
    if acc_ref is None:
        out_ref[...] = term
        blk = tile_ref[k]
        e0 = pl.multiple_of(blk * BLK, BLK)
        rows = lax.broadcasted_iota(jnp.int32, (BLK, BLK), 0)
        cols = lax.broadcasted_iota(jnp.int32, (BLK, BLK), 1)
        dvals = diag_ref[pl.ds(blk, 1), :] * flag_ref[k].astype(jnp.float32)
        out_ref[:, pl.ds(e0, BLK)] += jnp.where(rows == cols, dvals, 0.0)
    else:
        out_ref[...] = acc_ref[...] + term


def gram_rows(slab, weights, live_blocks, src_left, src_right, out_tiles, diagonal, flags, group, acc=None):
    height = slab.shape[0]
    col_blocks = L // BLK
    out_blocks = src_left.shape[0]
    in_specs = [
        pl.BlockSpec((height, L), lambda k, *_: (0, 0)),
        pl.BlockSpec((height, 1), lambda k, *_: (0, 0)),
        pl.BlockSpec((col_blocks, BLK), lambda k, *_: (0, 0)),
    ]
    operands = [slab, weights.reshape(height, 1), diagonal.reshape(col_blocks, BLK)]
    aliases = {}
    out_spec = pl.BlockSpec((None, BLK, L), lambda k, *_: (k // group, k % group, 0))
    if acc is not None:
        in_specs.append(out_spec)
        operands.append(acc)
        aliases = {8: 0}
    grid_spec = pltpu.PrefetchScalarGridSpec(
        num_scalar_prefetch=5,
        grid=(out_blocks,),
        in_specs=in_specs,
        out_specs=out_spec,
        scratch_shapes=[pltpu.VMEM((height, L), jnp.bfloat16), pltpu.VMEM((BLK, height), jnp.bfloat16)],
    )
    return pl.pallas_call(
        gram_kernel,
        grid_spec=grid_spec,
        out_shape=jax.ShapeDtypeStruct((out_blocks // group, group * BLK, L), jnp.float32),
        input_output_aliases=aliases,
        compiler_params=pltpu.CompilerParams(vmem_limit_bytes=56 * 1024 * 1024),
    )(src_left, src_right, out_tiles, live_blocks.reshape(-1), flags, *operands)


HIGHEST = lax.Precision.HIGHEST


def join_segments(earlier_seg, later_seg):
    top_one, cross_one, bottom_one = earlier_seg
    top_two, cross_two, bottom_two = later_seg
    middle = bottom_one + top_two
    middle = 0.5 * (middle + middle.T)
    factor = jnp.linalg.cholesky(middle)
    half_width = top_one.shape[0]
    solved = lax.linalg.triangular_solve(
        factor, jnp.concatenate([cross_one.T, cross_two], axis=1), left_side=True, lower=True
    )
    solve_one = solved[:, :half_width]
    solve_two = solved[:, half_width:]
    top_new = top_one - jnp.dot(solve_one.T, solve_one, precision=HIGHEST)
    cross_new = -jnp.dot(solve_one.T, solve_two, precision=HIGHEST)
    bottom_new = bottom_two - jnp.dot(solve_two.T, solve_two, precision=HIGHEST)
    return (top_new, cross_new, bottom_new)


def contract_rows(left_cols, right_cols):
    return lax.dot_general(
        left_cols, right_cols, (((0,), (0,)), ((), ())), preferred_element_type=jnp.float32
    )


def local(coupling, row_scale, block_mask, link_map, tile_order, link_diag):
    local_slab = coupling[0]
    row_weights = row_scale[0]
    live_blocks = block_mask[0]
    block_map = link_map[0]
    diagonal = link_diag[0]
    slab_height = local_slab.shape[0]
    block_count = L // BLK
    my_index = lax.axis_index("row")
    block_ids = jnp.arange(block_count, dtype=jnp.int32)
    source = jnp.sum(
        block_ids[None, :] * (block_map[None, :] == block_ids[:, None]).astype(jnp.int32), axis=1
    )

    def edge_cols(global_block):
        local_block = source[global_block]
        cols = lax.dynamic_slice_in_dim(local_slab, local_block * BLK, BLK, axis=1)
        live = lax.dynamic_index_in_dim(live_blocks, local_block, 1, False)
        cols = (cols.reshape(slab_height // BLK, BLK, BLK) * live.astype(jnp.bfloat16)[:, None, None])
        cols = cols.reshape(slab_height, BLK)
        weighted = (row_weights[:, None] * cols.astype(jnp.float32)).astype(jnp.bfloat16)
        return cols, weighted

    first_cols, first_scaled = edge_cols(0)
    final_cols, final_scaled = edge_cols(block_count - 1)
    part_pieces = jnp.stack(
        [
            contract_rows(first_cols, first_scaled),
            contract_rows(first_cols, final_scaled),
            contract_rows(final_cols, final_scaled),
        ]
    )
    owners = lax.axis_size("row")
    own_blocks = block_count // owners

    def exchange(value, step):
        return lax.ppermute(value, "row", [(src, src ^ step) for src in range(owners)])

    kernel_slab, part_pieces = lax.optimization_barrier((local_slab, part_pieces))
    packed_side = jnp.concatenate([row_weights, live_blocks.reshape(-1).astype(jnp.float32)])
    side_slots = jnp.zeros((owners, packed_side.shape[0]), jnp.float32)
    side_slots = lax.dynamic_update_index_in_dim(side_slots, packed_side, my_index, 0)
    piece_count = part_pieces.size
    summed_all = jnp.concatenate([part_pieces.reshape(-1), side_slots.reshape(-1)])
    if owners == 4:
        summed_all = summed_all + exchange(summed_all, 1)
        summed_all = summed_all + exchange(summed_all, 2)
    else:
        summed_all = lax.psum(summed_all, "row")
    summed = summed_all[:piece_count].reshape(part_pieces.shape)
    every_side = summed_all[piece_count:].reshape(side_slots.shape)
    eye = jnp.eye(BLK, dtype=jnp.float32)
    segment = jnp.stack([
        summed[0] + eye * diagonal[:BLK][None, :],
        summed[1],
        summed[2] + eye * diagonal[L - BLK :][None, :],
    ])

    if owners == 4:
        send_slab, summed_all = lax.optimization_barrier((local_slab, summed_all))
        across_slab = exchange(send_slab, 2)
        across_side = lax.dynamic_index_in_dim(every_side, my_index ^ 2, 0, False)
        across_weights = across_side[:slab_height]
        across_live = across_side[slab_height:].reshape(live_blocks.shape).astype(jnp.int32)
        order = jnp.concatenate(
            [lax.dynamic_slice_in_dim(tile_order, (my_index ^ q) * own_blocks, own_blocks) for q in range(2)]
        )
        flags = (jnp.arange(2 * own_blocks) < own_blocks).astype(jnp.int32)
        left_src = jnp.take(source, order)
        partial = gram_rows(
            kernel_slab, row_weights, live_blocks, left_src, source, order, diagonal, flags, own_blocks,
        )
        partial, segment = lax.optimization_barrier((partial, segment))
        partial = gram_rows(
            across_slab, across_weights, across_live, left_src, source, order, diagonal, flags,
            own_blocks, partial,
        )
        owned = partial[0] + exchange(partial[1], 1)
    else:
        flags = jnp.full((block_count,), (my_index == 0).astype(jnp.int32))
        partial = gram_rows(
            kernel_slab, row_weights, live_blocks, jnp.take(source, tile_order), source,
            tile_order, diagonal, flags, own_blocks,
        )
        owned = lax.psum_scatter(
            partial.reshape(L, L), "row", scatter_dimension=0, tiled=True
        )

    times = lax.axis_size("tm")
    position = lax.axis_index("tm")
    running = (segment[0], segment[1], segment[2])
    shift = 1
    while shift < times:
        pairs = [(src, src + shift) for src in range(times - shift)]
        moved = lax.ppermute(jnp.stack(running), "tm", pairs)
        earlier = (moved[0], moved[1], moved[2])
        joined = join_segments(earlier, running)
        take = position >= shift
        running = tuple(jnp.where(take, new, old) for new, old in zip(joined, running))
        shift *= 2
    chain_out = jnp.stack(running)[None]
    return (owned[None], chain_out)


def solution(mesh):
    placed = (
        P("tm", "row", None),
        P("tm", "row"),
        P("tm", "row", None),
        P("tm", None),
        P(),
        P("tm", None),
    )
    return jax.shard_map(
        local,
        mesh=mesh,
        in_specs=placed,
        out_specs=(P("tm", "row", None), P("tm", None, None, None)),
        check_vma=False,
    )
```

```python
import jax
import jax.numpy as jnp
from jax import lax
from jax.sharding import PartitionSpec as P
from jax.experimental import pallas as pl
from jax.experimental.pallas import tpu as pltpu

L = 2048
BLK = 128


def gram_kernel(src_left, src_right, tile_ref, mask_ref, flag_ref, g_ref, w_ref, diag_ref, *rest):
    if len(rest) == 4:
        acc_ref, out_ref, s_ref, lt_ref = rest
    else:
        acc_ref = None
        out_ref, s_ref, lt_ref = rest
    k = pl.program_id(0)
    row_blocks = g_ref.shape[0] // BLK
    col_blocks = g_ref.shape[1] // BLK

    @pl.when(k == 0)
    def _():
        def fill(j, carry):
            src = src_right[j]
            c0 = pl.multiple_of(src * BLK, BLK)
            d0 = pl.multiple_of(j * BLK, BLK)
            for rb in range(row_blocks):
                live = mask_ref[rb * col_blocks + src].astype(jnp.float32)
                vals = g_ref[rb * BLK:(rb + 1) * BLK, pl.ds(c0, BLK)].astype(jnp.float32)
                wts = w_ref[rb * BLK:(rb + 1) * BLK, :]
                s_ref[rb * BLK:(rb + 1) * BLK, pl.ds(d0, BLK)] = (wts * (vals * live)).astype(jnp.bfloat16)
            return carry
        lax.fori_loop(0, col_blocks, fill, 0)

    src = src_left[k]
    c0 = pl.multiple_of(src * BLK, BLK)
    for rb in range(row_blocks):
        live = mask_ref[rb * col_blocks + src].astype(jnp.float32)
        vals = g_ref[rb * BLK:(rb + 1) * BLK, pl.ds(c0, BLK)].astype(jnp.float32) * live
        lt_ref[:, rb * BLK:(rb + 1) * BLK] = vals.T.astype(jnp.bfloat16)
    term = jnp.dot(lt_ref[...], s_ref[...], preferred_element_type=jnp.float32)
    if acc_ref is None:
        out_ref[...] = term
        blk = tile_ref[k]
        e0 = pl.multiple_of(blk * BLK, BLK)
        rows = lax.broadcasted_iota(jnp.int32, (BLK, BLK), 0)
        cols = lax.broadcasted_iota(jnp.int32, (BLK, BLK), 1)
        dvals = diag_ref[pl.ds(blk, 1), :] * flag_ref[k].astype(jnp.float32)
        out_ref[:, pl.ds(e0, BLK)] += jnp.where(rows == cols, dvals, 0.0)
    else:
        out_ref[...] = acc_ref[...] + term


def gram_rows(slab, weights, live_blocks, src_left, src_right, out_tiles, diagonal, flags, group, acc=None):
    height = slab.shape[0]
    col_blocks = L // BLK
    out_blocks = src_left.shape[0]
    in_specs = [
        pl.BlockSpec((height, L), lambda k, *_: (0, 0)),
        pl.BlockSpec((height, 1), lambda k, *_: (0, 0)),
        pl.BlockSpec((col_blocks, BLK), lambda k, *_: (0, 0)),
    ]
    operands = [slab, weights.reshape(height, 1), diagonal.reshape(col_blocks, BLK)]
    aliases = {}
    out_spec = pl.BlockSpec((None, BLK, L), lambda k, *_: (k // group, k % group, 0))
    if acc is not None:
        in_specs.append(out_spec)
        operands.append(acc)
        aliases = {8: 0}
    grid_spec = pltpu.PrefetchScalarGridSpec(
        num_scalar_prefetch=5,
        grid=(out_blocks,),
        in_specs=in_specs,
        out_specs=out_spec,
        scratch_shapes=[pltpu.VMEM((height, L), jnp.bfloat16), pltpu.VMEM((BLK, height), jnp.bfloat16)],
    )
    return pl.pallas_call(
        gram_kernel,
        grid_spec=grid_spec,
        out_shape=jax.ShapeDtypeStruct((out_blocks // group, group * BLK, L), jnp.float32),
        input_output_aliases=aliases,
        compiler_params=pltpu.CompilerParams(vmem_limit_bytes=56 * 1024 * 1024),
    )(src_left, src_right, out_tiles, live_blocks.reshape(-1), flags, *operands)


HIGHEST = lax.Precision.HIGHEST


def join_segments(earlier_seg, later_seg):
    top_one, cross_one, bottom_one = earlier_seg
    top_two, cross_two, bottom_two = later_seg
    middle = bottom_one + top_two
    middle = 0.5 * (middle + middle.T)
    factor = jnp.linalg.cholesky(middle)
    half_width = top_one.shape[0]
    solved = lax.linalg.triangular_solve(
        factor, jnp.concatenate([cross_one.T, cross_two], axis=1), left_side=True, lower=True
    )
    solve_one = solved[:, :half_width]
    solve_two = solved[:, half_width:]
    top_new = top_one - jnp.dot(solve_one.T, solve_one, precision=HIGHEST)
    cross_new = -jnp.dot(solve_one.T, solve_two, precision=HIGHEST)
    bottom_new = bottom_two - jnp.dot(solve_two.T, solve_two, precision=HIGHEST)
    return (top_new, cross_new, bottom_new)


def contract_rows(left_cols, right_cols):
    return lax.dot_general(
        left_cols, right_cols, (((0,), (0,)), ((), ())), preferred_element_type=jnp.float32
    )


def local(coupling, row_scale, block_mask, link_map, tile_order, link_diag):
    local_slab = coupling[0]
    row_weights = row_scale[0]
    live_blocks = block_mask[0]
    block_map = link_map[0]
    diagonal = link_diag[0]
    slab_height = local_slab.shape[0]
    block_count = L // BLK
    my_index = lax.axis_index("row")
    block_ids = jnp.arange(block_count, dtype=jnp.int32)
    source = jnp.sum(
        block_ids[None, :] * (block_map[None, :] == block_ids[:, None]).astype(jnp.int32), axis=1
    )

    def edge_cols(global_block):
        local_block = source[global_block]
        cols = lax.dynamic_slice_in_dim(local_slab, local_block * BLK, BLK, axis=1)
        live = lax.dynamic_index_in_dim(live_blocks, local_block, 1, False)
        cols = (cols.reshape(slab_height // BLK, BLK, BLK) * live.astype(jnp.bfloat16)[:, None, None])
        cols = cols.reshape(slab_height, BLK)
        weighted = (row_weights[:, None] * cols.astype(jnp.float32)).astype(jnp.bfloat16)
        return cols, weighted

    first_cols, first_scaled = edge_cols(0)
    final_cols, final_scaled = edge_cols(block_count - 1)
    part_pieces = jnp.stack(
        [
            contract_rows(first_cols, first_scaled),
            contract_rows(first_cols, final_scaled),
            contract_rows(final_cols, final_scaled),
        ]
    )
    owners = lax.axis_size("row")
    own_blocks = block_count // owners

    def exchange(value, step):
        return lax.ppermute(value, "row", [(src, src ^ step) for src in range(owners)])

    packed_side = jnp.concatenate([row_weights, live_blocks.reshape(-1).astype(jnp.float32)])
    side_slots = jnp.zeros((owners, packed_side.shape[0]), jnp.float32)
    side_slots = lax.dynamic_update_index_in_dim(side_slots, packed_side, my_index, 0)
    piece_count = part_pieces.size
    summed_all = jnp.concatenate([part_pieces.reshape(-1), side_slots.reshape(-1)])
    if owners == 4:
        summed_all = summed_all + exchange(summed_all, 1)
        summed_all = summed_all + exchange(summed_all, 2)
    else:
        summed_all = lax.psum(summed_all, "row")
    kernel_slab, summed_all = lax.optimization_barrier((local_slab, summed_all))
    summed = summed_all[:piece_count].reshape(part_pieces.shape)
    every_side = summed_all[piece_count:].reshape(side_slots.shape)
    eye = jnp.eye(BLK, dtype=jnp.float32)
    segment = jnp.stack([
        summed[0] + eye * diagonal[:BLK][None, :],
        summed[1],
        summed[2] + eye * diagonal[L - BLK :][None, :],
    ])

    if owners == 4:
        across_slab = exchange(kernel_slab, 2)
        across_side = lax.dynamic_index_in_dim(every_side, my_index ^ 2, 0, False)
        across_weights = across_side[:slab_height]
        across_live = across_side[slab_height:].reshape(live_blocks.shape).astype(jnp.int32)
        order = jnp.concatenate(
            [lax.dynamic_slice_in_dim(tile_order, (my_index ^ q) * own_blocks, own_blocks) for q in range(2)]
        )
        flags = (jnp.arange(2 * own_blocks) < own_blocks).astype(jnp.int32)
        left_src = jnp.take(source, order)
        partial = gram_rows(
            kernel_slab, row_weights, live_blocks, left_src, source, order, diagonal, flags, own_blocks,
        )
        partial, segment = lax.optimization_barrier((partial, segment))
        partial = gram_rows(
            across_slab, across_weights, across_live, left_src, source, order, diagonal, flags,
            own_blocks, partial,
        )
        owned = partial[0] + exchange(partial[1], 1)
    else:
        flags = jnp.full((block_count,), (my_index == 0).astype(jnp.int32))
        partial = gram_rows(
            kernel_slab, row_weights, live_blocks, jnp.take(source, tile_order), source,
            tile_order, diagonal, flags, own_blocks,
        )
        owned = lax.psum_scatter(
            partial.reshape(L, L), "row", scatter_dimension=0, tiled=True
        )

    times = lax.axis_size("tm")
    position = lax.axis_index("tm")
    running = (segment[0], segment[1], segment[2])
    shift = 1
    while shift < times:
        pairs = [(src, src + shift) for src in range(times - shift)]
        moved = lax.ppermute(jnp.stack(running), "tm", pairs)
        earlier = (moved[0], moved[1], moved[2])
        joined = join_segments(earlier, running)
        take = position >= shift
        running = tuple(jnp.where(take, new, old) for new, old in zip(joined, running))
        shift *= 2
    chain_out = jnp.stack(running)[None]
    return (owned[None], chain_out)


def solution(mesh):
    placed = (
        P("tm", "row", None),
        P("tm", "row"),
        P("tm", "row", None),
        P("tm", None),
        P(),
        P("tm", None),
    )
    return jax.shard_map(
        local,
        mesh=mesh,
        in_specs=placed,
        out_specs=(P("tm", "row", None), P("tm", None, None, None)),
        check_vma=False,
    )
```

```python
import jax
import jax.numpy as jnp
from jax import lax
from jax.sharding import PartitionSpec as P
from jax.experimental import pallas as pl
from jax.experimental.pallas import tpu as pltpu

L = 2048
BLK = 128


def gram_kernel(src_left, src_right, tile_ref, mask_ref, flag_ref, g_ref, w_ref, diag_ref,
                out_ref, s_ref, lt_ref):
    k = pl.program_id(0)
    row_blocks = g_ref.shape[0] // BLK
    col_blocks = g_ref.shape[1] // BLK

    @pl.when(k == 0)
    def _():
        def fill(j, carry):
            src = src_right[j]
            c0 = pl.multiple_of(src * BLK, BLK)
            d0 = pl.multiple_of(j * BLK, BLK)
            for rb in range(row_blocks):
                live = mask_ref[rb * col_blocks + src].astype(jnp.float32)
                vals = g_ref[rb * BLK:(rb + 1) * BLK, pl.ds(c0, BLK)].astype(jnp.float32)
                wts = w_ref[rb * BLK:(rb + 1) * BLK, :]
                s_ref[rb * BLK:(rb + 1) * BLK, pl.ds(d0, BLK)] = (wts * (vals * live)).astype(jnp.bfloat16)
            return carry
        lax.fori_loop(0, col_blocks, fill, 0)

    src = src_left[k]
    c0 = pl.multiple_of(src * BLK, BLK)
    for rb in range(row_blocks):
        live = mask_ref[rb * col_blocks + src].astype(jnp.float32)
        vals = g_ref[rb * BLK:(rb + 1) * BLK, pl.ds(c0, BLK)].astype(jnp.float32) * live
        lt_ref[:, rb * BLK:(rb + 1) * BLK] = vals.T.astype(jnp.bfloat16)
    out_ref[...] = jnp.dot(lt_ref[...], s_ref[...], preferred_element_type=jnp.float32)
    blk = tile_ref[k]
    e0 = pl.multiple_of(blk * BLK, BLK)
    rows = lax.broadcasted_iota(jnp.int32, (BLK, BLK), 0)
    cols = lax.broadcasted_iota(jnp.int32, (BLK, BLK), 1)
    dvals = diag_ref[pl.ds(blk, 1), :] * flag_ref[0].astype(jnp.float32)
    out_ref[:, pl.ds(e0, BLK)] += jnp.where(rows == cols, dvals, 0.0)


def gram_rows(slab, weights, live_blocks, src_left, src_right, tile_order, diagonal, flag):
    height = slab.shape[0]
    col_blocks = L // BLK
    grid_spec = pltpu.PrefetchScalarGridSpec(
        num_scalar_prefetch=5,
        grid=(src_left.shape[0],),
        in_specs=[
            pl.BlockSpec((height, L), lambda k, *_: (0, 0)),
            pl.BlockSpec((height, 1), lambda k, *_: (0, 0)),
            pl.BlockSpec((col_blocks, BLK), lambda k, *_: (0, 0)),
        ],
        out_specs=pl.BlockSpec((BLK, L), lambda k, *_: (k, 0)),
        scratch_shapes=[pltpu.VMEM((height, L), jnp.bfloat16), pltpu.VMEM((BLK, height), jnp.bfloat16)],
    )
    return pl.pallas_call(
        gram_kernel,
        grid_spec=grid_spec,
        out_shape=jax.ShapeDtypeStruct((src_left.shape[0] * BLK, L), jnp.float32),
        compiler_params=pltpu.CompilerParams(vmem_limit_bytes=56 * 1024 * 1024),
    )(src_left, src_right, tile_order, live_blocks.reshape(-1), flag.reshape(1),
      slab, weights.reshape(height, 1), diagonal.reshape(col_blocks, BLK))


HIGHEST = lax.Precision.HIGHEST


def join_segments(earlier_seg, later_seg):
    top_one, cross_one, bottom_one = earlier_seg
    top_two, cross_two, bottom_two = later_seg
    middle = bottom_one + top_two
    middle = 0.5 * (middle + middle.T)
    factor = jnp.linalg.cholesky(middle)
    half_width = top_one.shape[0]
    solved = jax.scipy.linalg.cho_solve(
        (factor, True), jnp.concatenate([cross_one.T, cross_two], axis=1)
    )
    solve_one = solved[:, :half_width]
    solve_two = solved[:, half_width:]
    top_new = top_one - jnp.dot(cross_one, solve_one, precision=HIGHEST)
    cross_new = -jnp.dot(cross_one, solve_two, precision=HIGHEST)
    bottom_new = bottom_two - jnp.dot(cross_two.T, solve_two, precision=HIGHEST)
    return (top_new, cross_new, bottom_new)


def contract_rows(left_cols, right_cols):
    return lax.dot_general(
        left_cols, right_cols, (((0,), (0,)), ((), ())), preferred_element_type=jnp.float32
    )


def local(coupling, row_scale, block_mask, link_map, tile_order, link_diag):
    local_slab = coupling[0]
    row_weights = row_scale[0]
    live_blocks = block_mask[0]
    block_map = link_map[0]
    diagonal = link_diag[0]
    slab_height = local_slab.shape[0]
    block_count = L // BLK
    my_index = lax.axis_index("row")
    block_ids = jnp.arange(block_count, dtype=jnp.int32)
    source = jnp.sum(
        block_ids[None, :] * (block_map[None, :] == block_ids[:, None]).astype(jnp.int32), axis=1
    )

    def edge_cols(global_block):
        local_block = source[global_block]
        cols = lax.dynamic_slice_in_dim(local_slab, local_block * BLK, BLK, axis=1)
        live = lax.dynamic_index_in_dim(live_blocks, local_block, 1, False)
        cols = (cols.reshape(slab_height // BLK, BLK, BLK) * live.astype(jnp.bfloat16)[:, None, None])
        cols = cols.reshape(slab_height, BLK)
        weighted = (row_weights[:, None] * cols.astype(jnp.float32)).astype(jnp.bfloat16)
        return cols, weighted

    first_cols, first_scaled = edge_cols(0)
    final_cols, final_scaled = edge_cols(block_count - 1)
    part_pieces = jnp.stack(
        [
            contract_rows(first_cols, first_scaled),
            contract_rows(first_cols, final_scaled),
            contract_rows(final_cols, final_scaled),
        ]
    )
    summed = lax.psum(part_pieces, "row")
    eye = jnp.eye(BLK, dtype=jnp.float32)
    segment = (
        summed[0] + eye * diagonal[:BLK][None, :],
        summed[1],
        summed[2] + eye * diagonal[L - BLK :][None, :],
    )

    times = lax.axis_size("tm")
    position = lax.axis_index("tm")
    running = segment
    shift = 1
    while shift < times:
        pairs = [(src, src + shift) for src in range(times - shift)]
        moved = lax.ppermute(jnp.stack(running), "tm", pairs)
        earlier = (moved[0], moved[1], moved[2])
        joined = join_segments(earlier, running)
        take = position >= shift
        running = tuple(jnp.where(take, new, old) for new, old in zip(joined, running))
        shift *= 2
    chain_out = jnp.stack(running)[None]

    flag = (my_index == 0).astype(jnp.int32)
    owners = lax.axis_size("row")
    own_blocks = block_count // owners
    half = max(own_blocks // 2, 1)
    by_owner = tile_order.reshape(owners, own_blocks)
    pieces = []
    for lo, hi in ((0, half), (half, own_blocks)):
        if lo == hi:
            continue
        order = by_owner[:, lo:hi].reshape(-1)
        partial = gram_rows(
            local_slab, row_weights, live_blocks, jnp.take(source, order), source,
            order, diagonal, flag,
        )
        pieces.append(lax.psum_scatter(partial, "row", scatter_dimension=0, tiled=True))
    owned = jnp.concatenate(pieces, axis=0) if len(pieces) > 1 else pieces[0]
    return (owned[None], chain_out)


def solution(mesh):
    placed = (
        P("tm", "row", None),
        P("tm", "row"),
        P("tm", "row", None),
        P("tm", None),
        P(),
        P("tm", None),
    )
    return jax.shard_map(
        local,
        mesh=mesh,
        in_specs=placed,
        out_specs=(P("tm", "row", None), P("tm", None, None, None)),
        check_vma=False,
    )
```

```python
import jax
import jax.numpy as jnp
from jax import lax
from jax.sharding import PartitionSpec as P
from jax.experimental import pallas as pl
from jax.experimental.pallas import tpu as pltpu

L = 2048
BLK = 128


def gram_kernel(src_left, src_right, tile_ref, mask_ref, flag_ref, g_ref, w_ref, diag_ref, *rest):
    if len(rest) == 4:
        acc_ref, out_ref, s_ref, lt_ref = rest
    else:
        acc_ref = None
        out_ref, s_ref, lt_ref = rest
    k = pl.program_id(0)
    row_blocks = g_ref.shape[0] // BLK
    col_blocks = g_ref.shape[1] // BLK

    @pl.when(k == 0)
    def _():
        def fill(j, carry):
            src = src_right[j]
            c0 = pl.multiple_of(src * BLK, BLK)
            d0 = pl.multiple_of(j * BLK, BLK)
            for rb in range(row_blocks):
                live = mask_ref[rb * col_blocks + src].astype(jnp.float32)
                vals = g_ref[rb * BLK:(rb + 1) * BLK, pl.ds(c0, BLK)].astype(jnp.float32)
                wts = w_ref[rb * BLK:(rb + 1) * BLK, :]
                s_ref[rb * BLK:(rb + 1) * BLK, pl.ds(d0, BLK)] = (wts * (vals * live)).astype(jnp.bfloat16)
            return carry
        lax.fori_loop(0, col_blocks, fill, 0)

    src = src_left[k]
    c0 = pl.multiple_of(src * BLK, BLK)
    for rb in range(row_blocks):
        live = mask_ref[rb * col_blocks + src].astype(jnp.float32)
        vals = g_ref[rb * BLK:(rb + 1) * BLK, pl.ds(c0, BLK)].astype(jnp.float32) * live
        lt_ref[:, rb * BLK:(rb + 1) * BLK] = vals.T.astype(jnp.bfloat16)
    term = jnp.dot(lt_ref[...], s_ref[...], preferred_element_type=jnp.float32)
    if acc_ref is None:
        out_ref[...] = term
        blk = tile_ref[k]
        e0 = pl.multiple_of(blk * BLK, BLK)
        rows = lax.broadcasted_iota(jnp.int32, (BLK, BLK), 0)
        cols = lax.broadcasted_iota(jnp.int32, (BLK, BLK), 1)
        dvals = diag_ref[pl.ds(blk, 1), :] * flag_ref[k].astype(jnp.float32)
        out_ref[:, pl.ds(e0, BLK)] += jnp.where(rows == cols, dvals, 0.0)
    else:
        out_ref[...] = acc_ref[...] + term


def gram_rows(slab, weights, live_blocks, src_left, src_right, out_tiles, diagonal, flags, group, acc=None):
    height = slab.shape[0]
    col_blocks = L // BLK
    out_blocks = src_left.shape[0]
    in_specs = [
        pl.BlockSpec((height, L), lambda k, *_: (0, 0)),
        pl.BlockSpec((height, 1), lambda k, *_: (0, 0)),
        pl.BlockSpec((col_blocks, BLK), lambda k, *_: (0, 0)),
    ]
    operands = [slab, weights.reshape(height, 1), diagonal.reshape(col_blocks, BLK)]
    aliases = {}
    out_spec = pl.BlockSpec((None, BLK, L), lambda k, *_: (k // group, k % group, 0))
    if acc is not None:
        in_specs.append(out_spec)
        operands.append(acc)
        aliases = {8: 0}
    grid_spec = pltpu.PrefetchScalarGridSpec(
        num_scalar_prefetch=5,
        grid=(out_blocks,),
        in_specs=in_specs,
        out_specs=out_spec,
        scratch_shapes=[pltpu.VMEM((height, L), jnp.bfloat16), pltpu.VMEM((BLK, height), jnp.bfloat16)],
    )
    return pl.pallas_call(
        gram_kernel,
        grid_spec=grid_spec,
        out_shape=jax.ShapeDtypeStruct((out_blocks // group, group * BLK, L), jnp.float32),
        input_output_aliases=aliases,
        compiler_params=pltpu.CompilerParams(vmem_limit_bytes=56 * 1024 * 1024),
    )(src_left, src_right, out_tiles, live_blocks.reshape(-1), flags, *operands)


HIGHEST = lax.Precision.HIGHEST


def join_segments(earlier_seg, later_seg):
    top_one, cross_one, bottom_one = earlier_seg
    top_two, cross_two, bottom_two = later_seg
    middle = bottom_one + top_two
    middle = 0.5 * (middle + middle.T)
    factor = jnp.linalg.cholesky(middle)
    half_width = top_one.shape[0]
    solved = lax.linalg.triangular_solve(
        factor, jnp.concatenate([cross_one.T, cross_two], axis=1), left_side=True, lower=True
    )
    solve_one = solved[:, :half_width]
    solve_two = solved[:, half_width:]
    top_new = top_one - jnp.dot(solve_one.T, solve_one, precision=HIGHEST)
    cross_new = -jnp.dot(solve_one.T, solve_two, precision=HIGHEST)
    bottom_new = bottom_two - jnp.dot(solve_two.T, solve_two, precision=HIGHEST)
    return (top_new, cross_new, bottom_new)


def contract_rows(left_cols, right_cols):
    return lax.dot_general(
        left_cols, right_cols, (((0,), (0,)), ((), ())), preferred_element_type=jnp.float32
    )


def local(coupling, row_scale, block_mask, link_map, tile_order, link_diag):
    local_slab = coupling[0]
    row_weights = row_scale[0]
    live_blocks = block_mask[0]
    block_map = link_map[0]
    diagonal = link_diag[0]
    slab_height = local_slab.shape[0]
    block_count = L // BLK
    my_index = lax.axis_index("row")
    block_ids = jnp.arange(block_count, dtype=jnp.int32)
    source = jnp.sum(
        block_ids[None, :] * (block_map[None, :] == block_ids[:, None]).astype(jnp.int32), axis=1
    )

    def edge_cols(global_block):
        local_block = source[global_block]
        cols = lax.dynamic_slice_in_dim(local_slab, local_block * BLK, BLK, axis=1)
        live = lax.dynamic_index_in_dim(live_blocks, local_block, 1, False)
        cols = (cols.reshape(slab_height // BLK, BLK, BLK) * live.astype(jnp.bfloat16)[:, None, None])
        cols = cols.reshape(slab_height, BLK)
        weighted = (row_weights[:, None] * cols.astype(jnp.float32)).astype(jnp.bfloat16)
        return cols, weighted

    first_cols, first_scaled = edge_cols(0)
    final_cols, final_scaled = edge_cols(block_count - 1)
    part_pieces = jnp.stack(
        [
            contract_rows(first_cols, first_scaled),
            contract_rows(first_cols, final_scaled),
            contract_rows(final_cols, final_scaled),
        ]
    )
    owners = lax.axis_size("row")
    own_blocks = block_count // owners

    def exchange(value, step):
        return lax.ppermute(value, "row", [(src, src ^ step) for src in range(owners)])

    packed_side = jnp.concatenate([row_weights, live_blocks.reshape(-1).astype(jnp.float32)])
    side_slots = jnp.zeros((owners, packed_side.shape[0]), jnp.float32)
    side_slots = lax.dynamic_update_index_in_dim(side_slots, packed_side, my_index, 0)
    piece_count = part_pieces.size
    summed_all = jnp.concatenate([part_pieces.reshape(-1), side_slots.reshape(-1)])
    if owners == 4:
        summed_all = summed_all + exchange(summed_all, 1)
        summed_all = summed_all + exchange(summed_all, 2)
    else:
        summed_all = lax.psum(summed_all, "row")
    kernel_slab, summed_all = lax.optimization_barrier((local_slab, summed_all))
    summed = summed_all[:piece_count].reshape(part_pieces.shape)
    every_side = summed_all[piece_count:].reshape(side_slots.shape)
    eye = jnp.eye(BLK, dtype=jnp.float32)
    segment = jnp.stack([
        summed[0] + eye * diagonal[:BLK][None, :],
        summed[1],
        summed[2] + eye * diagonal[L - BLK :][None, :],
    ])

    if owners == 4:
        across_slab = exchange(kernel_slab, 2)
        across_side = lax.dynamic_index_in_dim(every_side, my_index ^ 2, 0, False)
        across_weights = across_side[:slab_height]
        across_live = across_side[slab_height:].reshape(live_blocks.shape).astype(jnp.int32)
        order = jnp.concatenate(
            [lax.dynamic_slice_in_dim(tile_order, (my_index ^ q) * own_blocks, own_blocks) for q in range(2)]
        )
        flags = (jnp.arange(2 * own_blocks) < own_blocks).astype(jnp.int32)
        left_src = jnp.take(source, order)

        def own_part(slab_in):
            return gram_rows(
                slab_in, row_weights, live_blocks, left_src, source, order, diagonal, flags, own_blocks,
            )

        def across_part(slab_in, partial):
            total = gram_rows(
                slab_in, across_weights, across_live, left_src, source, order, diagonal, flags,
                own_blocks, partial,
            )
            return total[0] + exchange(total[1], 1)

        hooks = {1: ("own", kernel_slab), 2: ("across", across_slab)}
    else:
        hooks = {}
        flags = jnp.full((block_count,), (my_index == 0).astype(jnp.int32))
        partial = gram_rows(
            kernel_slab, row_weights, live_blocks, jnp.take(source, tile_order), source,
            tile_order, diagonal, flags, own_blocks,
        )
        owned = lax.psum_scatter(
            partial.reshape(L, L), "row", scatter_dimension=0, tiled=True
        )

    times = lax.axis_size("tm")
    position = lax.axis_index("tm")
    running = (segment[0], segment[1], segment[2])
    shift = 1
    round_index = 0
    state = {}

    def run_hook(kind, slab_in, running):
        slab_in, running = lax.optimization_barrier((slab_in, running))
        if kind == "own":
            state["partial"] = own_part(slab_in)
        else:
            state["owned"] = across_part(slab_in, state["partial"])
        return running

    while shift < times:
        if round_index in hooks:
            running = run_hook(*hooks.pop(round_index), running)
        round_index += 1
        pairs = [(src, src + shift) for src in range(times - shift)]
        moved = lax.ppermute(jnp.stack(running), "tm", pairs)
        earlier = (moved[0], moved[1], moved[2])
        joined = join_segments(earlier, running)
        take = position >= shift
        running = tuple(jnp.where(take, new, old) for new, old in zip(joined, running))
        shift *= 2
    for key in sorted(hooks):
        running = run_hook(*hooks[key], running)
    if "owned" in state:
        owned = state["owned"]
    chain_out = jnp.stack(running)[None]
    return (owned[None], chain_out)


def solution(mesh):
    placed = (
        P("tm", "row", None),
        P("tm", "row"),
        P("tm", "row", None),
        P("tm", None),
        P(),
        P("tm", None),
    )
    return jax.shard_map(
        local,
        mesh=mesh,
        in_specs=placed,
        out_specs=(P("tm", "row", None), P("tm", None, None, None)),
        check_vma=False,
    )
```

```python
import functools

import jax
import jax.numpy as jnp
from jax import lax
from jax.sharding import PartitionSpec as P
from jax.experimental import pallas as pl
from jax.experimental.pallas import tpu as pltpu

L = 2048
BLK = 128


def gram_kernel(src_left, src_right, tile_ref, mask_ref, flag_ref, g_ref, w_ref, diag_ref, *rest):
    if len(rest) == 4:
        acc_ref, out_ref, s_ref, lt_ref = rest
    else:
        acc_ref = None
        out_ref, s_ref, lt_ref = rest
    k = pl.program_id(0)
    row_blocks = g_ref.shape[0] // BLK
    col_blocks = g_ref.shape[1] // BLK

    @pl.when(k == 0)
    def _():
        def fill(j, carry):
            src = src_right[j]
            c0 = pl.multiple_of(src * BLK, BLK)
            d0 = pl.multiple_of(j * BLK, BLK)
            for rb in range(row_blocks):
                live = mask_ref[rb * col_blocks + src].astype(jnp.float32)
                vals = g_ref[rb * BLK:(rb + 1) * BLK, pl.ds(c0, BLK)].astype(jnp.float32)
                wts = w_ref[rb * BLK:(rb + 1) * BLK, :]
                s_ref[rb * BLK:(rb + 1) * BLK, pl.ds(d0, BLK)] = (wts * (vals * live)).astype(jnp.bfloat16)
            return carry
        lax.fori_loop(0, col_blocks, fill, 0)

    src = src_left[k]
    c0 = pl.multiple_of(src * BLK, BLK)
    for rb in range(row_blocks):
        live = mask_ref[rb * col_blocks + src].astype(jnp.float32)
        vals = g_ref[rb * BLK:(rb + 1) * BLK, pl.ds(c0, BLK)].astype(jnp.float32) * live
        lt_ref[:, rb * BLK:(rb + 1) * BLK] = vals.T.astype(jnp.bfloat16)
    term = jnp.dot(lt_ref[...], s_ref[...], preferred_element_type=jnp.float32)
    if acc_ref is None:
        out_ref[...] = term
        blk = tile_ref[k]
        e0 = pl.multiple_of(blk * BLK, BLK)
        rows = lax.broadcasted_iota(jnp.int32, (BLK, BLK), 0)
        cols = lax.broadcasted_iota(jnp.int32, (BLK, BLK), 1)
        dvals = diag_ref[pl.ds(blk, 1), :] * flag_ref[k].astype(jnp.float32)
        out_ref[:, pl.ds(e0, BLK)] += jnp.where(rows == cols, dvals, 0.0)
    else:
        out_ref[...] = acc_ref[...] + term


def gram_rows(slab, weights, live_blocks, src_left, src_right, out_tiles, diagonal, flags, group, acc=None):
    height = slab.shape[0]
    col_blocks = L // BLK
    out_blocks = src_left.shape[0]
    in_specs = [
        pl.BlockSpec((height, L), lambda k, *_: (0, 0)),
        pl.BlockSpec((height, 1), lambda k, *_: (0, 0)),
        pl.BlockSpec((col_blocks, BLK), lambda k, *_: (0, 0)),
    ]
    operands = [slab, weights.reshape(height, 1), diagonal.reshape(col_blocks, BLK)]
    aliases = {}
    out_spec = pl.BlockSpec((None, BLK, L), lambda k, *_: (k // group, k % group, 0))
    if acc is not None:
        in_specs.append(out_spec)
        operands.append(acc)
        aliases = {8: 0}
    grid_spec = pltpu.PrefetchScalarGridSpec(
        num_scalar_prefetch=5,
        grid=(out_blocks,),
        in_specs=in_specs,
        out_specs=out_spec,
        scratch_shapes=[pltpu.VMEM((height, L), jnp.bfloat16), pltpu.VMEM((BLK, height), jnp.bfloat16)],
    )
    return pl.pallas_call(
        gram_kernel,
        grid_spec=grid_spec,
        out_shape=jax.ShapeDtypeStruct((out_blocks // group, group * BLK, L), jnp.float32),
        input_output_aliases=aliases,
        compiler_params=pltpu.CompilerParams(vmem_limit_bytes=56 * 1024 * 1024),
    )(src_left, src_right, out_tiles, live_blocks.reshape(-1), flags, *operands)


def split_kernel(src_left, src_right, tile_ref, mask_ref, flag_ref, g_ref, w_ref, diag_ref, *rest,
                 group, accumulate):
    if accumulate:
        acc_first, acc_second, out_first, out_second, s_ref, lt_ref = rest
    else:
        acc_first = acc_second = None
        out_first, out_second, s_ref, lt_ref = rest
    k = pl.program_id(0)
    row_blocks = g_ref.shape[0] // BLK
    col_blocks = g_ref.shape[1] // BLK

    @pl.when(k == 0)
    def _():
        def fill(j, carry):
            src = src_right[j]
            c0 = pl.multiple_of(src * BLK, BLK)
            d0 = pl.multiple_of(j * BLK, BLK)
            for rb in range(row_blocks):
                live = mask_ref[rb * col_blocks + src].astype(jnp.float32)
                vals = g_ref[rb * BLK:(rb + 1) * BLK, pl.ds(c0, BLK)].astype(jnp.float32)
                wts = w_ref[rb * BLK:(rb + 1) * BLK, :]
                s_ref[rb * BLK:(rb + 1) * BLK, pl.ds(d0, BLK)] = (wts * (vals * live)).astype(jnp.bfloat16)
            return carry
        lax.fori_loop(0, col_blocks, fill, 0)

    src = src_left[k]
    c0 = pl.multiple_of(src * BLK, BLK)
    for rb in range(row_blocks):
        live = mask_ref[rb * col_blocks + src].astype(jnp.float32)
        vals = g_ref[rb * BLK:(rb + 1) * BLK, pl.ds(c0, BLK)].astype(jnp.float32) * live
        lt_ref[:, rb * BLK:(rb + 1) * BLK] = vals.T.astype(jnp.bfloat16)
    term = jnp.dot(lt_ref[...], s_ref[...], preferred_element_type=jnp.float32)

    def store(out_ref, acc_ref):
        if acc_ref is None:
            out_ref[...] = term
            blk = tile_ref[k]
            e0 = pl.multiple_of(blk * BLK, BLK)
            rows = lax.broadcasted_iota(jnp.int32, (BLK, BLK), 0)
            cols = lax.broadcasted_iota(jnp.int32, (BLK, BLK), 1)
            dvals = diag_ref[pl.ds(blk, 1), :] * flag_ref[k].astype(jnp.float32)
            out_ref[:, pl.ds(e0, BLK)] += jnp.where(rows == cols, dvals, 0.0)
        else:
            out_ref[...] = acc_ref[...] + term

    @pl.when(k < group)
    def _():
        store(out_first, acc_first)

    @pl.when(k >= group)
    def _():
        store(out_second, acc_second)


def split_rows(slab, weights, live_blocks, src_left, src_right, out_tiles, diagonal, flags, group,
               acc=None):
    height = slab.shape[0]
    col_blocks = L // BLK
    in_specs = [
        pl.BlockSpec((height, L), lambda k, *_: (0, 0)),
        pl.BlockSpec((height, 1), lambda k, *_: (0, 0)),
        pl.BlockSpec((col_blocks, BLK), lambda k, *_: (0, 0)),
    ]
    operands = [slab, weights.reshape(height, 1), diagonal.reshape(col_blocks, BLK)]
    first_spec = pl.BlockSpec((BLK, L), lambda k, *_: (jnp.minimum(k, group - 1), 0))
    second_spec = pl.BlockSpec((BLK, L), lambda k, *_: (jnp.maximum(k - group, 0), 0))
    aliases = {}
    if acc is not None:
        in_specs += [first_spec, second_spec]
        operands += list(acc)
        aliases = {8: 0, 9: 1}
    grid_spec = pltpu.PrefetchScalarGridSpec(
        num_scalar_prefetch=5,
        grid=(2 * group,),
        in_specs=in_specs,
        out_specs=[first_spec, second_spec],
        scratch_shapes=[pltpu.VMEM((height, L), jnp.bfloat16), pltpu.VMEM((BLK, height), jnp.bfloat16)],
    )
    shape = jax.ShapeDtypeStruct((group * BLK, L), jnp.float32)
    return pl.pallas_call(
        functools.partial(split_kernel, group=group, accumulate=acc is not None),
        grid_spec=grid_spec,
        out_shape=(shape, shape),
        input_output_aliases=aliases,
        compiler_params=pltpu.CompilerParams(vmem_limit_bytes=56 * 1024 * 1024),
    )(src_left, src_right, out_tiles, live_blocks.reshape(-1), flags, *operands)


HIGHEST = lax.Precision.HIGHEST


def join_segments(earlier_seg, later_seg):
    top_one, cross_one, bottom_one = earlier_seg
    top_two, cross_two, bottom_two = later_seg
    middle = bottom_one + top_two
    middle = 0.5 * (middle + middle.T)
    factor = jnp.linalg.cholesky(middle)
    half_width = top_one.shape[0]
    solved = lax.linalg.triangular_solve(
        factor, jnp.concatenate([cross_one.T, cross_two], axis=1), left_side=True, lower=True
    )
    solve_one = solved[:, :half_width]
    solve_two = solved[:, half_width:]
    top_new = top_one - jnp.dot(solve_one.T, solve_one, precision=HIGHEST)
    cross_new = -jnp.dot(solve_one.T, solve_two, precision=HIGHEST)
    bottom_new = bottom_two - jnp.dot(solve_two.T, solve_two, precision=HIGHEST)
    return (top_new, cross_new, bottom_new)


def contract_rows(left_cols, right_cols):
    return lax.dot_general(
        left_cols, right_cols, (((0,), (0,)), ((), ())), preferred_element_type=jnp.float32
    )


def local(coupling, row_scale, block_mask, link_map, tile_order, link_diag):
    local_slab = coupling[0]
    row_weights = row_scale[0]
    live_blocks = block_mask[0]
    block_map = link_map[0]
    diagonal = link_diag[0]
    slab_height = local_slab.shape[0]
    block_count = L // BLK
    my_index = lax.axis_index("row")
    block_ids = jnp.arange(block_count, dtype=jnp.int32)
    source = jnp.sum(
        block_ids[None, :] * (block_map[None, :] == block_ids[:, None]).astype(jnp.int32), axis=1
    )

    def edge_cols(global_block):
        local_block = source[global_block]
        cols = lax.dynamic_slice_in_dim(local_slab, local_block * BLK, BLK, axis=1)
        live = lax.dynamic_index_in_dim(live_blocks, local_block, 1, False)
        cols = (cols.reshape(slab_height // BLK, BLK, BLK) * live.astype(jnp.bfloat16)[:, None, None])
        cols = cols.reshape(slab_height, BLK)
        weighted = (row_weights[:, None] * cols.astype(jnp.float32)).astype(jnp.bfloat16)
        return cols, weighted

    first_cols, first_scaled = edge_cols(0)
    final_cols, final_scaled = edge_cols(block_count - 1)
    part_pieces = jnp.stack(
        [
            contract_rows(first_cols, first_scaled),
            contract_rows(first_cols, final_scaled),
            contract_rows(final_cols, final_scaled),
        ]
    )
    owners = lax.axis_size("row")
    own_blocks = block_count // owners

    def exchange(value, step):
        return lax.ppermute(value, "row", [(src, src ^ step) for src in range(owners)])

    packed_side = jnp.concatenate([row_weights, live_blocks.reshape(-1).astype(jnp.float32)])
    side_slots = jnp.zeros((owners, packed_side.shape[0]), jnp.float32)
    side_slots = lax.dynamic_update_index_in_dim(side_slots, packed_side, my_index, 0)
    piece_count = part_pieces.size
    summed_all = jnp.concatenate([part_pieces.reshape(-1), side_slots.reshape(-1)])
    if owners == 4:
        summed_all = summed_all + exchange(summed_all, 1)
        summed_all = summed_all + exchange(summed_all, 2)
    else:
        summed_all = lax.psum(summed_all, "row")
    kernel_slab, summed_all = lax.optimization_barrier((local_slab, summed_all))
    summed = summed_all[:piece_count].reshape(part_pieces.shape)
    every_side = summed_all[piece_count:].reshape(side_slots.shape)
    eye = jnp.eye(BLK, dtype=jnp.float32)
    segment = jnp.stack([
        summed[0] + eye * diagonal[:BLK][None, :],
        summed[1],
        summed[2] + eye * diagonal[L - BLK :][None, :],
    ])

    if owners == 4:
        across_slab = exchange(kernel_slab, 2)
        across_side = lax.dynamic_index_in_dim(every_side, my_index ^ 2, 0, False)
        across_weights = across_side[:slab_height]
        across_live = across_side[slab_height:].reshape(live_blocks.shape).astype(jnp.int32)
        order = jnp.concatenate(
            [lax.dynamic_slice_in_dim(tile_order, (my_index ^ q) * own_blocks, own_blocks) for q in range(2)]
        )
        flags = (jnp.arange(2 * own_blocks) < own_blocks).astype(jnp.int32)
        left_src = jnp.take(source, order)

        def own_part(slab_in):
            return split_rows(
                slab_in, row_weights, live_blocks, left_src, source, order, diagonal, flags, own_blocks,
            )

        def across_part(slab_in, partial):
            mine, partners = split_rows(
                slab_in, across_weights, across_live, left_src, source, order, diagonal, flags,
                own_blocks, partial,
            )
            return mine + exchange(partners, 1)

        hooks = {1: ("own", kernel_slab), 2: ("across", across_slab)}
    else:
        hooks = {}
        flags = jnp.full((block_count,), (my_index == 0).astype(jnp.int32))
        partial = gram_rows(
            kernel_slab, row_weights, live_blocks, jnp.take(source, tile_order), source,
            tile_order, diagonal, flags, own_blocks,
        )
        owned = lax.psum_scatter(
            partial.reshape(L, L), "row", scatter_dimension=0, tiled=True
        )

    times = lax.axis_size("tm")
    position = lax.axis_index("tm")
    running = (segment[0], segment[1], segment[2])
    shift = 1
    round_index = 0
    state = {}

    def run_hook(kind, slab_in, running):
        slab_in, running = lax.optimization_barrier((slab_in, running))
        if kind == "own":
            state["partial"] = own_part(slab_in)
        else:
            state["owned"] = across_part(slab_in, state["partial"])
        return running

    while shift < times:
        if round_index in hooks:
            running = run_hook(*hooks.pop(round_index), running)
        round_index += 1
        pairs = [(src, src + shift) for src in range(times - shift)]
        moved = lax.ppermute(jnp.stack(running), "tm", pairs)
        earlier = (moved[0], moved[1], moved[2])
        joined = join_segments(earlier, running)
        take = position >= shift
        running = tuple(jnp.where(take, new, old) for new, old in zip(joined, running))
        shift *= 2
    for key in sorted(hooks):
        running = run_hook(*hooks[key], running)
    if "owned" in state:
        owned = state["owned"]
    chain_out = jnp.stack(running)[None]
    return (owned[None], chain_out)


def solution(mesh):
    placed = (
        P("tm", "row", None),
        P("tm", "row"),
        P("tm", "row", None),
        P("tm", None),
        P(),
        P("tm", None),
    )
    return jax.shard_map(
        local,
        mesh=mesh,
        in_specs=placed,
        out_specs=(P("tm", "row", None), P("tm", None, None, None)),
        check_vma=False,
    )
```

```python
import functools

import jax
import jax.numpy as jnp
from jax import lax
from jax.sharding import PartitionSpec as P
from jax.experimental import pallas as pl
from jax.experimental.pallas import tpu as pltpu

L = 2048
BLK = 128


def gram_kernel(src_left, src_right, tile_ref, mask_ref, flag_ref, g_ref, w_ref, diag_ref, *rest):
    if len(rest) == 4:
        acc_ref, out_ref, s_ref, lt_ref = rest
    else:
        acc_ref = None
        out_ref, s_ref, lt_ref = rest
    k = pl.program_id(0)
    row_blocks = g_ref.shape[0] // BLK
    col_blocks = g_ref.shape[1] // BLK

    @pl.when(k == 0)
    def _():
        def fill(j, carry):
            src = src_right[j]
            c0 = pl.multiple_of(src * BLK, BLK)
            d0 = pl.multiple_of(j * BLK, BLK)
            for rb in range(row_blocks):
                live = mask_ref[rb * col_blocks + src].astype(jnp.float32)
                vals = g_ref[rb * BLK:(rb + 1) * BLK, pl.ds(c0, BLK)].astype(jnp.float32)
                wts = w_ref[rb * BLK:(rb + 1) * BLK, :]
                s_ref[rb * BLK:(rb + 1) * BLK, pl.ds(d0, BLK)] = (wts * (vals * live)).astype(jnp.bfloat16)
            return carry
        lax.fori_loop(0, col_blocks, fill, 0)

    src = src_left[k]
    c0 = pl.multiple_of(src * BLK, BLK)
    for rb in range(row_blocks):
        live = mask_ref[rb * col_blocks + src].astype(jnp.float32)
        vals = g_ref[rb * BLK:(rb + 1) * BLK, pl.ds(c0, BLK)].astype(jnp.float32) * live
        lt_ref[:, rb * BLK:(rb + 1) * BLK] = vals.T.astype(jnp.bfloat16)
    term = jnp.dot(lt_ref[...], s_ref[...], preferred_element_type=jnp.float32)
    if acc_ref is None:
        out_ref[...] = term
        blk = tile_ref[k]
        e0 = pl.multiple_of(blk * BLK, BLK)
        rows = lax.broadcasted_iota(jnp.int32, (BLK, BLK), 0)
        cols = lax.broadcasted_iota(jnp.int32, (BLK, BLK), 1)
        dvals = diag_ref[pl.ds(blk, 1), :] * flag_ref[k].astype(jnp.float32)
        out_ref[:, pl.ds(e0, BLK)] += jnp.where(rows == cols, dvals, 0.0)
    else:
        out_ref[...] = acc_ref[...] + term


def gram_rows(slab, weights, live_blocks, src_left, src_right, out_tiles, diagonal, flags, group, acc=None):
    height = slab.shape[0]
    col_blocks = L // BLK
    out_blocks = src_left.shape[0]
    in_specs = [
        pl.BlockSpec((height, L), lambda k, *_: (0, 0)),
        pl.BlockSpec((height, 1), lambda k, *_: (0, 0)),
        pl.BlockSpec((col_blocks, BLK), lambda k, *_: (0, 0)),
    ]
    operands = [slab, weights.reshape(height, 1), diagonal.reshape(col_blocks, BLK)]
    aliases = {}
    out_spec = pl.BlockSpec((None, BLK, L), lambda k, *_: (k // group, k % group, 0))
    if acc is not None:
        in_specs.append(out_spec)
        operands.append(acc)
        aliases = {8: 0}
    grid_spec = pltpu.PrefetchScalarGridSpec(
        num_scalar_prefetch=5,
        grid=(out_blocks,),
        in_specs=in_specs,
        out_specs=out_spec,
        scratch_shapes=[pltpu.VMEM((height, L), jnp.bfloat16), pltpu.VMEM((BLK, height), jnp.bfloat16)],
    )
    return pl.pallas_call(
        gram_kernel,
        grid_spec=grid_spec,
        out_shape=jax.ShapeDtypeStruct((out_blocks // group, group * BLK, L), jnp.float32),
        input_output_aliases=aliases,
        compiler_params=pltpu.CompilerParams(vmem_limit_bytes=56 * 1024 * 1024),
    )(src_left, src_right, out_tiles, live_blocks.reshape(-1), flags, *operands)


def split_kernel(src_left, src_right, tile_ref, mask_ref, flag_ref, g_ref, w_ref, diag_ref, *rest,
                 group, accumulate):
    if accumulate:
        acc_first, acc_second, out_first, out_second, s_ref, lt_ref = rest
    else:
        acc_first = acc_second = None
        out_first, out_second, s_ref, lt_ref = rest
    k = pl.program_id(0)
    row_blocks = g_ref.shape[0] // BLK
    col_blocks = g_ref.shape[1] // BLK

    @pl.when(k == 0)
    def _():
        def fill(j, carry):
            src = src_right[j]
            c0 = pl.multiple_of(src * BLK, BLK)
            d0 = pl.multiple_of(j * BLK, BLK)
            for rb in range(row_blocks):
                live = mask_ref[rb * col_blocks + src].astype(jnp.float32)
                vals = g_ref[rb * BLK:(rb + 1) * BLK, pl.ds(c0, BLK)].astype(jnp.float32)
                wts = w_ref[rb * BLK:(rb + 1) * BLK, :]
                s_ref[rb * BLK:(rb + 1) * BLK, pl.ds(d0, BLK)] = (wts * (vals * live)).astype(jnp.bfloat16)
            return carry
        lax.fori_loop(0, col_blocks, fill, 0)

    src = src_left[k]
    c0 = pl.multiple_of(src * BLK, BLK)
    for rb in range(row_blocks):
        live = mask_ref[rb * col_blocks + src].astype(jnp.float32)
        vals = g_ref[rb * BLK:(rb + 1) * BLK, pl.ds(c0, BLK)].astype(jnp.float32) * live
        lt_ref[:, rb * BLK:(rb + 1) * BLK] = vals.T.astype(jnp.bfloat16)
    term = jnp.dot(lt_ref[...], s_ref[...], preferred_element_type=jnp.float32)

    def store(out_ref, acc_ref):
        if acc_ref is None:
            out_ref[...] = term
            blk = tile_ref[k]
            e0 = pl.multiple_of(blk * BLK, BLK)
            rows = lax.broadcasted_iota(jnp.int32, (BLK, BLK), 0)
            cols = lax.broadcasted_iota(jnp.int32, (BLK, BLK), 1)
            dvals = diag_ref[pl.ds(blk, 1), :] * flag_ref[k].astype(jnp.float32)
            out_ref[:, pl.ds(e0, BLK)] += jnp.where(rows == cols, dvals, 0.0)
        else:
            out_ref[...] = acc_ref[...] + term

    @pl.when(k < group)
    def _():
        store(out_first, acc_first)

    @pl.when(k >= group)
    def _():
        store(out_second, acc_second)


def split_rows(slab, weights, live_blocks, src_left, src_right, out_tiles, diagonal, flags, group,
               acc=None):
    height = slab.shape[0]
    col_blocks = L // BLK
    in_specs = [
        pl.BlockSpec((height, L), lambda k, *_: (0, 0)),
        pl.BlockSpec((height, 1), lambda k, *_: (0, 0)),
        pl.BlockSpec((col_blocks, BLK), lambda k, *_: (0, 0)),
    ]
    operands = [slab, weights.reshape(height, 1), diagonal.reshape(col_blocks, BLK)]
    first_spec = pl.BlockSpec((BLK, L), lambda k, *_: (jnp.minimum(k, group - 1), 0))
    second_spec = pl.BlockSpec((BLK, L), lambda k, *_: (jnp.maximum(k - group, 0), 0))
    aliases = {}
    if acc is not None:
        in_specs += [first_spec, second_spec]
        operands += list(acc)
        aliases = {8: 0, 9: 1}
    grid_spec = pltpu.PrefetchScalarGridSpec(
        num_scalar_prefetch=5,
        grid=(2 * group,),
        in_specs=in_specs,
        out_specs=[first_spec, second_spec],
        scratch_shapes=[pltpu.VMEM((height, L), jnp.bfloat16), pltpu.VMEM((BLK, height), jnp.bfloat16)],
    )
    shape = jax.ShapeDtypeStruct((group * BLK, L), jnp.float32)
    return pl.pallas_call(
        functools.partial(split_kernel, group=group, accumulate=acc is not None),
        grid_spec=grid_spec,
        out_shape=(shape, shape),
        input_output_aliases=aliases,
        compiler_params=pltpu.CompilerParams(vmem_limit_bytes=56 * 1024 * 1024),
    )(src_left, src_right, out_tiles, live_blocks.reshape(-1), flags, *operands)


HIGHEST = lax.Precision.HIGHEST


def join_segments(earlier_seg, later_seg):
    top_one, cross_one, bottom_one = earlier_seg
    top_two, cross_two, bottom_two = later_seg
    middle = bottom_one + top_two
    middle = 0.5 * (middle + middle.T)
    factor = jnp.linalg.cholesky(middle)
    half_width = top_one.shape[0]
    solved = lax.linalg.triangular_solve(
        factor, jnp.concatenate([cross_one.T, cross_two], axis=1), left_side=True, lower=True
    )
    solve_one = solved[:, :half_width]
    solve_two = solved[:, half_width:]
    top_new = top_one - jnp.dot(solve_one.T, solve_one, precision=HIGHEST)
    cross_new = -jnp.dot(solve_one.T, solve_two, precision=HIGHEST)
    bottom_new = bottom_two - jnp.dot(solve_two.T, solve_two, precision=HIGHEST)
    return (top_new, cross_new, bottom_new)


def contract_rows(left_cols, right_cols):
    return lax.dot_general(
        left_cols, right_cols, (((0,), (0,)), ((), ())), preferred_element_type=jnp.float32
    )


def local(coupling, row_scale, block_mask, link_map, tile_order, link_diag):
    local_slab = coupling[0]
    row_weights = row_scale[0]
    live_blocks = block_mask[0]
    block_map = link_map[0]
    diagonal = link_diag[0]
    slab_height = local_slab.shape[0]
    block_count = L // BLK
    my_index = lax.axis_index("row")
    block_ids = jnp.arange(block_count, dtype=jnp.int32)
    source = jnp.sum(
        block_ids[None, :] * (block_map[None, :] == block_ids[:, None]).astype(jnp.int32), axis=1
    )

    def edge_cols(global_block):
        local_block = source[global_block]
        cols = lax.dynamic_slice_in_dim(local_slab, local_block * BLK, BLK, axis=1)
        live = lax.dynamic_index_in_dim(live_blocks, local_block, 1, False)
        cols = (cols.reshape(slab_height // BLK, BLK, BLK) * live.astype(jnp.bfloat16)[:, None, None])
        cols = cols.reshape(slab_height, BLK)
        weighted = (row_weights[:, None] * cols.astype(jnp.float32)).astype(jnp.bfloat16)
        return cols, weighted

    first_cols, first_scaled = edge_cols(0)
    final_cols, final_scaled = edge_cols(block_count - 1)
    part_pieces = jnp.stack(
        [
            contract_rows(first_cols, first_scaled),
            contract_rows(first_cols, final_scaled),
            contract_rows(final_cols, final_scaled),
        ]
    )
    owners = lax.axis_size("row")
    own_blocks = block_count // owners

    def exchange(value, step):
        return lax.ppermute(value, "row", [(src, src ^ step) for src in range(owners)])

    packed_side = jnp.concatenate([row_weights, live_blocks.reshape(-1).astype(jnp.float32)])
    side_slots = jnp.zeros((owners, packed_side.shape[0]), jnp.float32)
    side_slots = lax.dynamic_update_index_in_dim(side_slots, packed_side, my_index, 0)
    piece_count = part_pieces.size
    summed_all = jnp.concatenate([part_pieces.reshape(-1), side_slots.reshape(-1)])
    if owners == 4:
        summed_all = summed_all + exchange(summed_all, 1)
        summed_all = summed_all + exchange(summed_all, 2)
    else:
        summed_all = lax.psum(summed_all, "row")
    kernel_slab, summed_all = lax.optimization_barrier((local_slab, summed_all))
    summed = summed_all[:piece_count].reshape(part_pieces.shape)
    every_side = summed_all[piece_count:].reshape(side_slots.shape)
    eye = jnp.eye(BLK, dtype=jnp.float32)
    segment = jnp.stack([
        summed[0] + eye * diagonal[:BLK][None, :],
        summed[1],
        summed[2] + eye * diagonal[L - BLK :][None, :],
    ])

    if owners == 4:
        across_slab = exchange(kernel_slab, 2)
        across_side = lax.dynamic_index_in_dim(every_side, my_index ^ 2, 0, False)
        across_weights = across_side[:slab_height]
        across_live = across_side[slab_height:].reshape(live_blocks.shape).astype(jnp.int32)
        order = jnp.concatenate(
            [lax.dynamic_slice_in_dim(tile_order, (my_index ^ q) * own_blocks, own_blocks) for q in range(2)]
        )
        flags = (jnp.arange(2 * own_blocks) < own_blocks).astype(jnp.int32)
        left_src = jnp.take(source, order)

        def own_part(slab_in):
            return split_rows(
                slab_in, row_weights, live_blocks, left_src, source, order, diagonal, flags, own_blocks,
            )

        def across_part(slab_in, partial):
            mine, partners = split_rows(
                slab_in, across_weights, across_live, left_src, source, order, diagonal, flags,
                own_blocks, partial,
            )
            return mine + exchange(partners, 1)

        hooks = {1: ("own", kernel_slab), 3: ("across", across_slab)}
    else:
        hooks = {}
        flags = jnp.full((block_count,), (my_index == 0).astype(jnp.int32))
        partial = gram_rows(
            kernel_slab, row_weights, live_blocks, jnp.take(source, tile_order), source,
            tile_order, diagonal, flags, own_blocks,
        )
        owned = lax.psum_scatter(
            partial.reshape(L, L), "row", scatter_dimension=0, tiled=True
        )

    times = lax.axis_size("tm")
    position = lax.axis_index("tm")
    running = (segment[0], segment[1], segment[2])
    shift = 1
    round_index = 0
    state = {}

    def run_hook(kind, slab_in, running):
        slab_in, running = lax.optimization_barrier((slab_in, running))
        if kind == "own":
            state["partial"] = own_part(slab_in)
        else:
            state["owned"] = across_part(slab_in, state["partial"])
        return running

    while shift < times:
        if round_index in hooks:
            running = run_hook(*hooks.pop(round_index), running)
        round_index += 1
        pairs = [(src, src + shift) for src in range(times - shift)]
        moved = lax.ppermute(jnp.stack(running), "tm", pairs)
        earlier = (moved[0], moved[1], moved[2])
        joined = join_segments(earlier, running)
        take = position >= shift
        running = tuple(jnp.where(take, new, old) for new, old in zip(joined, running))
        shift *= 2
    for key in sorted(hooks):
        running = run_hook(*hooks[key], running)
    if "owned" in state:
        owned = state["owned"]
    chain_out = jnp.stack(running)[None]
    return (owned[None], chain_out)


def solution(mesh):
    placed = (
        P("tm", "row", None),
        P("tm", "row"),
        P("tm", "row", None),
        P("tm", None),
        P(),
        P("tm", None),
    )
    return jax.shard_map(
        local,
        mesh=mesh,
        in_specs=placed,
        out_specs=(P("tm", "row", None), P("tm", None, None, None)),
        check_vma=False,
    )
```

```python
import functools

import jax
import jax.numpy as jnp
from jax import lax
from jax.sharding import PartitionSpec as P
from jax.experimental import pallas as pl
from jax.experimental.pallas import tpu as pltpu

L = 2048
BLK = 128


def gram_kernel(src_left, src_right, tile_ref, mask_ref, flag_ref, g_ref, w_ref, diag_ref, *rest):
    if len(rest) == 4:
        acc_ref, out_ref, s_ref, lt_ref = rest
    else:
        acc_ref = None
        out_ref, s_ref, lt_ref = rest
    k = pl.program_id(0)
    row_blocks = g_ref.shape[0] // BLK
    col_blocks = g_ref.shape[1] // BLK

    @pl.when(k == 0)
    def _():
        def fill(j, carry):
            src = src_right[j]
            c0 = pl.multiple_of(src * BLK, BLK)
            d0 = pl.multiple_of(j * BLK, BLK)
            for rb in range(row_blocks):
                live = mask_ref[rb * col_blocks + src].astype(jnp.float32)
                vals = g_ref[rb * BLK:(rb + 1) * BLK, pl.ds(c0, BLK)].astype(jnp.float32)
                wts = w_ref[rb * BLK:(rb + 1) * BLK, :]
                s_ref[rb * BLK:(rb + 1) * BLK, pl.ds(d0, BLK)] = (wts * (vals * live)).astype(jnp.bfloat16)
            return carry
        lax.fori_loop(0, col_blocks, fill, 0)

    src = src_left[k]
    c0 = pl.multiple_of(src * BLK, BLK)
    for rb in range(row_blocks):
        live = mask_ref[rb * col_blocks + src].astype(jnp.float32)
        vals = g_ref[rb * BLK:(rb + 1) * BLK, pl.ds(c0, BLK)].astype(jnp.float32) * live
        lt_ref[:, rb * BLK:(rb + 1) * BLK] = vals.T.astype(jnp.bfloat16)
    term = jnp.dot(lt_ref[...], s_ref[...], preferred_element_type=jnp.float32)
    if acc_ref is None:
        out_ref[...] = term
        blk = tile_ref[k]
        e0 = pl.multiple_of(blk * BLK, BLK)
        rows = lax.broadcasted_iota(jnp.int32, (BLK, BLK), 0)
        cols = lax.broadcasted_iota(jnp.int32, (BLK, BLK), 1)
        dvals = diag_ref[pl.ds(blk, 1), :] * flag_ref[k].astype(jnp.float32)
        out_ref[:, pl.ds(e0, BLK)] += jnp.where(rows == cols, dvals, 0.0)
    else:
        out_ref[...] = acc_ref[...] + term


def gram_rows(slab, weights, live_blocks, src_left, src_right, out_tiles, diagonal, flags, group, acc=None):
    height = slab.shape[0]
    col_blocks = L // BLK
    out_blocks = src_left.shape[0]
    in_specs = [
        pl.BlockSpec((height, L), lambda k, *_: (0, 0)),
        pl.BlockSpec((height, 1), lambda k, *_: (0, 0)),
        pl.BlockSpec((col_blocks, BLK), lambda k, *_: (0, 0)),
    ]
    operands = [slab, weights.reshape(height, 1), diagonal.reshape(col_blocks, BLK)]
    aliases = {}
    out_spec = pl.BlockSpec((None, BLK, L), lambda k, *_: (k // group, k % group, 0))
    if acc is not None:
        in_specs.append(out_spec)
        operands.append(acc)
        aliases = {8: 0}
    grid_spec = pltpu.PrefetchScalarGridSpec(
        num_scalar_prefetch=5,
        grid=(out_blocks,),
        in_specs=in_specs,
        out_specs=out_spec,
        scratch_shapes=[pltpu.VMEM((height, L), jnp.bfloat16), pltpu.VMEM((BLK, height), jnp.bfloat16)],
    )
    return pl.pallas_call(
        gram_kernel,
        grid_spec=grid_spec,
        out_shape=jax.ShapeDtypeStruct((out_blocks // group, group * BLK, L), jnp.float32),
        input_output_aliases=aliases,
        compiler_params=pltpu.CompilerParams(vmem_limit_bytes=56 * 1024 * 1024),
    )(src_left, src_right, out_tiles, live_blocks.reshape(-1), flags, *operands)


def split_kernel(src_left, src_right, tile_ref, mask_ref, flag_ref, g_ref, w_ref, diag_ref, *rest,
                 group, accumulate):
    if accumulate:
        acc_first, acc_second, out_first, out_second, s_ref, lt_ref = rest
    else:
        acc_first = acc_second = None
        out_first, out_second, s_ref, lt_ref = rest
    k = pl.program_id(0)
    row_blocks = g_ref.shape[0] // BLK
    col_blocks = g_ref.shape[1] // BLK

    @pl.when(k == 0)
    def _():
        def fill(j, carry):
            src = src_right[j]
            c0 = pl.multiple_of(src * BLK, BLK)
            d0 = pl.multiple_of(j * BLK, BLK)
            for rb in range(row_blocks):
                live = mask_ref[rb * col_blocks + src].astype(jnp.float32)
                vals = g_ref[rb * BLK:(rb + 1) * BLK, pl.ds(c0, BLK)].astype(jnp.float32)
                wts = w_ref[rb * BLK:(rb + 1) * BLK, :]
                s_ref[rb * BLK:(rb + 1) * BLK, pl.ds(d0, BLK)] = (wts * (vals * live)).astype(jnp.bfloat16)
            return carry
        lax.fori_loop(0, col_blocks, fill, 0)

    src = src_left[k]
    c0 = pl.multiple_of(src * BLK, BLK)
    for rb in range(row_blocks):
        live = mask_ref[rb * col_blocks + src].astype(jnp.float32)
        vals = g_ref[rb * BLK:(rb + 1) * BLK, pl.ds(c0, BLK)].astype(jnp.float32) * live
        lt_ref[:, rb * BLK:(rb + 1) * BLK] = vals.T.astype(jnp.bfloat16)
    term = jnp.dot(lt_ref[...], s_ref[...], preferred_element_type=jnp.float32)

    def store(out_ref, acc_ref):
        if acc_ref is None:
            out_ref[...] = term
            blk = tile_ref[k]
            e0 = pl.multiple_of(blk * BLK, BLK)
            rows = lax.broadcasted_iota(jnp.int32, (BLK, BLK), 0)
            cols = lax.broadcasted_iota(jnp.int32, (BLK, BLK), 1)
            dvals = diag_ref[pl.ds(blk, 1), :] * flag_ref[k].astype(jnp.float32)
            out_ref[:, pl.ds(e0, BLK)] += jnp.where(rows == cols, dvals, 0.0)
        else:
            out_ref[...] = acc_ref[...] + term

    @pl.when(k < group)
    def _():
        store(out_first, acc_first)

    @pl.when(k >= group)
    def _():
        store(out_second, acc_second)


def split_rows(slab, weights, live_blocks, src_left, src_right, out_tiles, diagonal, flags, group,
               acc=None):
    height = slab.shape[0]
    col_blocks = L // BLK
    in_specs = [
        pl.BlockSpec((height, L), lambda k, *_: (0, 0)),
        pl.BlockSpec((height, 1), lambda k, *_: (0, 0)),
        pl.BlockSpec((col_blocks, BLK), lambda k, *_: (0, 0)),
    ]
    operands = [slab, weights.reshape(height, 1), diagonal.reshape(col_blocks, BLK)]
    first_spec = pl.BlockSpec((BLK, L), lambda k, *_: (jnp.minimum(k, group - 1), 0))
    second_spec = pl.BlockSpec((BLK, L), lambda k, *_: (jnp.maximum(k - group, 0), 0))
    aliases = {}
    if acc is not None:
        in_specs += [first_spec, second_spec]
        operands += list(acc)
        aliases = {8: 0, 9: 1}
    grid_spec = pltpu.PrefetchScalarGridSpec(
        num_scalar_prefetch=5,
        grid=(2 * group,),
        in_specs=in_specs,
        out_specs=[first_spec, second_spec],
        scratch_shapes=[pltpu.VMEM((height, L), jnp.bfloat16), pltpu.VMEM((BLK, height), jnp.bfloat16)],
    )
    shape = jax.ShapeDtypeStruct((group * BLK, L), jnp.float32)
    return pl.pallas_call(
        functools.partial(split_kernel, group=group, accumulate=acc is not None),
        grid_spec=grid_spec,
        out_shape=(shape, shape),
        input_output_aliases=aliases,
        compiler_params=pltpu.CompilerParams(vmem_limit_bytes=56 * 1024 * 1024),
    )(src_left, src_right, out_tiles, live_blocks.reshape(-1), flags, *operands)


HIGHEST = lax.Precision.HIGHEST


def join_segments(earlier_seg, later_seg):
    top_one, cross_one, bottom_one = earlier_seg
    top_two, cross_two, bottom_two = later_seg
    middle = bottom_one + top_two
    middle = 0.5 * (middle + middle.T)
    factor = jnp.linalg.cholesky(middle)
    half_width = top_one.shape[0]
    solved = lax.linalg.triangular_solve(
        factor, jnp.concatenate([cross_one.T, cross_two], axis=1), left_side=True, lower=True
    )
    solve_one = solved[:, :half_width]
    solve_two = solved[:, half_width:]
    top_new = top_one - jnp.dot(solve_one.T, solve_one, precision=HIGHEST)
    cross_new = -jnp.dot(solve_one.T, solve_two, precision=HIGHEST)
    bottom_new = bottom_two - jnp.dot(solve_two.T, solve_two, precision=HIGHEST)
    return (top_new, cross_new, bottom_new)


def contract_rows(left_cols, right_cols):
    return lax.dot_general(
        left_cols, right_cols, (((0,), (0,)), ((), ())), preferred_element_type=jnp.float32
    )


def local(coupling, row_scale, block_mask, link_map, tile_order, link_diag):
    local_slab = coupling[0]
    row_weights = row_scale[0]
    live_blocks = block_mask[0]
    block_map = link_map[0]
    diagonal = link_diag[0]
    slab_height = local_slab.shape[0]
    block_count = L // BLK
    my_index = lax.axis_index("row")
    block_ids = jnp.arange(block_count, dtype=jnp.int32)
    source = jnp.sum(
        block_ids[None, :] * (block_map[None, :] == block_ids[:, None]).astype(jnp.int32), axis=1
    )

    def edge_cols(global_block):
        local_block = source[global_block]
        cols = lax.dynamic_slice_in_dim(local_slab, local_block * BLK, BLK, axis=1)
        live = lax.dynamic_index_in_dim(live_blocks, local_block, 1, False)
        cols = (cols.reshape(slab_height // BLK, BLK, BLK) * live.astype(jnp.bfloat16)[:, None, None])
        cols = cols.reshape(slab_height, BLK)
        weighted = (row_weights[:, None] * cols.astype(jnp.float32)).astype(jnp.bfloat16)
        return cols, weighted

    first_cols, first_scaled = edge_cols(0)
    final_cols, final_scaled = edge_cols(block_count - 1)
    part_pieces = jnp.stack(
        [
            contract_rows(first_cols, first_scaled),
            contract_rows(first_cols, final_scaled),
            contract_rows(final_cols, final_scaled),
        ]
    )
    owners = lax.axis_size("row")
    own_blocks = block_count // owners

    def exchange(value, step):
        return lax.ppermute(value, "row", [(src, src ^ step) for src in range(owners)])

    packed_side = jnp.concatenate([row_weights, live_blocks.reshape(-1).astype(jnp.float32)])
    side_slots = jnp.zeros((owners, packed_side.shape[0]), jnp.float32)
    side_slots = lax.dynamic_update_index_in_dim(side_slots, packed_side, my_index, 0)
    piece_count = part_pieces.size
    summed_all = jnp.concatenate([part_pieces.reshape(-1), side_slots.reshape(-1)])
    if owners == 4:
        summed_all = summed_all + exchange(summed_all, 1)
        summed_all = summed_all + exchange(summed_all, 2)
    else:
        summed_all = lax.psum(summed_all, "row")
    kernel_slab, summed_all = lax.optimization_barrier((local_slab, summed_all))
    summed = summed_all[:piece_count].reshape(part_pieces.shape)
    every_side = summed_all[piece_count:].reshape(side_slots.shape)
    eye = jnp.eye(BLK, dtype=jnp.float32)
    segment = jnp.stack([
        summed[0] + eye * diagonal[:BLK][None, :],
        summed[1],
        summed[2] + eye * diagonal[L - BLK :][None, :],
    ])

    if owners == 4:
        halves = 2
        half_rows = slab_height // halves
        across_halves = [
            exchange(lax.slice_in_dim(kernel_slab, h * half_rows, (h + 1) * half_rows), 2)
            for h in range(halves)
        ]
        across_side = lax.dynamic_index_in_dim(every_side, my_index ^ 2, 0, False)
        across_weights = across_side[:slab_height]
        across_live = across_side[slab_height:].reshape(live_blocks.shape).astype(jnp.int32)
        order = jnp.concatenate(
            [lax.dynamic_slice_in_dim(tile_order, (my_index ^ q) * own_blocks, own_blocks) for q in range(2)]
        )
        flags = (jnp.arange(2 * own_blocks) < own_blocks).astype(jnp.int32)
        left_src = jnp.take(source, order)

        def own_part(slab_in):
            return split_rows(
                slab_in, row_weights, live_blocks, left_src, source, order, diagonal, flags, own_blocks,
            )

        def across_part(slab_in, partial, half):
            rows = lax.slice_in_dim(across_weights, half * half_rows, (half + 1) * half_rows)
            live = lax.slice_in_dim(
                across_live, half * (half_rows // BLK), (half + 1) * (half_rows // BLK)
            )
            return split_rows(
                slab_in, rows, live, left_src, source, order, diagonal, flags, own_blocks, partial,
            )

        hooks = {1: ("own", kernel_slab), 2: ("across", across_halves[0]), 3: ("last", across_halves[1])}
    else:
        hooks = {}
        flags = jnp.full((block_count,), (my_index == 0).astype(jnp.int32))
        partial = gram_rows(
            kernel_slab, row_weights, live_blocks, jnp.take(source, tile_order), source,
            tile_order, diagonal, flags, own_blocks,
        )
        owned = lax.psum_scatter(
            partial.reshape(L, L), "row", scatter_dimension=0, tiled=True
        )

    times = lax.axis_size("tm")
    position = lax.axis_index("tm")
    running = (segment[0], segment[1], segment[2])
    shift = 1
    round_index = 0
    state = {}

    def run_hook(kind, slab_in, running):
        slab_in, running = lax.optimization_barrier((slab_in, running))
        if kind == "own":
            state["partial"] = own_part(slab_in)
        elif kind == "across":
            state["partial"] = across_part(slab_in, state["partial"], 0)
        else:
            mine, partners = across_part(slab_in, state["partial"], 1)
            state["owned"] = mine + exchange(partners, 1)
        return running

    while shift < times:
        if round_index in hooks:
            running = run_hook(*hooks.pop(round_index), running)
        round_index += 1
        pairs = [(src, src + shift) for src in range(times - shift)]
        moved = lax.ppermute(jnp.stack(running), "tm", pairs)
        earlier = (moved[0], moved[1], moved[2])
        joined = join_segments(earlier, running)
        take = position >= shift
        running = tuple(jnp.where(take, new, old) for new, old in zip(joined, running))
        shift *= 2
    for key in sorted(hooks):
        running = run_hook(*hooks[key], running)
    if "owned" in state:
        owned = state["owned"]
    chain_out = jnp.stack(running)[None]
    return (owned[None], chain_out)


def solution(mesh):
    placed = (
        P("tm", "row", None),
        P("tm", "row"),
        P("tm", "row", None),
        P("tm", None),
        P(),
        P("tm", None),
    )
    return jax.shard_map(
        local,
        mesh=mesh,
        in_specs=placed,
        out_specs=(P("tm", "row", None), P("tm", None, None, None)),
        check_vma=False,
    )
```

```python
import functools

import jax
import jax.numpy as jnp
from jax import lax
from jax.sharding import PartitionSpec as P
from jax.experimental import pallas as pl
from jax.experimental.pallas import tpu as pltpu

L = 2048
BLK = 128


def gram_kernel(src_left, src_right, tile_ref, mask_ref, flag_ref, g_ref, w_ref, diag_ref, *rest):
    extra_ref = None
    if len(rest) == 5:
        acc_ref, extra_ref, out_ref, s_ref, lt_ref = rest
    elif len(rest) == 4:
        acc_ref, out_ref, s_ref, lt_ref = rest
    else:
        acc_ref = None
        out_ref, s_ref, lt_ref = rest
    k = pl.program_id(0)
    row_blocks = g_ref.shape[0] // BLK
    col_blocks = g_ref.shape[1] // BLK

    @pl.when(k == 0)
    def _():
        def fill(j, carry):
            src = src_right[j]
            c0 = pl.multiple_of(src * BLK, BLK)
            d0 = pl.multiple_of(j * BLK, BLK)
            for rb in range(row_blocks):
                live = mask_ref[rb * col_blocks + src].astype(jnp.float32)
                vals = g_ref[rb * BLK:(rb + 1) * BLK, pl.ds(c0, BLK)].astype(jnp.float32)
                wts = w_ref[rb * BLK:(rb + 1) * BLK, :]
                s_ref[rb * BLK:(rb + 1) * BLK, pl.ds(d0, BLK)] = (wts * (vals * live)).astype(jnp.bfloat16)
            return carry
        lax.fori_loop(0, col_blocks, fill, 0)

    src = src_left[k]
    c0 = pl.multiple_of(src * BLK, BLK)
    for rb in range(row_blocks):
        live = mask_ref[rb * col_blocks + src].astype(jnp.float32)
        vals = g_ref[rb * BLK:(rb + 1) * BLK, pl.ds(c0, BLK)].astype(jnp.float32) * live
        lt_ref[:, rb * BLK:(rb + 1) * BLK] = vals.T.astype(jnp.bfloat16)
    term = jnp.dot(lt_ref[...], s_ref[...], preferred_element_type=jnp.float32)
    if acc_ref is None:
        out_ref[...] = term
        blk = tile_ref[k]
        e0 = pl.multiple_of(blk * BLK, BLK)
        rows = lax.broadcasted_iota(jnp.int32, (BLK, BLK), 0)
        cols = lax.broadcasted_iota(jnp.int32, (BLK, BLK), 1)
        dvals = diag_ref[pl.ds(blk, 1), :] * flag_ref[k].astype(jnp.float32)
        out_ref[:, pl.ds(e0, BLK)] += jnp.where(rows == cols, dvals, 0.0)
    elif extra_ref is None:
        out_ref[...] = acc_ref[...] + term
    else:
        out_ref[...] = (acc_ref[...] + extra_ref[...]) + term


def gram_rows(slab, weights, live_blocks, src_left, src_right, out_tiles, diagonal, flags, group, acc=None,
              extra=None):
    height = slab.shape[0]
    col_blocks = L // BLK
    out_blocks = src_left.shape[0]
    in_specs = [
        pl.BlockSpec((height, L), lambda k, *_: (0, 0)),
        pl.BlockSpec((height, 1), lambda k, *_: (0, 0)),
        pl.BlockSpec((col_blocks, BLK), lambda k, *_: (0, 0)),
    ]
    operands = [slab, weights.reshape(height, 1), diagonal.reshape(col_blocks, BLK)]
    aliases = {}
    out_spec = pl.BlockSpec((None, BLK, L), lambda k, *_: (k // group, k % group, 0))
    if acc is not None:
        in_specs.append(out_spec)
        operands.append(acc)
        aliases = {8: 0}
    if extra is not None:
        in_specs.append(out_spec)
        operands.append(extra)
    grid_spec = pltpu.PrefetchScalarGridSpec(
        num_scalar_prefetch=5,
        grid=(out_blocks,),
        in_specs=in_specs,
        out_specs=out_spec,
        scratch_shapes=[pltpu.VMEM((height, L), jnp.bfloat16), pltpu.VMEM((BLK, height), jnp.bfloat16)],
    )
    return pl.pallas_call(
        gram_kernel,
        grid_spec=grid_spec,
        out_shape=jax.ShapeDtypeStruct((out_blocks // group, group * BLK, L), jnp.float32),
        input_output_aliases=aliases,
        compiler_params=pltpu.CompilerParams(vmem_limit_bytes=56 * 1024 * 1024),
    )(src_left, src_right, out_tiles, live_blocks.reshape(-1), flags, *operands)


def split_kernel(src_left, src_right, tile_ref, mask_ref, flag_ref, g_ref, w_ref, diag_ref, *rest,
                 group, accumulate):
    if accumulate:
        acc_first, acc_second, out_first, out_second, s_ref, lt_ref = rest
    else:
        acc_first = acc_second = None
        out_first, out_second, s_ref, lt_ref = rest
    k = pl.program_id(0)
    row_blocks = g_ref.shape[0] // BLK
    col_blocks = g_ref.shape[1] // BLK

    @pl.when(k == 0)
    def _():
        def fill(j, carry):
            src = src_right[j]
            c0 = pl.multiple_of(src * BLK, BLK)
            d0 = pl.multiple_of(j * BLK, BLK)
            for rb in range(row_blocks):
                live = mask_ref[rb * col_blocks + src].astype(jnp.float32)
                vals = g_ref[rb * BLK:(rb + 1) * BLK, pl.ds(c0, BLK)].astype(jnp.float32)
                wts = w_ref[rb * BLK:(rb + 1) * BLK, :]
                s_ref[rb * BLK:(rb + 1) * BLK, pl.ds(d0, BLK)] = (wts * (vals * live)).astype(jnp.bfloat16)
            return carry
        lax.fori_loop(0, col_blocks, fill, 0)

    src = src_left[k]
    c0 = pl.multiple_of(src * BLK, BLK)
    for rb in range(row_blocks):
        live = mask_ref[rb * col_blocks + src].astype(jnp.float32)
        vals = g_ref[rb * BLK:(rb + 1) * BLK, pl.ds(c0, BLK)].astype(jnp.float32) * live
        lt_ref[:, rb * BLK:(rb + 1) * BLK] = vals.T.astype(jnp.bfloat16)
    term = jnp.dot(lt_ref[...], s_ref[...], preferred_element_type=jnp.float32)

    def store(out_ref, acc_ref):
        if acc_ref is None:
            out_ref[...] = term
            blk = tile_ref[k]
            e0 = pl.multiple_of(blk * BLK, BLK)
            rows = lax.broadcasted_iota(jnp.int32, (BLK, BLK), 0)
            cols = lax.broadcasted_iota(jnp.int32, (BLK, BLK), 1)
            dvals = diag_ref[pl.ds(blk, 1), :] * flag_ref[k].astype(jnp.float32)
            out_ref[:, pl.ds(e0, BLK)] += jnp.where(rows == cols, dvals, 0.0)
        else:
            out_ref[...] = acc_ref[...] + term

    @pl.when(k < group)
    def _():
        store(out_first, acc_first)

    @pl.when(k >= group)
    def _():
        store(out_second, acc_second)


def split_rows(slab, weights, live_blocks, src_left, src_right, out_tiles, diagonal, flags, group,
               acc=None):
    height = slab.shape[0]
    col_blocks = L // BLK
    in_specs = [
        pl.BlockSpec((height, L), lambda k, *_: (0, 0)),
        pl.BlockSpec((height, 1), lambda k, *_: (0, 0)),
        pl.BlockSpec((col_blocks, BLK), lambda k, *_: (0, 0)),
    ]
    operands = [slab, weights.reshape(height, 1), diagonal.reshape(col_blocks, BLK)]
    first_spec = pl.BlockSpec((BLK, L), lambda k, *_: (jnp.minimum(k, group - 1), 0))
    second_spec = pl.BlockSpec((BLK, L), lambda k, *_: (jnp.maximum(k - group, 0), 0))
    aliases = {}
    if acc is not None:
        in_specs += [first_spec, second_spec]
        operands += list(acc)
        aliases = {8: 0, 9: 1}
    grid_spec = pltpu.PrefetchScalarGridSpec(
        num_scalar_prefetch=5,
        grid=(2 * group,),
        in_specs=in_specs,
        out_specs=[first_spec, second_spec],
        scratch_shapes=[pltpu.VMEM((height, L), jnp.bfloat16), pltpu.VMEM((BLK, height), jnp.bfloat16)],
    )
    shape = jax.ShapeDtypeStruct((group * BLK, L), jnp.float32)
    return pl.pallas_call(
        functools.partial(split_kernel, group=group, accumulate=acc is not None),
        grid_spec=grid_spec,
        out_shape=(shape, shape),
        input_output_aliases=aliases,
        compiler_params=pltpu.CompilerParams(vmem_limit_bytes=56 * 1024 * 1024),
    )(src_left, src_right, out_tiles, live_blocks.reshape(-1), flags, *operands)


HIGHEST = lax.Precision.HIGHEST


def join_segments(earlier_seg, later_seg):
    top_one, cross_one, bottom_one = earlier_seg
    top_two, cross_two, bottom_two = later_seg
    middle = bottom_one + top_two
    middle = 0.5 * (middle + middle.T)
    factor = jnp.linalg.cholesky(middle)
    half_width = top_one.shape[0]
    solved = lax.linalg.triangular_solve(
        factor, jnp.concatenate([cross_one.T, cross_two], axis=1), left_side=True, lower=True
    )
    solve_one = solved[:, :half_width]
    solve_two = solved[:, half_width:]
    top_new = top_one - jnp.dot(solve_one.T, solve_one, precision=HIGHEST)
    cross_new = -jnp.dot(solve_one.T, solve_two, precision=HIGHEST)
    bottom_new = bottom_two - jnp.dot(solve_two.T, solve_two, precision=HIGHEST)
    return (top_new, cross_new, bottom_new)


def contract_rows(left_cols, right_cols):
    return lax.dot_general(
        left_cols, right_cols, (((0,), (0,)), ((), ())), preferred_element_type=jnp.float32
    )


def local(coupling, row_scale, block_mask, link_map, tile_order, link_diag):
    local_slab = coupling[0]
    row_weights = row_scale[0]
    live_blocks = block_mask[0]
    block_map = link_map[0]
    diagonal = link_diag[0]
    slab_height = local_slab.shape[0]
    block_count = L // BLK
    my_index = lax.axis_index("row")
    block_ids = jnp.arange(block_count, dtype=jnp.int32)
    source = jnp.sum(
        block_ids[None, :] * (block_map[None, :] == block_ids[:, None]).astype(jnp.int32), axis=1
    )

    def edge_cols(global_block):
        local_block = source[global_block]
        cols = lax.dynamic_slice_in_dim(local_slab, local_block * BLK, BLK, axis=1)
        live = lax.dynamic_index_in_dim(live_blocks, local_block, 1, False)
        cols = (cols.reshape(slab_height // BLK, BLK, BLK) * live.astype(jnp.bfloat16)[:, None, None])
        cols = cols.reshape(slab_height, BLK)
        weighted = (row_weights[:, None] * cols.astype(jnp.float32)).astype(jnp.bfloat16)
        return cols, weighted

    first_cols, first_scaled = edge_cols(0)
    final_cols, final_scaled = edge_cols(block_count - 1)
    part_pieces = jnp.stack(
        [
            contract_rows(first_cols, first_scaled),
            contract_rows(first_cols, final_scaled),
            contract_rows(final_cols, final_scaled),
        ]
    )
    owners = lax.axis_size("row")
    own_blocks = block_count // owners

    def exchange(value, step):
        return lax.ppermute(value, "row", [(src, src ^ step) for src in range(owners)])

    packed_side = jnp.concatenate([row_weights, live_blocks.reshape(-1).astype(jnp.float32)])
    side_slots = jnp.zeros((owners, packed_side.shape[0]), jnp.float32)
    side_slots = lax.dynamic_update_index_in_dim(side_slots, packed_side, my_index, 0)
    piece_count = part_pieces.size
    summed_all = jnp.concatenate([part_pieces.reshape(-1), side_slots.reshape(-1)])
    if owners == 4:
        summed_all = summed_all + exchange(summed_all, 1)
        summed_all = summed_all + exchange(summed_all, 2)
    else:
        summed_all = lax.psum(summed_all, "row")
    kernel_slab, summed_all = lax.optimization_barrier((local_slab, summed_all))
    summed = summed_all[:piece_count].reshape(part_pieces.shape)
    every_side = summed_all[piece_count:].reshape(side_slots.shape)
    eye = jnp.eye(BLK, dtype=jnp.float32)
    segment = jnp.stack([
        summed[0] + eye * diagonal[:BLK][None, :],
        summed[1],
        summed[2] + eye * diagonal[L - BLK :][None, :],
    ])

    if owners == 4:
        halves = 2
        half_rows = slab_height // halves
        across_halves = [
            exchange(lax.slice_in_dim(kernel_slab, h * half_rows, (h + 1) * half_rows), 2)
            for h in range(halves)
        ]
        across_side = lax.dynamic_index_in_dim(every_side, my_index ^ 2, 0, False)
        across_weights = across_side[:slab_height]
        across_live = across_side[slab_height:].reshape(live_blocks.shape).astype(jnp.int32)
        order = jnp.concatenate(
            [lax.dynamic_slice_in_dim(tile_order, (my_index ^ q) * own_blocks, own_blocks) for q in range(2)]
        )
        flags = (jnp.arange(2 * own_blocks) < own_blocks).astype(jnp.int32)
        left_src = jnp.take(source, order)

        def own_part(slab_in):
            return split_rows(
                slab_in, row_weights, live_blocks, left_src, source, order, diagonal, flags, own_blocks,
            )

        def across_part(slab_in, partial, half):
            rows = lax.slice_in_dim(across_weights, half * half_rows, (half + 1) * half_rows)
            live = lax.slice_in_dim(
                across_live, half * (half_rows // BLK), (half + 1) * (half_rows // BLK)
            )
            return split_rows(
                slab_in, rows, live, left_src, source, order, diagonal, flags, own_blocks, partial,
            )

        partner_side = lax.dynamic_index_in_dim(every_side, my_index ^ 3, 0, False)
        partner_weights = partner_side[:slab_height]
        partner_live = partner_side[slab_height:].reshape(live_blocks.shape).astype(jnp.int32)
        last_weights = jnp.concatenate([
            lax.slice_in_dim(across_weights, half_rows, slab_height),
            lax.slice_in_dim(partner_weights, half_rows, slab_height),
        ])
        last_live = jnp.concatenate([
            lax.slice_in_dim(across_live, half_rows // BLK, slab_height // BLK),
            lax.slice_in_dim(partner_live, half_rows // BLK, slab_height // BLK),
        ])
        mine_order = order[:own_blocks]

        def last_part(slab_in, mine, received):
            total = gram_rows(
                slab_in, last_weights, last_live, jnp.take(source, mine_order), source, mine_order,
                diagonal, flags[:own_blocks], own_blocks, mine[None], received[None],
            )
            return total[0]

        hooks = {1: ("own", kernel_slab), 2: ("across", across_halves[0]), 3: ("last", across_halves[1])}
    else:
        hooks = {}
        flags = jnp.full((block_count,), (my_index == 0).astype(jnp.int32))
        partial = gram_rows(
            kernel_slab, row_weights, live_blocks, jnp.take(source, tile_order), source,
            tile_order, diagonal, flags, own_blocks,
        )
        owned = lax.psum_scatter(
            partial.reshape(L, L), "row", scatter_dimension=0, tiled=True
        )

    times = lax.axis_size("tm")
    position = lax.axis_index("tm")
    running = (segment[0], segment[1], segment[2])
    shift = 1
    round_index = 0
    state = {}

    def run_hook(kind, slab_in, running):
        slab_in, running = lax.optimization_barrier((slab_in, running))
        if kind == "own":
            state["partial"] = own_part(slab_in)
        elif kind == "across":
            mine, partners = across_part(slab_in, state["partial"], 0)
            state["mine"] = mine
            state["received"] = exchange(partners, 1)
        else:
            both = jnp.concatenate([slab_in, exchange(slab_in, 1)], axis=0)
            state["owned"] = last_part(both, state["mine"], state["received"])
        return running

    while shift < times:
        if round_index in hooks:
            running = run_hook(*hooks.pop(round_index), running)
        round_index += 1
        pairs = [(src, src + shift) for src in range(times - shift)]
        moved = lax.ppermute(jnp.stack(running), "tm", pairs)
        earlier = (moved[0], moved[1], moved[2])
        joined = join_segments(earlier, running)
        take = position >= shift
        running = tuple(jnp.where(take, new, old) for new, old in zip(joined, running))
        shift *= 2
    for key in sorted(hooks):
        running = run_hook(*hooks[key], running)
    if "owned" in state:
        owned = state["owned"]
    chain_out = jnp.stack(running)[None]
    return (owned[None], chain_out)


def solution(mesh):
    placed = (
        P("tm", "row", None),
        P("tm", "row"),
        P("tm", "row", None),
        P("tm", None),
        P(),
        P("tm", None),
    )
    return jax.shard_map(
        local,
        mesh=mesh,
        in_specs=placed,
        out_specs=(P("tm", "row", None), P("tm", None, None, None)),
        check_vma=False,
    )
```

```python
import functools

import jax
import jax.numpy as jnp
from jax import lax
from jax.sharding import PartitionSpec as P
from jax.experimental import pallas as pl
from jax.experimental.pallas import tpu as pltpu

L = 2048
BLK = 128


def gram_kernel(src_left, src_right, tile_ref, mask_ref, flag_ref, g_ref, w_ref, diag_ref, *rest):
    extra_ref = None
    if len(rest) == 5:
        acc_ref, extra_ref, out_ref, s_ref, lt_ref = rest
    elif len(rest) == 4:
        acc_ref, out_ref, s_ref, lt_ref = rest
    else:
        acc_ref = None
        out_ref, s_ref, lt_ref = rest
    k = pl.program_id(0)
    row_blocks = g_ref.shape[0] // BLK
    col_blocks = g_ref.shape[1] // BLK

    @pl.when(k == 0)
    def _():
        def fill(j, carry):
            src = src_right[j]
            c0 = pl.multiple_of(src * BLK, BLK)
            d0 = pl.multiple_of(j * BLK, BLK)
            for rb in range(row_blocks):
                live = mask_ref[rb * col_blocks + src].astype(jnp.float32)
                vals = g_ref[rb * BLK:(rb + 1) * BLK, pl.ds(c0, BLK)].astype(jnp.float32)
                wts = w_ref[rb * BLK:(rb + 1) * BLK, :]
                s_ref[rb * BLK:(rb + 1) * BLK, pl.ds(d0, BLK)] = (wts * (vals * live)).astype(jnp.bfloat16)
            return carry
        lax.fori_loop(0, col_blocks, fill, 0)

    src = src_left[k]
    c0 = pl.multiple_of(src * BLK, BLK)
    for rb in range(row_blocks):
        live = mask_ref[rb * col_blocks + src].astype(jnp.float32)
        vals = g_ref[rb * BLK:(rb + 1) * BLK, pl.ds(c0, BLK)].astype(jnp.float32) * live
        lt_ref[:, rb * BLK:(rb + 1) * BLK] = vals.T.astype(jnp.bfloat16)
    term = jnp.dot(lt_ref[...], s_ref[...], preferred_element_type=jnp.float32)
    if acc_ref is None:
        out_ref[...] = term
        blk = tile_ref[k]
        e0 = pl.multiple_of(blk * BLK, BLK)
        rows = lax.broadcasted_iota(jnp.int32, (BLK, BLK), 0)
        cols = lax.broadcasted_iota(jnp.int32, (BLK, BLK), 1)
        dvals = diag_ref[pl.ds(blk, 1), :] * flag_ref[k].astype(jnp.float32)
        out_ref[:, pl.ds(e0, BLK)] += jnp.where(rows == cols, dvals, 0.0)
    elif extra_ref is None:
        out_ref[...] = acc_ref[...] + term
    else:
        out_ref[...] = (acc_ref[...] + extra_ref[...]) + term


def gram_rows(slab, weights, live_blocks, src_left, src_right, out_tiles, diagonal, flags, group, acc=None,
              extra=None):
    height = slab.shape[0]
    col_blocks = L // BLK
    out_blocks = src_left.shape[0]
    in_specs = [
        pl.BlockSpec((height, L), lambda k, *_: (0, 0)),
        pl.BlockSpec((height, 1), lambda k, *_: (0, 0)),
        pl.BlockSpec((col_blocks, BLK), lambda k, *_: (0, 0)),
    ]
    operands = [slab, weights.reshape(height, 1), diagonal.reshape(col_blocks, BLK)]
    aliases = {}
    out_spec = pl.BlockSpec((None, BLK, L), lambda k, *_: (k // group, k % group, 0))
    if acc is not None:
        in_specs.append(out_spec)
        operands.append(acc)
        aliases = {8: 0}
    if extra is not None:
        in_specs.append(out_spec)
        operands.append(extra)
    grid_spec = pltpu.PrefetchScalarGridSpec(
        num_scalar_prefetch=5,
        grid=(out_blocks,),
        in_specs=in_specs,
        out_specs=out_spec,
        scratch_shapes=[pltpu.VMEM((height, L), jnp.bfloat16), pltpu.VMEM((BLK, height), jnp.bfloat16)],
    )
    return pl.pallas_call(
        gram_kernel,
        grid_spec=grid_spec,
        out_shape=jax.ShapeDtypeStruct((out_blocks // group, group * BLK, L), jnp.float32),
        input_output_aliases=aliases,
        compiler_params=pltpu.CompilerParams(vmem_limit_bytes=56 * 1024 * 1024),
    )(src_left, src_right, out_tiles, live_blocks.reshape(-1), flags, *operands)


def split_kernel(src_left, src_right, tile_ref, mask_ref, flag_ref, g_ref, w_ref, diag_ref, *rest,
                 group, accumulate):
    if accumulate:
        acc_first, acc_second, out_first, out_second, s_ref, lt_ref = rest
    else:
        acc_first = acc_second = None
        out_first, out_second, s_ref, lt_ref = rest
    k = pl.program_id(0)
    row_blocks = g_ref.shape[0] // BLK
    col_blocks = g_ref.shape[1] // BLK

    @pl.when(k == 0)
    def _():
        def fill(j, carry):
            src = src_right[j]
            c0 = pl.multiple_of(src * BLK, BLK)
            d0 = pl.multiple_of(j * BLK, BLK)
            for rb in range(row_blocks):
                live = mask_ref[rb * col_blocks + src].astype(jnp.float32)
                vals = g_ref[rb * BLK:(rb + 1) * BLK, pl.ds(c0, BLK)].astype(jnp.float32)
                wts = w_ref[rb * BLK:(rb + 1) * BLK, :]
                s_ref[rb * BLK:(rb + 1) * BLK, pl.ds(d0, BLK)] = (wts * (vals * live)).astype(jnp.bfloat16)
            return carry
        lax.fori_loop(0, col_blocks, fill, 0)

    src = src_left[k]
    c0 = pl.multiple_of(src * BLK, BLK)
    for rb in range(row_blocks):
        live = mask_ref[rb * col_blocks + src].astype(jnp.float32)
        vals = g_ref[rb * BLK:(rb + 1) * BLK, pl.ds(c0, BLK)].astype(jnp.float32) * live
        lt_ref[:, rb * BLK:(rb + 1) * BLK] = vals.T.astype(jnp.bfloat16)
    term = jnp.dot(lt_ref[...], s_ref[...], preferred_element_type=jnp.float32)

    def store(out_ref, acc_ref):
        if acc_ref is None:
            out_ref[...] = term
            blk = tile_ref[k]
            e0 = pl.multiple_of(blk * BLK, BLK)
            rows = lax.broadcasted_iota(jnp.int32, (BLK, BLK), 0)
            cols = lax.broadcasted_iota(jnp.int32, (BLK, BLK), 1)
            dvals = diag_ref[pl.ds(blk, 1), :] * flag_ref[k].astype(jnp.float32)
            out_ref[:, pl.ds(e0, BLK)] += jnp.where(rows == cols, dvals, 0.0)
        else:
            out_ref[...] = acc_ref[...] + term

    @pl.when(k < group)
    def _():
        store(out_first, acc_first)

    @pl.when(k >= group)
    def _():
        store(out_second, acc_second)


def split_rows(slab, weights, live_blocks, src_left, src_right, out_tiles, diagonal, flags, group,
               acc=None):
    height = slab.shape[0]
    col_blocks = L // BLK
    in_specs = [
        pl.BlockSpec((height, L), lambda k, *_: (0, 0)),
        pl.BlockSpec((height, 1), lambda k, *_: (0, 0)),
        pl.BlockSpec((col_blocks, BLK), lambda k, *_: (0, 0)),
    ]
    operands = [slab, weights.reshape(height, 1), diagonal.reshape(col_blocks, BLK)]
    first_spec = pl.BlockSpec((BLK, L), lambda k, *_: (jnp.minimum(k, group - 1), 0))
    second_spec = pl.BlockSpec((BLK, L), lambda k, *_: (jnp.maximum(k - group, 0), 0))
    aliases = {}
    if acc is not None:
        in_specs += [first_spec, second_spec]
        operands += list(acc)
        aliases = {8: 0, 9: 1}
    grid_spec = pltpu.PrefetchScalarGridSpec(
        num_scalar_prefetch=5,
        grid=(2 * group,),
        in_specs=in_specs,
        out_specs=[first_spec, second_spec],
        scratch_shapes=[pltpu.VMEM((height, L), jnp.bfloat16), pltpu.VMEM((BLK, height), jnp.bfloat16)],
    )
    shape = jax.ShapeDtypeStruct((group * BLK, L), jnp.float32)
    return pl.pallas_call(
        functools.partial(split_kernel, group=group, accumulate=acc is not None),
        grid_spec=grid_spec,
        out_shape=(shape, shape),
        input_output_aliases=aliases,
        compiler_params=pltpu.CompilerParams(vmem_limit_bytes=56 * 1024 * 1024),
    )(src_left, src_right, out_tiles, live_blocks.reshape(-1), flags, *operands)


HIGHEST = lax.Precision.HIGHEST


def join_segments(earlier_seg, later_seg):
    top_one, cross_one, bottom_one = earlier_seg
    top_two, cross_two, bottom_two = later_seg
    middle = bottom_one + top_two
    middle = 0.5 * (middle + middle.T)
    factor = jnp.linalg.cholesky(middle)
    half_width = top_one.shape[0]
    solved = lax.linalg.triangular_solve(
        factor, jnp.concatenate([cross_one.T, cross_two], axis=1), left_side=True, lower=True
    )
    solve_one = solved[:, :half_width]
    solve_two = solved[:, half_width:]
    top_new = top_one - jnp.dot(solve_one.T, solve_one, precision=HIGHEST)
    cross_new = -jnp.dot(solve_one.T, solve_two, precision=HIGHEST)
    bottom_new = bottom_two - jnp.dot(solve_two.T, solve_two, precision=HIGHEST)
    return (top_new, cross_new, bottom_new)


def contract_rows(left_cols, right_cols):
    return lax.dot_general(
        left_cols, right_cols, (((0,), (0,)), ((), ())), preferred_element_type=jnp.float32
    )


def local(coupling, row_scale, block_mask, link_map, tile_order, link_diag):
    local_slab = coupling[0]
    row_weights = row_scale[0]
    live_blocks = block_mask[0]
    block_map = link_map[0]
    diagonal = link_diag[0]
    slab_height = local_slab.shape[0]
    block_count = L // BLK
    my_index = lax.axis_index("row")
    block_ids = jnp.arange(block_count, dtype=jnp.int32)
    source = jnp.sum(
        block_ids[None, :] * (block_map[None, :] == block_ids[:, None]).astype(jnp.int32), axis=1
    )

    def edge_cols(global_block):
        local_block = source[global_block]
        cols = lax.dynamic_slice_in_dim(local_slab, local_block * BLK, BLK, axis=1)
        live = lax.dynamic_index_in_dim(live_blocks, local_block, 1, False)
        cols = (cols.reshape(slab_height // BLK, BLK, BLK) * live.astype(jnp.bfloat16)[:, None, None])
        cols = cols.reshape(slab_height, BLK)
        weighted = (row_weights[:, None] * cols.astype(jnp.float32)).astype(jnp.bfloat16)
        return cols, weighted

    first_cols, first_scaled = edge_cols(0)
    final_cols, final_scaled = edge_cols(block_count - 1)
    edge_gram = contract_rows(
        jnp.concatenate([first_cols, final_cols], axis=1),
        jnp.concatenate([first_scaled, final_scaled], axis=1),
    )
    part_pieces = jnp.stack(
        [edge_gram[:BLK, :BLK], edge_gram[:BLK, BLK:], edge_gram[BLK:, BLK:]]
    )
    owners = lax.axis_size("row")
    own_blocks = block_count // owners

    def exchange(value, step):
        return lax.ppermute(value, "row", [(src, src ^ step) for src in range(owners)])

    packed_side = jnp.concatenate([row_weights, live_blocks.reshape(-1).astype(jnp.float32)])
    side_slots = jnp.zeros((owners, packed_side.shape[0]), jnp.float32)
    side_slots = lax.dynamic_update_index_in_dim(side_slots, packed_side, my_index, 0)
    piece_count = part_pieces.size
    summed_all = jnp.concatenate([part_pieces.reshape(-1), side_slots.reshape(-1)])
    if owners == 4:
        summed_all = summed_all + exchange(summed_all, 1)
        summed_all = summed_all + exchange(summed_all, 2)
    else:
        summed_all = lax.psum(summed_all, "row")
    kernel_slab, summed_all = lax.optimization_barrier((local_slab, summed_all))
    summed = summed_all[:piece_count].reshape(part_pieces.shape)
    every_side = summed_all[piece_count:].reshape(side_slots.shape)
    eye = jnp.eye(BLK, dtype=jnp.float32)
    segment = jnp.stack([
        summed[0] + eye * diagonal[:BLK][None, :],
        summed[1],
        summed[2] + eye * diagonal[L - BLK :][None, :],
    ])

    if owners == 4:
        halves = 2
        half_rows = slab_height // halves
        across_halves = [
            exchange(lax.slice_in_dim(kernel_slab, h * half_rows, (h + 1) * half_rows), 2)
            for h in range(halves)
        ]
        across_side = lax.dynamic_index_in_dim(every_side, my_index ^ 2, 0, False)
        across_weights = across_side[:slab_height]
        across_live = across_side[slab_height:].reshape(live_blocks.shape).astype(jnp.int32)
        order = jnp.concatenate(
            [lax.dynamic_slice_in_dim(tile_order, (my_index ^ q) * own_blocks, own_blocks) for q in range(2)]
        )
        flags = (jnp.arange(2 * own_blocks) < own_blocks).astype(jnp.int32)
        left_src = jnp.take(source, order)

        def own_part(slab_in):
            return split_rows(
                slab_in, row_weights, live_blocks, left_src, source, order, diagonal, flags, own_blocks,
            )

        def across_part(slab_in, partial, half):
            rows = lax.slice_in_dim(across_weights, half * half_rows, (half + 1) * half_rows)
            live = lax.slice_in_dim(
                across_live, half * (half_rows // BLK), (half + 1) * (half_rows // BLK)
            )
            return split_rows(
                slab_in, rows, live, left_src, source, order, diagonal, flags, own_blocks, partial,
            )

        partner_side = lax.dynamic_index_in_dim(every_side, my_index ^ 3, 0, False)
        partner_weights = partner_side[:slab_height]
        partner_live = partner_side[slab_height:].reshape(live_blocks.shape).astype(jnp.int32)
        last_weights = jnp.concatenate([
            lax.slice_in_dim(across_weights, half_rows, slab_height),
            lax.slice_in_dim(partner_weights, half_rows, slab_height),
        ])
        last_live = jnp.concatenate([
            lax.slice_in_dim(across_live, half_rows // BLK, slab_height // BLK),
            lax.slice_in_dim(partner_live, half_rows // BLK, slab_height // BLK),
        ])
        mine_order = order[:own_blocks]

        def last_part(slab_in, mine, received):
            total = gram_rows(
                slab_in, last_weights, last_live, jnp.take(source, mine_order), source, mine_order,
                diagonal, flags[:own_blocks], own_blocks, mine[None], received[None],
            )
            return total[0]

        hooks = {1: ("own", kernel_slab), 2: ("across", across_halves[0]), 3: ("last", across_halves[1])}
    else:
        hooks = {}
        flags = jnp.full((block_count,), (my_index == 0).astype(jnp.int32))
        partial = gram_rows(
            kernel_slab, row_weights, live_blocks, jnp.take(source, tile_order), source,
            tile_order, diagonal, flags, own_blocks,
        )
        owned = lax.psum_scatter(
            partial.reshape(L, L), "row", scatter_dimension=0, tiled=True
        )

    times = lax.axis_size("tm")
    position = lax.axis_index("tm")
    running = (segment[0], segment[1], segment[2])
    shift = 1
    round_index = 0
    state = {}

    def run_hook(kind, slab_in, running):
        slab_in, running = lax.optimization_barrier((slab_in, running))
        if kind == "own":
            state["partial"] = own_part(slab_in)
        elif kind == "across":
            mine, partners = across_part(slab_in, state["partial"], 0)
            state["mine"] = mine
            state["received"] = exchange(partners, 1)
        else:
            both = jnp.concatenate([slab_in, exchange(slab_in, 1)], axis=0)
            state["owned"] = last_part(both, state["mine"], state["received"])
        return running

    while shift < times:
        if round_index in hooks:
            running = run_hook(*hooks.pop(round_index), running)
        round_index += 1
        pairs = [(src, src + shift) for src in range(times - shift)]
        moved = lax.ppermute(jnp.stack(running), "tm", pairs)
        earlier = (moved[0], moved[1], moved[2])
        joined = join_segments(earlier, running)
        take = position >= shift
        running = tuple(jnp.where(take, new, old) for new, old in zip(joined, running))
        shift *= 2
    for key in sorted(hooks):
        running = run_hook(*hooks[key], running)
    if "owned" in state:
        owned = state["owned"]
    chain_out = jnp.stack(running)[None]
    return (owned[None], chain_out)


def solution(mesh):
    placed = (
        P("tm", "row", None),
        P("tm", "row"),
        P("tm", "row", None),
        P("tm", None),
        P(),
        P("tm", None),
    )
    return jax.shard_map(
        local,
        mesh=mesh,
        in_specs=placed,
        out_specs=(P("tm", "row", None), P("tm", None, None, None)),
        check_vma=False,
    )
```

```python
import functools

import jax
import jax.numpy as jnp
from jax import lax
from jax.sharding import PartitionSpec as P
from jax.experimental import pallas as pl
from jax.experimental.pallas import tpu as pltpu

L = 2048
BLK = 128


def gram_kernel(src_left, src_right, tile_ref, mask_ref, flag_ref, g_ref, w_ref, diag_ref, *rest):
    extra_ref = None
    if len(rest) == 5:
        acc_ref, extra_ref, out_ref, s_ref, lt_ref = rest
    elif len(rest) == 4:
        acc_ref, out_ref, s_ref, lt_ref = rest
    else:
        acc_ref = None
        out_ref, s_ref, lt_ref = rest
    k = pl.program_id(0)
    row_blocks = g_ref.shape[0] // BLK
    col_blocks = g_ref.shape[1] // BLK

    @pl.when(k == 0)
    def _():
        def fill(j, carry):
            src = src_right[j]
            c0 = pl.multiple_of(src * BLK, BLK)
            d0 = pl.multiple_of(j * BLK, BLK)
            for rb in range(row_blocks):
                live = mask_ref[rb * col_blocks + src].astype(jnp.float32)
                vals = g_ref[rb * BLK:(rb + 1) * BLK, pl.ds(c0, BLK)].astype(jnp.float32)
                wts = w_ref[rb * BLK:(rb + 1) * BLK, :]
                s_ref[rb * BLK:(rb + 1) * BLK, pl.ds(d0, BLK)] = (wts * (vals * live)).astype(jnp.bfloat16)
            return carry
        lax.fori_loop(0, col_blocks, fill, 0)

    src = src_left[k]
    c0 = pl.multiple_of(src * BLK, BLK)
    for rb in range(row_blocks):
        live = mask_ref[rb * col_blocks + src].astype(jnp.float32)
        vals = g_ref[rb * BLK:(rb + 1) * BLK, pl.ds(c0, BLK)].astype(jnp.float32) * live
        lt_ref[:, rb * BLK:(rb + 1) * BLK] = vals.T.astype(jnp.bfloat16)
    term = jnp.dot(lt_ref[...], s_ref[...], preferred_element_type=jnp.float32)
    if acc_ref is None:
        out_ref[...] = term
        blk = tile_ref[k]
        e0 = pl.multiple_of(blk * BLK, BLK)
        rows = lax.broadcasted_iota(jnp.int32, (BLK, BLK), 0)
        cols = lax.broadcasted_iota(jnp.int32, (BLK, BLK), 1)
        dvals = diag_ref[pl.ds(blk, 1), :] * flag_ref[k].astype(jnp.float32)
        out_ref[:, pl.ds(e0, BLK)] += jnp.where(rows == cols, dvals, 0.0)
    elif extra_ref is None:
        out_ref[...] = acc_ref[...] + term
    else:
        out_ref[...] = (acc_ref[...] + extra_ref[...]) + term


def gram_rows(slab, weights, live_blocks, src_left, src_right, out_tiles, diagonal, flags, group, acc=None,
              extra=None):
    height = slab.shape[0]
    col_blocks = L // BLK
    out_blocks = src_left.shape[0]
    in_specs = [
        pl.BlockSpec((height, L), lambda k, *_: (0, 0)),
        pl.BlockSpec((height, BLK), lambda k, *_: (0, 0)),
        pl.BlockSpec((col_blocks, BLK), lambda k, *_: (0, 0)),
    ]
    operands = [slab, jnp.broadcast_to(weights.reshape(height, 1), (height, BLK)), diagonal.reshape(col_blocks, BLK)]
    aliases = {}
    out_spec = pl.BlockSpec((None, BLK, L), lambda k, *_: (k // group, k % group, 0))
    if acc is not None:
        in_specs.append(out_spec)
        operands.append(acc)
        aliases = {8: 0}
    if extra is not None:
        in_specs.append(out_spec)
        operands.append(extra)
    grid_spec = pltpu.PrefetchScalarGridSpec(
        num_scalar_prefetch=5,
        grid=(out_blocks,),
        in_specs=in_specs,
        out_specs=out_spec,
        scratch_shapes=[pltpu.VMEM((height, L), jnp.bfloat16), pltpu.VMEM((BLK, height), jnp.bfloat16)],
    )
    return pl.pallas_call(
        gram_kernel,
        grid_spec=grid_spec,
        out_shape=jax.ShapeDtypeStruct((out_blocks // group, group * BLK, L), jnp.float32),
        input_output_aliases=aliases,
        compiler_params=pltpu.CompilerParams(vmem_limit_bytes=56 * 1024 * 1024),
    )(src_left, src_right, out_tiles, live_blocks.reshape(-1), flags, *operands)


def split_kernel(src_left, src_right, tile_ref, mask_ref, flag_ref, g_ref, w_ref, diag_ref, *rest,
                 group, accumulate):
    if accumulate:
        acc_first, acc_second, out_first, out_second, s_ref, lt_ref = rest
    else:
        acc_first = acc_second = None
        out_first, out_second, s_ref, lt_ref = rest
    k = pl.program_id(0)
    row_blocks = g_ref.shape[0] // BLK
    col_blocks = g_ref.shape[1] // BLK

    @pl.when(k == 0)
    def _():
        def fill(j, carry):
            src = src_right[j]
            c0 = pl.multiple_of(src * BLK, BLK)
            d0 = pl.multiple_of(j * BLK, BLK)
            for rb in range(row_blocks):
                live = mask_ref[rb * col_blocks + src].astype(jnp.float32)
                vals = g_ref[rb * BLK:(rb + 1) * BLK, pl.ds(c0, BLK)].astype(jnp.float32)
                wts = w_ref[rb * BLK:(rb + 1) * BLK, :]
                s_ref[rb * BLK:(rb + 1) * BLK, pl.ds(d0, BLK)] = (wts * (vals * live)).astype(jnp.bfloat16)
            return carry
        lax.fori_loop(0, col_blocks, fill, 0)

    src = src_left[k]
    c0 = pl.multiple_of(src * BLK, BLK)
    for rb in range(row_blocks):
        live = mask_ref[rb * col_blocks + src].astype(jnp.float32)
        vals = g_ref[rb * BLK:(rb + 1) * BLK, pl.ds(c0, BLK)].astype(jnp.float32) * live
        lt_ref[:, rb * BLK:(rb + 1) * BLK] = vals.T.astype(jnp.bfloat16)
    term = jnp.dot(lt_ref[...], s_ref[...], preferred_element_type=jnp.float32)

    def store(out_ref, acc_ref):
        if acc_ref is None:
            out_ref[...] = term
            blk = tile_ref[k]
            e0 = pl.multiple_of(blk * BLK, BLK)
            rows = lax.broadcasted_iota(jnp.int32, (BLK, BLK), 0)
            cols = lax.broadcasted_iota(jnp.int32, (BLK, BLK), 1)
            dvals = diag_ref[pl.ds(blk, 1), :] * flag_ref[k].astype(jnp.float32)
            out_ref[:, pl.ds(e0, BLK)] += jnp.where(rows == cols, dvals, 0.0)
        else:
            out_ref[...] = acc_ref[...] + term

    @pl.when(k < group)
    def _():
        store(out_first, acc_first)

    @pl.when(k >= group)
    def _():
        store(out_second, acc_second)


def split_rows(slab, weights, live_blocks, src_left, src_right, out_tiles, diagonal, flags, group,
               acc=None):
    height = slab.shape[0]
    col_blocks = L // BLK
    in_specs = [
        pl.BlockSpec((height, L), lambda k, *_: (0, 0)),
        pl.BlockSpec((height, BLK), lambda k, *_: (0, 0)),
        pl.BlockSpec((col_blocks, BLK), lambda k, *_: (0, 0)),
    ]
    operands = [slab, jnp.broadcast_to(weights.reshape(height, 1), (height, BLK)), diagonal.reshape(col_blocks, BLK)]
    first_spec = pl.BlockSpec((BLK, L), lambda k, *_: (jnp.minimum(k, group - 1), 0))
    second_spec = pl.BlockSpec((BLK, L), lambda k, *_: (jnp.maximum(k - group, 0), 0))
    aliases = {}
    if acc is not None:
        in_specs += [first_spec, second_spec]
        operands += list(acc)
        aliases = {8: 0, 9: 1}
    grid_spec = pltpu.PrefetchScalarGridSpec(
        num_scalar_prefetch=5,
        grid=(2 * group,),
        in_specs=in_specs,
        out_specs=[first_spec, second_spec],
        scratch_shapes=[pltpu.VMEM((height, L), jnp.bfloat16), pltpu.VMEM((BLK, height), jnp.bfloat16)],
    )
    shape = jax.ShapeDtypeStruct((group * BLK, L), jnp.float32)
    return pl.pallas_call(
        functools.partial(split_kernel, group=group, accumulate=acc is not None),
        grid_spec=grid_spec,
        out_shape=(shape, shape),
        input_output_aliases=aliases,
        compiler_params=pltpu.CompilerParams(vmem_limit_bytes=56 * 1024 * 1024),
    )(src_left, src_right, out_tiles, live_blocks.reshape(-1), flags, *operands)


HIGHEST = lax.Precision.HIGHEST


def join_segments(earlier_seg, later_seg):
    top_one, cross_one, bottom_one = earlier_seg
    top_two, cross_two, bottom_two = later_seg
    middle = bottom_one + top_two
    middle = 0.5 * (middle + middle.T)
    factor = jnp.linalg.cholesky(middle)
    half_width = top_one.shape[0]
    solved = lax.linalg.triangular_solve(
        factor, jnp.concatenate([cross_one.T, cross_two], axis=1), left_side=True, lower=True
    )
    solve_one = solved[:, :half_width]
    solve_two = solved[:, half_width:]
    top_new = top_one - jnp.dot(solve_one.T, solve_one, precision=HIGHEST)
    cross_new = -jnp.dot(solve_one.T, solve_two, precision=HIGHEST)
    bottom_new = bottom_two - jnp.dot(solve_two.T, solve_two, precision=HIGHEST)
    return (top_new, cross_new, bottom_new)


def contract_rows(left_cols, right_cols):
    return lax.dot_general(
        left_cols, right_cols, (((0,), (0,)), ((), ())), preferred_element_type=jnp.float32
    )


def local(coupling, row_scale, block_mask, link_map, tile_order, link_diag):
    local_slab = coupling[0]
    row_weights = row_scale[0]
    live_blocks = block_mask[0]
    block_map = link_map[0]
    diagonal = link_diag[0]
    slab_height = local_slab.shape[0]
    block_count = L // BLK
    my_index = lax.axis_index("row")
    block_ids = jnp.arange(block_count, dtype=jnp.int32)
    source = jnp.sum(
        block_ids[None, :] * (block_map[None, :] == block_ids[:, None]).astype(jnp.int32), axis=1
    )

    def edge_cols(global_block):
        local_block = source[global_block]
        cols = lax.dynamic_slice_in_dim(local_slab, local_block * BLK, BLK, axis=1)
        live = lax.dynamic_index_in_dim(live_blocks, local_block, 1, False)
        cols = (cols.reshape(slab_height // BLK, BLK, BLK) * live.astype(jnp.bfloat16)[:, None, None])
        cols = cols.reshape(slab_height, BLK)
        weighted = (row_weights[:, None] * cols.astype(jnp.float32)).astype(jnp.bfloat16)
        return cols, weighted

    first_cols, first_scaled = edge_cols(0)
    final_cols, final_scaled = edge_cols(block_count - 1)
    edge_gram = contract_rows(
        jnp.concatenate([first_cols, final_cols], axis=1),
        jnp.concatenate([first_scaled, final_scaled], axis=1),
    )
    part_pieces = jnp.stack(
        [edge_gram[:BLK, :BLK], edge_gram[:BLK, BLK:], edge_gram[BLK:, BLK:]]
    )
    owners = lax.axis_size("row")
    own_blocks = block_count // owners

    def exchange(value, step):
        return lax.ppermute(value, "row", [(src, src ^ step) for src in range(owners)])

    packed_side = jnp.concatenate([row_weights, live_blocks.reshape(-1).astype(jnp.float32)])
    side_slots = jnp.zeros((owners, packed_side.shape[0]), jnp.float32)
    side_slots = lax.dynamic_update_index_in_dim(side_slots, packed_side, my_index, 0)
    piece_count = part_pieces.size
    summed_all = jnp.concatenate([part_pieces.reshape(-1), side_slots.reshape(-1)])
    if owners == 4:
        summed_all = summed_all + exchange(summed_all, 1)
        summed_all = summed_all + exchange(summed_all, 2)
    else:
        summed_all = lax.psum(summed_all, "row")
    kernel_slab, summed_all = lax.optimization_barrier((local_slab, summed_all))
    summed = summed_all[:piece_count].reshape(part_pieces.shape)
    every_side = summed_all[piece_count:].reshape(side_slots.shape)
    eye = jnp.eye(BLK, dtype=jnp.float32)
    segment = jnp.stack([
        summed[0] + eye * diagonal[:BLK][None, :],
        summed[1],
        summed[2] + eye * diagonal[L - BLK :][None, :],
    ])

    if owners == 4:
        halves = 2
        half_rows = slab_height // halves
        across_halves = [
            exchange(lax.slice_in_dim(kernel_slab, h * half_rows, (h + 1) * half_rows), 2)
            for h in range(halves)
        ]
        across_side = lax.dynamic_index_in_dim(every_side, my_index ^ 2, 0, False)
        across_weights = across_side[:slab_height]
        across_live = across_side[slab_height:].reshape(live_blocks.shape).astype(jnp.int32)
        order = jnp.concatenate(
            [lax.dynamic_slice_in_dim(tile_order, (my_index ^ q) * own_blocks, own_blocks) for q in range(2)]
        )
        flags = (jnp.arange(2 * own_blocks) < own_blocks).astype(jnp.int32)
        left_src = jnp.take(source, order)

        def own_part(slab_in):
            return split_rows(
                slab_in, row_weights, live_blocks, left_src, source, order, diagonal, flags, own_blocks,
            )

        def across_part(slab_in, partial, half):
            rows = lax.slice_in_dim(across_weights, half * half_rows, (half + 1) * half_rows)
            live = lax.slice_in_dim(
                across_live, half * (half_rows // BLK), (half + 1) * (half_rows // BLK)
            )
            return split_rows(
                slab_in, rows, live, left_src, source, order, diagonal, flags, own_blocks, partial,
            )

        partner_side = lax.dynamic_index_in_dim(every_side, my_index ^ 3, 0, False)
        partner_weights = partner_side[:slab_height]
        partner_live = partner_side[slab_height:].reshape(live_blocks.shape).astype(jnp.int32)
        last_weights = jnp.concatenate([
            lax.slice_in_dim(across_weights, half_rows, slab_height),
            lax.slice_in_dim(partner_weights, half_rows, slab_height),
        ])
        last_live = jnp.concatenate([
            lax.slice_in_dim(across_live, half_rows // BLK, slab_height // BLK),
            lax.slice_in_dim(partner_live, half_rows // BLK, slab_height // BLK),
        ])
        mine_order = order[:own_blocks]

        def last_part(slab_in, mine, received):
            total = gram_rows(
                slab_in, last_weights, last_live, jnp.take(source, mine_order), source, mine_order,
                diagonal, flags[:own_blocks], own_blocks, mine[None], received[None],
            )
            return total[0]

        hooks = {1: ("own", kernel_slab), 2: ("across", across_halves[0]), 3: ("last", across_halves[1])}
    else:
        hooks = {}
        flags = jnp.full((block_count,), (my_index == 0).astype(jnp.int32))
        partial = gram_rows(
            kernel_slab, row_weights, live_blocks, jnp.take(source, tile_order), source,
            tile_order, diagonal, flags, own_blocks,
        )
        owned = lax.psum_scatter(
            partial.reshape(L, L), "row", scatter_dimension=0, tiled=True
        )

    times = lax.axis_size("tm")
    position = lax.axis_index("tm")
    running = (segment[0], segment[1], segment[2])
    shift = 1
    round_index = 0
    state = {}

    def run_hook(kind, slab_in, running):
        slab_in, running = lax.optimization_barrier((slab_in, running))
        if kind == "own":
            state["partial"] = own_part(slab_in)
        elif kind == "across":
            mine, partners = across_part(slab_in, state["partial"], 0)
            state["mine"] = mine
            state["received"] = exchange(partners, 1)
        else:
            both = jnp.concatenate([slab_in, exchange(slab_in, 1)], axis=0)
            state["owned"] = last_part(both, state["mine"], state["received"])
        return running

    while shift < times:
        if round_index in hooks:
            running = run_hook(*hooks.pop(round_index), running)
        round_index += 1
        pairs = [(src, src + shift) for src in range(times - shift)]
        moved = lax.ppermute(jnp.stack(running), "tm", pairs)
        earlier = (moved[0], moved[1], moved[2])
        joined = join_segments(earlier, running)
        take = position >= shift
        running = tuple(jnp.where(take, new, old) for new, old in zip(joined, running))
        shift *= 2
    for key in sorted(hooks):
        running = run_hook(*hooks[key], running)
    if "owned" in state:
        owned = state["owned"]
    chain_out = jnp.stack(running)[None]
    return (owned[None], chain_out)


def solution(mesh):
    placed = (
        P("tm", "row", None),
        P("tm", "row"),
        P("tm", "row", None),
        P("tm", None),
        P(),
        P("tm", None),
    )
    return jax.shard_map(
        local,
        mesh=mesh,
        in_specs=placed,
        out_specs=(P("tm", "row", None), P("tm", None, None, None)),
        check_vma=False,
    )
```

```python
import functools

import jax
import jax.numpy as jnp
from jax import lax
from jax.sharding import PartitionSpec as P
from jax.experimental import pallas as pl
from jax.experimental.pallas import tpu as pltpu

L = 2048
BLK = 128


def gram_kernel(src_left, src_right, tile_ref, mask_ref, flag_ref, g_ref, w_ref, diag_ref, *rest):
    extra_ref = None
    if len(rest) == 5:
        acc_ref, extra_ref, out_ref, s_ref, lt_ref = rest
    elif len(rest) == 4:
        acc_ref, out_ref, s_ref, lt_ref = rest
    else:
        acc_ref = None
        out_ref, s_ref, lt_ref = rest
    k = pl.program_id(0)
    row_blocks = g_ref.shape[0] // BLK
    col_blocks = g_ref.shape[1] // BLK

    @pl.when(k == 0)
    def _():
        def fill(j, carry):
            src = src_right[j]
            c0 = pl.multiple_of(src * BLK, BLK)
            d0 = pl.multiple_of(j * BLK, BLK)
            for rb in range(row_blocks):
                live = mask_ref[rb * col_blocks + src].astype(jnp.float32)
                vals = g_ref[rb * BLK:(rb + 1) * BLK, pl.ds(c0, BLK)].astype(jnp.float32)
                wts = w_ref[rb * BLK:(rb + 1) * BLK, :]
                s_ref[rb * BLK:(rb + 1) * BLK, pl.ds(d0, BLK)] = (wts * (vals * live)).astype(jnp.bfloat16)
            return carry
        lax.fori_loop(0, col_blocks, fill, 0)

    src = src_left[k]
    c0 = pl.multiple_of(src * BLK, BLK)
    for rb in range(row_blocks):
        live = mask_ref[rb * col_blocks + src].astype(jnp.float32)
        vals = g_ref[rb * BLK:(rb + 1) * BLK, pl.ds(c0, BLK)].astype(jnp.float32) * live
        lt_ref[:, rb * BLK:(rb + 1) * BLK] = vals.T.astype(jnp.bfloat16)
    term = jnp.dot(lt_ref[...], s_ref[...], preferred_element_type=jnp.float32)
    if acc_ref is None:
        out_ref[...] = term
        blk = tile_ref[k]
        e0 = pl.multiple_of(blk * BLK, BLK)
        rows = lax.broadcasted_iota(jnp.int32, (BLK, BLK), 0)
        cols = lax.broadcasted_iota(jnp.int32, (BLK, BLK), 1)
        dvals = diag_ref[pl.ds(blk, 1), :] * flag_ref[k].astype(jnp.float32)
        out_ref[:, pl.ds(e0, BLK)] += jnp.where(rows == cols, dvals, 0.0)
    elif extra_ref is None:
        out_ref[...] = acc_ref[...] + term
    else:
        out_ref[...] = (acc_ref[...] + extra_ref[...]) + term


def gram_rows(slab, weights, live_blocks, src_left, src_right, out_tiles, diagonal, flags, group, acc=None,
              extra=None):
    height = slab.shape[0]
    col_blocks = L // BLK
    out_blocks = src_left.shape[0]
    in_specs = [
        pl.BlockSpec((height, L), lambda k, *_: (0, 0)),
        pl.BlockSpec((height, BLK), lambda k, *_: (0, 0)),
        pl.BlockSpec((col_blocks, BLK), lambda k, *_: (0, 0)),
    ]
    operands = [slab, jnp.broadcast_to(weights.reshape(height, 1), (height, BLK)), diagonal.reshape(col_blocks, BLK)]
    aliases = {}
    out_spec = pl.BlockSpec((None, BLK, L), lambda k, *_: (k // group, k % group, 0))
    if acc is not None:
        in_specs.append(out_spec)
        operands.append(acc)
        aliases = {8: 0}
    if extra is not None:
        in_specs.append(out_spec)
        operands.append(extra)
    grid_spec = pltpu.PrefetchScalarGridSpec(
        num_scalar_prefetch=5,
        grid=(out_blocks,),
        in_specs=in_specs,
        out_specs=out_spec,
        scratch_shapes=[pltpu.VMEM((height, L), jnp.bfloat16), pltpu.VMEM((BLK, height), jnp.bfloat16)],
    )
    return pl.pallas_call(
        gram_kernel,
        grid_spec=grid_spec,
        out_shape=jax.ShapeDtypeStruct((out_blocks // group, group * BLK, L), jnp.float32),
        input_output_aliases=aliases,
        compiler_params=pltpu.CompilerParams(vmem_limit_bytes=56 * 1024 * 1024),
    )(src_left, src_right, out_tiles, live_blocks.reshape(-1), flags, *operands)


def split_kernel(src_left, src_right, tile_ref, mask_ref, flag_ref, g_ref, w_ref, diag_ref, *rest,
                 group, accumulate):
    if accumulate:
        acc_first, acc_second, out_first, out_second, s_ref, lt_ref = rest
    else:
        acc_first = acc_second = None
        out_first, out_second, s_ref, lt_ref = rest
    k = pl.program_id(0)
    row_blocks = g_ref.shape[0] // BLK
    col_blocks = g_ref.shape[1] // BLK

    @pl.when(k == 0)
    def _():
        def fill(j, carry):
            src = src_right[j]
            c0 = pl.multiple_of(src * BLK, BLK)
            d0 = pl.multiple_of(j * BLK, BLK)
            for rb in range(row_blocks):
                live = mask_ref[rb * col_blocks + src].astype(jnp.float32)
                vals = g_ref[rb * BLK:(rb + 1) * BLK, pl.ds(c0, BLK)].astype(jnp.float32)
                wts = w_ref[rb * BLK:(rb + 1) * BLK, :]
                s_ref[rb * BLK:(rb + 1) * BLK, pl.ds(d0, BLK)] = (wts * (vals * live)).astype(jnp.bfloat16)
            return carry
        lax.fori_loop(0, col_blocks, fill, 0)

    src = src_left[k]
    c0 = pl.multiple_of(src * BLK, BLK)
    for rb in range(row_blocks):
        live = mask_ref[rb * col_blocks + src].astype(jnp.float32)
        vals = g_ref[rb * BLK:(rb + 1) * BLK, pl.ds(c0, BLK)].astype(jnp.float32) * live
        lt_ref[:, rb * BLK:(rb + 1) * BLK] = vals.T.astype(jnp.bfloat16)
    term = jnp.dot(lt_ref[...], s_ref[...], preferred_element_type=jnp.float32)

    def store(out_ref, acc_ref):
        if acc_ref is None:
            out_ref[...] = term
            blk = tile_ref[k]
            e0 = pl.multiple_of(blk * BLK, BLK)
            rows = lax.broadcasted_iota(jnp.int32, (BLK, BLK), 0)
            cols = lax.broadcasted_iota(jnp.int32, (BLK, BLK), 1)
            dvals = diag_ref[pl.ds(blk, 1), :] * flag_ref[k].astype(jnp.float32)
            out_ref[:, pl.ds(e0, BLK)] += jnp.where(rows == cols, dvals, 0.0)
        else:
            out_ref[...] = acc_ref[...] + term

    @pl.when(k < group)
    def _():
        store(out_first, acc_first)

    @pl.when(k >= group)
    def _():
        store(out_second, acc_second)


def split_rows(slab, weights, live_blocks, src_left, src_right, out_tiles, diagonal, flags, group,
               acc=None):
    height = slab.shape[0]
    col_blocks = L // BLK
    in_specs = [
        pl.BlockSpec((height, L), lambda k, *_: (0, 0)),
        pl.BlockSpec((height, BLK), lambda k, *_: (0, 0)),
        pl.BlockSpec((col_blocks, BLK), lambda k, *_: (0, 0)),
    ]
    operands = [slab, jnp.broadcast_to(weights.reshape(height, 1), (height, BLK)), diagonal.reshape(col_blocks, BLK)]
    first_spec = pl.BlockSpec((BLK, L), lambda k, *_: (jnp.minimum(k, group - 1), 0))
    second_spec = pl.BlockSpec((BLK, L), lambda k, *_: (jnp.maximum(k - group, 0), 0))
    aliases = {}
    if acc is not None:
        in_specs += [first_spec, second_spec]
        operands += list(acc)
        aliases = {8: 0, 9: 1}
    grid_spec = pltpu.PrefetchScalarGridSpec(
        num_scalar_prefetch=5,
        grid=(2 * group,),
        in_specs=in_specs,
        out_specs=[first_spec, second_spec],
        scratch_shapes=[pltpu.VMEM((height, L), jnp.bfloat16), pltpu.VMEM((BLK, height), jnp.bfloat16)],
    )
    shape = jax.ShapeDtypeStruct((group * BLK, L), jnp.float32)
    return pl.pallas_call(
        functools.partial(split_kernel, group=group, accumulate=acc is not None),
        grid_spec=grid_spec,
        out_shape=(shape, shape),
        input_output_aliases=aliases,
        compiler_params=pltpu.CompilerParams(vmem_limit_bytes=56 * 1024 * 1024),
    )(src_left, src_right, out_tiles, live_blocks.reshape(-1), flags, *operands)


def pair_kernel(src_left, src_right, tile_ref, mask_ref, flag_ref, g1_ref, g2_ref, w_ref, diag_ref,
                acc_ref, extra_ref, out_ref, s_ref, lt_ref):
    k = pl.program_id(0)
    first_blocks = g1_ref.shape[0] // BLK
    row_blocks = first_blocks + g2_ref.shape[0] // BLK
    col_blocks = g1_ref.shape[1] // BLK

    def rows_of(rb, cols):
        if rb < first_blocks:
            return g1_ref[rb * BLK:(rb + 1) * BLK, cols]
        return g2_ref[(rb - first_blocks) * BLK:(rb - first_blocks + 1) * BLK, cols]

    @pl.when(k == 0)
    def _():
        def fill(j, carry):
            src = src_right[j]
            c0 = pl.multiple_of(src * BLK, BLK)
            d0 = pl.multiple_of(j * BLK, BLK)
            for rb in range(row_blocks):
                live = mask_ref[rb * col_blocks + src].astype(jnp.float32)
                vals = rows_of(rb, pl.ds(c0, BLK)).astype(jnp.float32)
                wts = w_ref[rb * BLK:(rb + 1) * BLK, :]
                s_ref[rb * BLK:(rb + 1) * BLK, pl.ds(d0, BLK)] = (wts * (vals * live)).astype(jnp.bfloat16)
            return carry
        lax.fori_loop(0, col_blocks, fill, 0)

    src = src_left[k]
    c0 = pl.multiple_of(src * BLK, BLK)
    for rb in range(row_blocks):
        live = mask_ref[rb * col_blocks + src].astype(jnp.float32)
        vals = rows_of(rb, pl.ds(c0, BLK)).astype(jnp.float32) * live
        lt_ref[:, rb * BLK:(rb + 1) * BLK] = vals.T.astype(jnp.bfloat16)
    term = jnp.dot(lt_ref[...], s_ref[...], preferred_element_type=jnp.float32)
    out_ref[...] = (acc_ref[...] + extra_ref[...]) + term


def pair_rows(slab_one, slab_two, weights, live_blocks, src_left, src_right, out_tiles, diagonal, flags,
              group, acc, extra):
    height = slab_one.shape[0] + slab_two.shape[0]
    col_blocks = L // BLK
    out_blocks = src_left.shape[0]
    out_spec = pl.BlockSpec((None, BLK, L), lambda k, *_: (k // group, k % group, 0))
    grid_spec = pltpu.PrefetchScalarGridSpec(
        num_scalar_prefetch=5,
        grid=(out_blocks,),
        in_specs=[
            pl.BlockSpec(slab_one.shape, lambda k, *_: (0, 0)),
            pl.BlockSpec(slab_two.shape, lambda k, *_: (0, 0)),
            pl.BlockSpec((height, BLK), lambda k, *_: (0, 0)),
            pl.BlockSpec((col_blocks, BLK), lambda k, *_: (0, 0)),
            out_spec,
            out_spec,
        ],
        out_specs=out_spec,
        scratch_shapes=[pltpu.VMEM((height, L), jnp.bfloat16), pltpu.VMEM((BLK, height), jnp.bfloat16)],
    )
    return pl.pallas_call(
        pair_kernel,
        grid_spec=grid_spec,
        out_shape=jax.ShapeDtypeStruct((out_blocks // group, group * BLK, L), jnp.float32),
        input_output_aliases={9: 0},
        compiler_params=pltpu.CompilerParams(vmem_limit_bytes=56 * 1024 * 1024),
    )(src_left, src_right, out_tiles, live_blocks.reshape(-1), flags, slab_one, slab_two,
      jnp.broadcast_to(weights.reshape(height, 1), (height, BLK)), diagonal.reshape(col_blocks, BLK),
      acc, extra)


HIGHEST = lax.Precision.HIGHEST


def join_segments(earlier_seg, later_seg):
    top_one, cross_one, bottom_one = earlier_seg
    top_two, cross_two, bottom_two = later_seg
    middle = bottom_one + top_two
    middle = 0.5 * (middle + middle.T)
    factor = jnp.linalg.cholesky(middle)
    half_width = top_one.shape[0]
    solved = lax.linalg.triangular_solve(
        factor, jnp.concatenate([cross_one.T, cross_two], axis=1), left_side=True, lower=True
    )
    solve_one = solved[:, :half_width]
    solve_two = solved[:, half_width:]
    top_new = top_one - jnp.dot(solve_one.T, solve_one, precision=HIGHEST)
    cross_new = -jnp.dot(solve_one.T, solve_two, precision=HIGHEST)
    bottom_new = bottom_two - jnp.dot(solve_two.T, solve_two, precision=HIGHEST)
    return (top_new, cross_new, bottom_new)


def contract_rows(left_cols, right_cols):
    return lax.dot_general(
        left_cols, right_cols, (((0,), (0,)), ((), ())), preferred_element_type=jnp.float32
    )


def local(coupling, row_scale, block_mask, link_map, tile_order, link_diag):
    local_slab = coupling[0]
    row_weights = row_scale[0]
    live_blocks = block_mask[0]
    block_map = link_map[0]
    diagonal = link_diag[0]
    slab_height = local_slab.shape[0]
    block_count = L // BLK
    my_index = lax.axis_index("row")
    block_ids = jnp.arange(block_count, dtype=jnp.int32)
    source = jnp.sum(
        block_ids[None, :] * (block_map[None, :] == block_ids[:, None]).astype(jnp.int32), axis=1
    )

    def edge_cols(global_block):
        local_block = source[global_block]
        cols = lax.dynamic_slice_in_dim(local_slab, local_block * BLK, BLK, axis=1)
        live = lax.dynamic_index_in_dim(live_blocks, local_block, 1, False)
        cols = (cols.reshape(slab_height // BLK, BLK, BLK) * live.astype(jnp.bfloat16)[:, None, None])
        cols = cols.reshape(slab_height, BLK)
        weighted = (row_weights[:, None] * cols.astype(jnp.float32)).astype(jnp.bfloat16)
        return cols, weighted

    first_cols, first_scaled = edge_cols(0)
    final_cols, final_scaled = edge_cols(block_count - 1)
    edge_gram = contract_rows(
        jnp.concatenate([first_cols, final_cols], axis=1),
        jnp.concatenate([first_scaled, final_scaled], axis=1),
    )
    part_pieces = jnp.stack(
        [edge_gram[:BLK, :BLK], edge_gram[:BLK, BLK:], edge_gram[BLK:, BLK:]]
    )
    owners = lax.axis_size("row")
    own_blocks = block_count // owners

    def exchange(value, step):
        return lax.ppermute(value, "row", [(src, src ^ step) for src in range(owners)])

    packed_side = jnp.concatenate([row_weights, live_blocks.reshape(-1).astype(jnp.float32)])
    side_slots = jnp.zeros((owners, packed_side.shape[0]), jnp.float32)
    side_slots = lax.dynamic_update_index_in_dim(side_slots, packed_side, my_index, 0)
    piece_count = part_pieces.size
    summed_all = jnp.concatenate([part_pieces.reshape(-1), side_slots.reshape(-1)])
    if owners == 4:
        summed_all = summed_all + exchange(summed_all, 1)
        summed_all = summed_all + exchange(summed_all, 2)
    else:
        summed_all = lax.psum(summed_all, "row")
    kernel_slab, summed_all = lax.optimization_barrier((local_slab, summed_all))
    summed = summed_all[:piece_count].reshape(part_pieces.shape)
    every_side = summed_all[piece_count:].reshape(side_slots.shape)
    eye = jnp.eye(BLK, dtype=jnp.float32)
    segment = jnp.stack([
        summed[0] + eye * diagonal[:BLK][None, :],
        summed[1],
        summed[2] + eye * diagonal[L - BLK :][None, :],
    ])

    if owners == 4:
        halves = 2
        half_rows = slab_height // halves
        across_halves = [
            exchange(lax.slice_in_dim(kernel_slab, h * half_rows, (h + 1) * half_rows), 2)
            for h in range(halves)
        ]
        across_side = lax.dynamic_index_in_dim(every_side, my_index ^ 2, 0, False)
        across_weights = across_side[:slab_height]
        across_live = across_side[slab_height:].reshape(live_blocks.shape).astype(jnp.int32)
        order = jnp.concatenate(
            [lax.dynamic_slice_in_dim(tile_order, (my_index ^ q) * own_blocks, own_blocks) for q in range(2)]
        )
        flags = (jnp.arange(2 * own_blocks) < own_blocks).astype(jnp.int32)
        left_src = jnp.take(source, order)

        def own_part(slab_in):
            return split_rows(
                slab_in, row_weights, live_blocks, left_src, source, order, diagonal, flags, own_blocks,
            )

        def across_part(slab_in, partial, half):
            rows = lax.slice_in_dim(across_weights, half * half_rows, (half + 1) * half_rows)
            live = lax.slice_in_dim(
                across_live, half * (half_rows // BLK), (half + 1) * (half_rows // BLK)
            )
            return split_rows(
                slab_in, rows, live, left_src, source, order, diagonal, flags, own_blocks, partial,
            )

        partner_side = lax.dynamic_index_in_dim(every_side, my_index ^ 3, 0, False)
        partner_weights = partner_side[:slab_height]
        partner_live = partner_side[slab_height:].reshape(live_blocks.shape).astype(jnp.int32)
        last_weights = jnp.concatenate([
            lax.slice_in_dim(across_weights, half_rows, slab_height),
            lax.slice_in_dim(partner_weights, half_rows, slab_height),
        ])
        last_live = jnp.concatenate([
            lax.slice_in_dim(across_live, half_rows // BLK, slab_height // BLK),
            lax.slice_in_dim(partner_live, half_rows // BLK, slab_height // BLK),
        ])
        mine_order = order[:own_blocks]

        def last_part(slab_one, slab_two, mine, received):
            total = pair_rows(
                slab_one, slab_two, last_weights, last_live, jnp.take(source, mine_order), source,
                mine_order, diagonal, flags[:own_blocks], own_blocks, mine[None], received[None],
            )
            return total[0]

        hooks = {1: ("own", kernel_slab), 2: ("across", across_halves[0]), 3: ("last", across_halves[1])}
    else:
        hooks = {}
        flags = jnp.full((block_count,), (my_index == 0).astype(jnp.int32))
        partial = gram_rows(
            kernel_slab, row_weights, live_blocks, jnp.take(source, tile_order), source,
            tile_order, diagonal, flags, own_blocks,
        )
        owned = lax.psum_scatter(
            partial.reshape(L, L), "row", scatter_dimension=0, tiled=True
        )

    times = lax.axis_size("tm")
    position = lax.axis_index("tm")
    running = (segment[0], segment[1], segment[2])
    shift = 1
    round_index = 0
    state = {}

    def run_hook(kind, slab_in, running):
        slab_in, running = lax.optimization_barrier((slab_in, running))
        if kind == "own":
            state["partial"] = own_part(slab_in)
        elif kind == "across":
            mine, partners = across_part(slab_in, state["partial"], 0)
            state["mine"] = mine
            state["received"] = exchange(partners, 1)
        else:
            state["owned"] = last_part(
                slab_in, exchange(slab_in, 1), state["mine"], state["received"]
            )
        return running

    while shift < times:
        if round_index in hooks:
            running = run_hook(*hooks.pop(round_index), running)
        round_index += 1
        pairs = [(src, src + shift) for src in range(times - shift)]
        moved = lax.ppermute(jnp.stack(running), "tm", pairs)
        earlier = (moved[0], moved[1], moved[2])
        joined = join_segments(earlier, running)
        take = position >= shift
        running = tuple(jnp.where(take, new, old) for new, old in zip(joined, running))
        shift *= 2
    for key in sorted(hooks):
        running = run_hook(*hooks[key], running)
    if "owned" in state:
        owned = state["owned"]
    chain_out = jnp.stack(running)[None]
    return (owned[None], chain_out)


def solution(mesh):
    placed = (
        P("tm", "row", None),
        P("tm", "row"),
        P("tm", "row", None),
        P("tm", None),
        P(),
        P("tm", None),
    )
    return jax.shard_map(
        local,
        mesh=mesh,
        in_specs=placed,
        out_specs=(P("tm", "row", None), P("tm", None, None, None)),
        check_vma=False,
    )
```

```python
import functools

import jax
import jax.numpy as jnp
from jax import lax
from jax.sharding import PartitionSpec as P
from jax.experimental import pallas as pl
from jax.experimental.pallas import tpu as pltpu

L = 2048
BLK = 128


def gram_kernel(src_left, src_right, tile_ref, mask_ref, flag_ref, g_ref, w_ref, diag_ref, *rest):
    extra_ref = None
    if len(rest) == 5:
        acc_ref, extra_ref, out_ref, s_ref, lt_ref = rest
    elif len(rest) == 4:
        acc_ref, out_ref, s_ref, lt_ref = rest
    else:
        acc_ref = None
        out_ref, s_ref, lt_ref = rest
    k = pl.program_id(0)
    row_blocks = g_ref.shape[0] // BLK
    col_blocks = g_ref.shape[1] // BLK

    @pl.when(k == 0)
    def _():
        def fill(j, carry):
            src = src_right[j]
            c0 = pl.multiple_of(src * BLK, BLK)
            d0 = pl.multiple_of(j * BLK, BLK)
            for rb in range(row_blocks):
                live = mask_ref[rb * col_blocks + src].astype(jnp.float32)
                vals = g_ref[rb * BLK:(rb + 1) * BLK, pl.ds(c0, BLK)].astype(jnp.float32)
                wts = w_ref[rb * BLK:(rb + 1) * BLK, :]
                s_ref[rb * BLK:(rb + 1) * BLK, pl.ds(d0, BLK)] = (wts * (vals * live)).astype(jnp.bfloat16)
            return carry
        lax.fori_loop(0, col_blocks, fill, 0)

    src = src_left[k]
    c0 = pl.multiple_of(src * BLK, BLK)
    for rb in range(row_blocks):
        live = mask_ref[rb * col_blocks + src].astype(jnp.float32)
        vals = g_ref[rb * BLK:(rb + 1) * BLK, pl.ds(c0, BLK)].astype(jnp.float32) * live
        lt_ref[:, rb * BLK:(rb + 1) * BLK] = vals.T.astype(jnp.bfloat16)
    term = jnp.dot(lt_ref[...], s_ref[...], preferred_element_type=jnp.float32)
    if acc_ref is None:
        out_ref[...] = term
        blk = tile_ref[k]
        e0 = pl.multiple_of(blk * BLK, BLK)
        rows = lax.broadcasted_iota(jnp.int32, (BLK, BLK), 0)
        cols = lax.broadcasted_iota(jnp.int32, (BLK, BLK), 1)
        dvals = diag_ref[pl.ds(blk, 1), :] * flag_ref[k].astype(jnp.float32)
        out_ref[:, pl.ds(e0, BLK)] += jnp.where(rows == cols, dvals, 0.0)
    elif extra_ref is None:
        out_ref[...] = acc_ref[...] + term
    else:
        out_ref[...] = (acc_ref[...] + extra_ref[...]) + term


def gram_rows(slab, weights, live_blocks, src_left, src_right, out_tiles, diagonal, flags, group, acc=None,
              extra=None):
    height = slab.shape[0]
    col_blocks = L // BLK
    out_blocks = src_left.shape[0]
    in_specs = [
        pl.BlockSpec((height, L), lambda k, *_: (0, 0)),
        pl.BlockSpec((height, BLK), lambda k, *_: (0, 0)),
        pl.BlockSpec((col_blocks, BLK), lambda k, *_: (0, 0)),
    ]
    operands = [slab, jnp.broadcast_to(weights.reshape(height, 1), (height, BLK)), diagonal.reshape(col_blocks, BLK)]
    aliases = {}
    out_spec = pl.BlockSpec((None, BLK, L), lambda k, *_: (k // group, k % group, 0))
    if acc is not None:
        in_specs.append(out_spec)
        operands.append(acc)
        aliases = {8: 0}
    if extra is not None:
        in_specs.append(out_spec)
        operands.append(extra)
    grid_spec = pltpu.PrefetchScalarGridSpec(
        num_scalar_prefetch=5,
        grid=(out_blocks,),
        in_specs=in_specs,
        out_specs=out_spec,
        scratch_shapes=[pltpu.VMEM((height, L), jnp.bfloat16), pltpu.VMEM((BLK, height), jnp.bfloat16)],
    )
    return pl.pallas_call(
        gram_kernel,
        grid_spec=grid_spec,
        out_shape=jax.ShapeDtypeStruct((out_blocks // group, group * BLK, L), jnp.float32),
        input_output_aliases=aliases,
        compiler_params=pltpu.CompilerParams(vmem_limit_bytes=56 * 1024 * 1024),
    )(src_left, src_right, out_tiles, live_blocks.reshape(-1), flags, *operands)


def split_kernel(src_left, src_right, tile_ref, mask_ref, flag_ref, g_ref, w_ref, diag_ref, *rest,
                 group, accumulate):
    if accumulate:
        acc_first, acc_second, out_first, out_second, s_ref, lt_ref = rest
    else:
        acc_first = acc_second = None
        out_first, out_second, s_ref, lt_ref = rest
    k = pl.program_id(0)
    row_blocks = g_ref.shape[0] // BLK
    col_blocks = g_ref.shape[1] // BLK

    @pl.when(k == 0)
    def _():
        def fill(j, carry):
            src = src_right[j]
            c0 = pl.multiple_of(src * BLK, BLK)
            d0 = pl.multiple_of(j * BLK, BLK)
            for rb in range(row_blocks):
                live = mask_ref[rb * col_blocks + src].astype(jnp.float32)
                vals = g_ref[rb * BLK:(rb + 1) * BLK, pl.ds(c0, BLK)].astype(jnp.float32)
                wts = w_ref[rb * BLK:(rb + 1) * BLK, :]
                s_ref[rb * BLK:(rb + 1) * BLK, pl.ds(d0, BLK)] = (wts * (vals * live)).astype(jnp.bfloat16)
            return carry
        lax.fori_loop(0, col_blocks, fill, 0)

    src = src_left[k]
    c0 = pl.multiple_of(src * BLK, BLK)
    for rb in range(row_blocks):
        live = mask_ref[rb * col_blocks + src].astype(jnp.float32)
        vals = g_ref[rb * BLK:(rb + 1) * BLK, pl.ds(c0, BLK)].astype(jnp.float32) * live
        lt_ref[:, rb * BLK:(rb + 1) * BLK] = vals.T.astype(jnp.bfloat16)
    term = jnp.dot(lt_ref[...], s_ref[...], preferred_element_type=jnp.float32)

    def store(out_ref, acc_ref):
        if acc_ref is None:
            out_ref[...] = term
            blk = tile_ref[k]
            e0 = pl.multiple_of(blk * BLK, BLK)
            rows = lax.broadcasted_iota(jnp.int32, (BLK, BLK), 0)
            cols = lax.broadcasted_iota(jnp.int32, (BLK, BLK), 1)
            dvals = diag_ref[pl.ds(blk, 1), :] * flag_ref[k].astype(jnp.float32)
            out_ref[:, pl.ds(e0, BLK)] += jnp.where(rows == cols, dvals, 0.0)
        else:
            out_ref[...] = acc_ref[...] + term

    @pl.when(k < group)
    def _():
        store(out_first, acc_first)

    @pl.when(k >= group)
    def _():
        store(out_second, acc_second)


def split_rows(slab, weights, live_blocks, src_left, src_right, out_tiles, diagonal, flags, group,
               acc=None):
    height = slab.shape[0]
    col_blocks = L // BLK
    in_specs = [
        pl.BlockSpec((height, L), lambda k, *_: (0, 0)),
        pl.BlockSpec((height, BLK), lambda k, *_: (0, 0)),
        pl.BlockSpec((col_blocks, BLK), lambda k, *_: (0, 0)),
    ]
    operands = [slab, jnp.broadcast_to(weights.reshape(height, 1), (height, BLK)), diagonal.reshape(col_blocks, BLK)]
    first_spec = pl.BlockSpec((BLK, L), lambda k, *_: (jnp.minimum(k, group - 1), 0))
    second_spec = pl.BlockSpec((BLK, L), lambda k, *_: (jnp.maximum(k - group, 0), 0))
    aliases = {}
    if acc is not None:
        in_specs += [first_spec, second_spec]
        operands += list(acc)
        aliases = {8: 0, 9: 1}
    grid_spec = pltpu.PrefetchScalarGridSpec(
        num_scalar_prefetch=5,
        grid=(2 * group,),
        in_specs=in_specs,
        out_specs=[first_spec, second_spec],
        scratch_shapes=[pltpu.VMEM((height, L), jnp.bfloat16), pltpu.VMEM((BLK, height), jnp.bfloat16)],
    )
    shape = jax.ShapeDtypeStruct((group * BLK, L), jnp.float32)
    return pl.pallas_call(
        functools.partial(split_kernel, group=group, accumulate=acc is not None),
        grid_spec=grid_spec,
        out_shape=(shape, shape),
        input_output_aliases=aliases,
        compiler_params=pltpu.CompilerParams(vmem_limit_bytes=56 * 1024 * 1024),
    )(src_left, src_right, out_tiles, live_blocks.reshape(-1), flags, *operands)


def pair_kernel(src_left, src_right, tile_ref, mask_ref, flag_ref, g1_ref, g2_ref, w_ref, diag_ref,
                acc_ref, extra_ref, out_ref, s_ref, lt_ref):
    k = pl.program_id(0)
    first_blocks = g1_ref.shape[0] // BLK
    row_blocks = first_blocks + g2_ref.shape[0] // BLK
    col_blocks = g1_ref.shape[1] // BLK

    def rows_of(rb, cols):
        if rb < first_blocks:
            return g1_ref[rb * BLK:(rb + 1) * BLK, cols]
        return g2_ref[(rb - first_blocks) * BLK:(rb - first_blocks + 1) * BLK, cols]

    @pl.when(k == 0)
    def _():
        def fill(j, carry):
            src = src_right[j]
            c0 = pl.multiple_of(src * BLK, BLK)
            d0 = pl.multiple_of(j * BLK, BLK)
            for rb in range(row_blocks):
                live = mask_ref[rb * col_blocks + src].astype(jnp.float32)
                vals = rows_of(rb, pl.ds(c0, BLK)).astype(jnp.float32)
                wts = w_ref[rb * BLK:(rb + 1) * BLK, :]
                s_ref[rb * BLK:(rb + 1) * BLK, pl.ds(d0, BLK)] = (wts * (vals * live)).astype(jnp.bfloat16)
            return carry
        lax.fori_loop(0, col_blocks, fill, 0)

    src = src_left[k]
    c0 = pl.multiple_of(src * BLK, BLK)
    for rb in range(row_blocks):
        live = mask_ref[rb * col_blocks + src].astype(jnp.float32)
        vals = rows_of(rb, pl.ds(c0, BLK)).astype(jnp.float32) * live
        lt_ref[:, rb * BLK:(rb + 1) * BLK] = vals.T.astype(jnp.bfloat16)
    term = jnp.dot(lt_ref[...], s_ref[...], preferred_element_type=jnp.float32)
    out_ref[...] = (acc_ref[...] + extra_ref[...]) + term


def pair_rows(slab_one, slab_two, weights, live_blocks, src_left, src_right, out_tiles, diagonal, flags,
              group, acc, extra):
    height = slab_one.shape[0] + slab_two.shape[0]
    col_blocks = L // BLK
    out_blocks = src_left.shape[0]
    out_spec = pl.BlockSpec((None, BLK, L), lambda k, *_: (k // group, k % group, 0))
    grid_spec = pltpu.PrefetchScalarGridSpec(
        num_scalar_prefetch=5,
        grid=(out_blocks,),
        in_specs=[
            pl.BlockSpec(slab_one.shape, lambda k, *_: (0, 0)),
            pl.BlockSpec(slab_two.shape, lambda k, *_: (0, 0)),
            pl.BlockSpec((height, BLK), lambda k, *_: (0, 0)),
            pl.BlockSpec((col_blocks, BLK), lambda k, *_: (0, 0)),
            out_spec,
            out_spec,
        ],
        out_specs=out_spec,
        scratch_shapes=[pltpu.VMEM((height, L), jnp.bfloat16), pltpu.VMEM((BLK, height), jnp.bfloat16)],
    )
    return pl.pallas_call(
        pair_kernel,
        grid_spec=grid_spec,
        out_shape=jax.ShapeDtypeStruct((out_blocks // group, group * BLK, L), jnp.float32),
        input_output_aliases={9: 0},
        compiler_params=pltpu.CompilerParams(vmem_limit_bytes=56 * 1024 * 1024),
    )(src_left, src_right, out_tiles, live_blocks.reshape(-1), flags, slab_one, slab_two,
      jnp.broadcast_to(weights.reshape(height, 1), (height, BLK)), diagonal.reshape(col_blocks, BLK),
      acc, extra)


HIGHEST = lax.Precision.HIGHEST


def join_segments(earlier_seg, later_seg):
    top_one, cross_one, bottom_one = earlier_seg
    top_two, cross_two, bottom_two = later_seg
    middle = bottom_one + top_two
    middle = 0.5 * (middle + middle.T)
    factor = jnp.linalg.cholesky(middle)
    half_width = top_one.shape[0]
    solved = lax.linalg.triangular_solve(
        factor, jnp.concatenate([cross_one.T, cross_two], axis=1), left_side=True, lower=True
    )
    solve_one = solved[:, :half_width]
    solve_two = solved[:, half_width:]
    top_new = top_one - jnp.dot(solve_one.T, solve_one, precision=HIGHEST)
    cross_new = -jnp.dot(solve_one.T, solve_two, precision=HIGHEST)
    bottom_new = bottom_two - jnp.dot(solve_two.T, solve_two, precision=HIGHEST)
    return (top_new, cross_new, bottom_new)


def contract_rows(left_cols, right_cols):
    return lax.dot_general(
        left_cols, right_cols, (((0,), (0,)), ((), ())), preferred_element_type=jnp.float32
    )


def local(coupling, row_scale, block_mask, link_map, tile_order, link_diag):
    local_slab = coupling[0]
    row_weights = row_scale[0]
    live_blocks = block_mask[0]
    block_map = link_map[0]
    diagonal = link_diag[0]
    slab_height = local_slab.shape[0]
    block_count = L // BLK
    my_index = lax.axis_index("row")
    block_ids = jnp.arange(block_count, dtype=jnp.int32)
    source = jnp.sum(
        block_ids[None, :] * (block_map[None, :] == block_ids[:, None]).astype(jnp.int32), axis=1
    )

    def edge_cols(global_block):
        local_block = source[global_block]
        cols = lax.dynamic_slice_in_dim(local_slab, local_block * BLK, BLK, axis=1)
        live = lax.dynamic_index_in_dim(live_blocks, local_block, 1, False)
        cols = (cols.reshape(slab_height // BLK, BLK, BLK) * live.astype(jnp.bfloat16)[:, None, None])
        cols = cols.reshape(slab_height, BLK)
        weighted = (row_weights[:, None] * cols.astype(jnp.float32)).astype(jnp.bfloat16)
        return cols, weighted

    first_cols, first_scaled = edge_cols(0)
    final_cols, final_scaled = edge_cols(block_count - 1)
    edge_gram = contract_rows(
        jnp.concatenate([first_cols, final_cols], axis=1),
        jnp.concatenate([first_scaled, final_scaled], axis=1),
    )
    part_pieces = jnp.stack(
        [edge_gram[:BLK, :BLK], edge_gram[:BLK, BLK:], edge_gram[BLK:, BLK:]]
    )
    owners = lax.axis_size("row")
    own_blocks = block_count // owners

    def exchange(value, step):
        return lax.ppermute(value, "row", [(src, src ^ step) for src in range(owners)])

    packed_side = jnp.concatenate([row_weights, live_blocks.reshape(-1).astype(jnp.float32)])
    side_slots = jnp.zeros((owners, packed_side.shape[0]), jnp.float32)
    side_slots = lax.dynamic_update_index_in_dim(side_slots, packed_side, my_index, 0)
    piece_count = part_pieces.size
    summed_all = jnp.concatenate([part_pieces.reshape(-1), side_slots.reshape(-1)])
    if owners == 4:
        summed_all = summed_all + exchange(summed_all, 1)
        summed_all = summed_all + exchange(summed_all, 2)
    else:
        summed_all = lax.psum(summed_all, "row")
    kernel_slab, summed_all = lax.optimization_barrier((local_slab, summed_all))
    summed = summed_all[:piece_count].reshape(part_pieces.shape)
    every_side = summed_all[piece_count:].reshape(side_slots.shape)
    eye = jnp.eye(BLK, dtype=jnp.float32)
    segment = jnp.stack([
        summed[0] + eye * diagonal[:BLK][None, :],
        summed[1],
        summed[2] + eye * diagonal[L - BLK :][None, :],
    ])

    if owners == 4:
        halves = 2
        half_rows = slab_height // halves
        across_halves = [
            exchange(lax.slice_in_dim(kernel_slab, h * half_rows, (h + 1) * half_rows), 2)
            for h in range(halves)
        ]
        across_side = lax.dynamic_index_in_dim(every_side, my_index ^ 2, 0, False)
        across_weights = across_side[:slab_height]
        across_live = across_side[slab_height:].reshape(live_blocks.shape).astype(jnp.int32)
        order = jnp.concatenate(
            [lax.dynamic_slice_in_dim(tile_order, (my_index ^ q) * own_blocks, own_blocks) for q in range(2)]
        )
        flags = (jnp.arange(2 * own_blocks) < own_blocks).astype(jnp.int32)
        left_src = jnp.take(source, order)

        def own_part(slab_in):
            return split_rows(
                slab_in, row_weights, live_blocks, left_src, source, order, diagonal, flags, own_blocks,
            )

        def across_part(slab_in, partial, half):
            rows = lax.slice_in_dim(across_weights, half * half_rows, (half + 1) * half_rows)
            live = lax.slice_in_dim(
                across_live, half * (half_rows // BLK), (half + 1) * (half_rows // BLK)
            )
            return split_rows(
                slab_in, rows, live, left_src, source, order, diagonal, flags, own_blocks, partial,
            )

        partner_side = lax.dynamic_index_in_dim(every_side, my_index ^ 3, 0, False)
        partner_weights = partner_side[:slab_height]
        partner_live = partner_side[slab_height:].reshape(live_blocks.shape).astype(jnp.int32)
        last_weights = jnp.concatenate([
            lax.slice_in_dim(across_weights, half_rows, slab_height),
            lax.slice_in_dim(partner_weights, half_rows, slab_height),
        ])
        last_live = jnp.concatenate([
            lax.slice_in_dim(across_live, half_rows // BLK, slab_height // BLK),
            lax.slice_in_dim(partner_live, half_rows // BLK, slab_height // BLK),
        ])
        mine_order = order[:own_blocks]

        def last_part(slab_one, slab_two, mine, received):
            total = pair_rows(
                slab_one, slab_two, last_weights, last_live, jnp.take(source, mine_order), source,
                mine_order, diagonal, flags[:own_blocks], own_blocks, mine[None], received[None],
            )
            return total[0]

        hooks = {1: ("own", kernel_slab), 2: ("across", across_halves[0]), 3: ("last", across_halves[1])}
    else:
        hooks = {}
        flags = jnp.full((block_count,), (my_index == 0).astype(jnp.int32))
        partial = gram_rows(
            kernel_slab, row_weights, live_blocks, jnp.take(source, tile_order), source,
            tile_order, diagonal, flags, own_blocks,
        )
        owned = lax.psum_scatter(
            partial.reshape(L, L), "row", scatter_dimension=0, tiled=True
        )

    times = lax.axis_size("tm")
    position = lax.axis_index("tm")
    running = (segment[0], segment[1], segment[2])
    shift = 1
    round_index = 0
    state = {}

    def run_hook(kind, slab_in, running):
        slab_in, running = lax.optimization_barrier((slab_in, running))
        if kind == "own":
            state["partial"] = own_part(slab_in)
        elif kind == "across":
            mine, partners = across_part(slab_in, state["partial"], 0)
            second, mine, partners = lax.optimization_barrier((across_halves[1], mine, partners))
            state["second"] = (second, exchange(second, 1))
            state["mine"] = mine
            state["received"] = exchange(partners, 1)
        else:
            state["owned"] = last_part(
                *state["second"], state["mine"], state["received"]
            )
        return running

    while shift < times:
        if round_index in hooks:
            running = run_hook(*hooks.pop(round_index), running)
        round_index += 1
        pairs = [(src, src + shift) for src in range(times - shift)]
        moved = lax.ppermute(jnp.stack(running), "tm", pairs)
        earlier = (moved[0], moved[1], moved[2])
        joined = join_segments(earlier, running)
        take = position >= shift
        running = tuple(jnp.where(take, new, old) for new, old in zip(joined, running))
        shift *= 2
    for key in sorted(hooks):
        running = run_hook(*hooks[key], running)
    if "owned" in state:
        owned = state["owned"]
    chain_out = jnp.stack(running)[None]
    return (owned[None], chain_out)


def solution(mesh):
    placed = (
        P("tm", "row", None),
        P("tm", "row"),
        P("tm", "row", None),
        P("tm", None),
        P(),
        P("tm", None),
    )
    return jax.shard_map(
        local,
        mesh=mesh,
        in_specs=placed,
        out_specs=(P("tm", "row", None), P("tm", None, None, None)),
        check_vma=False,
    )
```

```python
import functools

import jax
import jax.numpy as jnp
from jax import lax
from jax.sharding import PartitionSpec as P
from jax.experimental import pallas as pl
from jax.experimental.pallas import tpu as pltpu

L = 2048
BLK = 128


def gram_kernel(src_left, src_right, tile_ref, mask_ref, flag_ref, g_ref, w_ref, diag_ref, *rest):
    extra_ref = None
    if len(rest) == 5:
        acc_ref, extra_ref, out_ref, s_ref, lt_ref = rest
    elif len(rest) == 4:
        acc_ref, out_ref, s_ref, lt_ref = rest
    else:
        acc_ref = None
        out_ref, s_ref, lt_ref = rest
    k = pl.program_id(0)
    row_blocks = g_ref.shape[0] // BLK
    col_blocks = g_ref.shape[1] // BLK

    @pl.when(k == 0)
    def _():
        def fill(j, carry):
            src = src_right[j]
            c0 = pl.multiple_of(src * BLK, BLK)
            d0 = pl.multiple_of(j * BLK, BLK)
            for rb in range(row_blocks):
                live = mask_ref[rb * col_blocks + src].astype(jnp.float32)
                vals = g_ref[rb * BLK:(rb + 1) * BLK, pl.ds(c0, BLK)].astype(jnp.float32)
                wts = w_ref[rb * BLK:(rb + 1) * BLK, :]
                s_ref[rb * BLK:(rb + 1) * BLK, pl.ds(d0, BLK)] = (wts * (vals * live)).astype(jnp.bfloat16)
            return carry
        lax.fori_loop(0, col_blocks, fill, 0)

    src = src_left[k]
    c0 = pl.multiple_of(src * BLK, BLK)
    for rb in range(row_blocks):
        live = mask_ref[rb * col_blocks + src].astype(jnp.float32)
        vals = g_ref[rb * BLK:(rb + 1) * BLK, pl.ds(c0, BLK)].astype(jnp.float32) * live
        lt_ref[:, rb * BLK:(rb + 1) * BLK] = vals.T.astype(jnp.bfloat16)
    term = jnp.dot(lt_ref[...], s_ref[...], preferred_element_type=jnp.float32)
    if acc_ref is None:
        out_ref[...] = term
        blk = tile_ref[k]
        e0 = pl.multiple_of(blk * BLK, BLK)
        rows = lax.broadcasted_iota(jnp.int32, (BLK, BLK), 0)
        cols = lax.broadcasted_iota(jnp.int32, (BLK, BLK), 1)
        dvals = diag_ref[pl.ds(blk, 1), :] * flag_ref[k].astype(jnp.float32)
        out_ref[:, pl.ds(e0, BLK)] += jnp.where(rows == cols, dvals, 0.0)
    elif extra_ref is None:
        out_ref[...] = acc_ref[...] + term
    else:
        out_ref[...] = (acc_ref[...] + extra_ref[...]) + term


def gram_rows(slab, weights, live_blocks, src_left, src_right, out_tiles, diagonal, flags, group, acc=None,
              extra=None):
    height = slab.shape[0]
    col_blocks = L // BLK
    out_blocks = src_left.shape[0]
    in_specs = [
        pl.BlockSpec((height, L), lambda k, *_: (0, 0)),
        pl.BlockSpec((height, BLK), lambda k, *_: (0, 0)),
        pl.BlockSpec((col_blocks, BLK), lambda k, *_: (0, 0)),
    ]
    operands = [slab, jnp.broadcast_to(weights.reshape(height, 1), (height, BLK)), diagonal.reshape(col_blocks, BLK)]
    aliases = {}
    out_spec = pl.BlockSpec((None, BLK, L), lambda k, *_: (k // group, k % group, 0))
    if acc is not None:
        in_specs.append(out_spec)
        operands.append(acc)
        aliases = {8: 0}
    if extra is not None:
        in_specs.append(out_spec)
        operands.append(extra)
    grid_spec = pltpu.PrefetchScalarGridSpec(
        num_scalar_prefetch=5,
        grid=(out_blocks,),
        in_specs=in_specs,
        out_specs=out_spec,
        scratch_shapes=[pltpu.VMEM((height, L), jnp.bfloat16), pltpu.VMEM((BLK, height), jnp.bfloat16)],
    )
    return pl.pallas_call(
        gram_kernel,
        grid_spec=grid_spec,
        out_shape=jax.ShapeDtypeStruct((out_blocks // group, group * BLK, L), jnp.float32),
        input_output_aliases=aliases,
        compiler_params=pltpu.CompilerParams(vmem_limit_bytes=56 * 1024 * 1024),
    )(src_left, src_right, out_tiles, live_blocks.reshape(-1), flags, *operands)


def split_kernel(src_left, src_right, tile_ref, mask_ref, flag_ref, g_ref, w_ref, diag_ref, *rest,
                 group, accumulate):
    if accumulate:
        acc_first, acc_second, out_first, out_second, s_ref, lt_ref = rest
    else:
        acc_first = acc_second = None
        out_first, out_second, s_ref, lt_ref = rest
    k = pl.program_id(0)
    row_blocks = g_ref.shape[0] // BLK
    col_blocks = g_ref.shape[1] // BLK

    @pl.when(k == 0)
    def _():
        def fill(j, carry):
            src = src_right[j]
            c0 = pl.multiple_of(src * BLK, BLK)
            d0 = pl.multiple_of(j * BLK, BLK)
            for rb in range(row_blocks):
                live = mask_ref[rb * col_blocks + src].astype(jnp.float32)
                vals = g_ref[rb * BLK:(rb + 1) * BLK, pl.ds(c0, BLK)].astype(jnp.float32)
                wts = w_ref[rb * BLK:(rb + 1) * BLK, :]
                s_ref[rb * BLK:(rb + 1) * BLK, pl.ds(d0, BLK)] = (wts * (vals * live)).astype(jnp.bfloat16)
            return carry
        lax.fori_loop(0, col_blocks, fill, 0)

    src = src_left[k]
    c0 = pl.multiple_of(src * BLK, BLK)
    for rb in range(row_blocks):
        live = mask_ref[rb * col_blocks + src].astype(jnp.float32)
        vals = g_ref[rb * BLK:(rb + 1) * BLK, pl.ds(c0, BLK)].astype(jnp.float32) * live
        lt_ref[:, rb * BLK:(rb + 1) * BLK] = vals.T.astype(jnp.bfloat16)
    term = jnp.dot(lt_ref[...], s_ref[...], preferred_element_type=jnp.float32)

    def store(out_ref, acc_ref):
        if acc_ref is None:
            out_ref[...] = term
            blk = tile_ref[k]
            e0 = pl.multiple_of(blk * BLK, BLK)
            rows = lax.broadcasted_iota(jnp.int32, (BLK, BLK), 0)
            cols = lax.broadcasted_iota(jnp.int32, (BLK, BLK), 1)
            dvals = diag_ref[pl.ds(blk, 1), :] * flag_ref[k].astype(jnp.float32)
            out_ref[:, pl.ds(e0, BLK)] += jnp.where(rows == cols, dvals, 0.0)
        else:
            out_ref[...] = acc_ref[...] + term

    @pl.when(k < group)
    def _():
        store(out_first, acc_first)

    @pl.when(k >= group)
    def _():
        store(out_second, acc_second)


def split_rows(slab, weights, live_blocks, src_left, src_right, out_tiles, diagonal, flags, group,
               acc=None):
    height = slab.shape[0]
    col_blocks = L // BLK
    in_specs = [
        pl.BlockSpec((height, L), lambda k, *_: (0, 0)),
        pl.BlockSpec((height, BLK), lambda k, *_: (0, 0)),
        pl.BlockSpec((col_blocks, BLK), lambda k, *_: (0, 0)),
    ]
    operands = [slab, jnp.broadcast_to(weights.reshape(height, 1), (height, BLK)), diagonal.reshape(col_blocks, BLK)]
    first_spec = pl.BlockSpec((BLK, L), lambda k, *_: (jnp.minimum(k, group - 1), 0))
    second_spec = pl.BlockSpec((BLK, L), lambda k, *_: (jnp.maximum(k - group, 0), 0))
    aliases = {}
    if acc is not None:
        in_specs += [first_spec, second_spec]
        operands += list(acc)
        aliases = {8: 0, 9: 1}
    grid_spec = pltpu.PrefetchScalarGridSpec(
        num_scalar_prefetch=5,
        grid=(2 * group,),
        in_specs=in_specs,
        out_specs=[first_spec, second_spec],
        scratch_shapes=[pltpu.VMEM((height, L), jnp.bfloat16), pltpu.VMEM((BLK, height), jnp.bfloat16)],
    )
    shape = jax.ShapeDtypeStruct((group * BLK, L), jnp.float32)
    return pl.pallas_call(
        functools.partial(split_kernel, group=group, accumulate=acc is not None),
        grid_spec=grid_spec,
        out_shape=(shape, shape),
        input_output_aliases=aliases,
        compiler_params=pltpu.CompilerParams(vmem_limit_bytes=56 * 1024 * 1024),
    )(src_left, src_right, out_tiles, live_blocks.reshape(-1), flags, *operands)


def pair_kernel(src_left, src_right, tile_ref, mask_ref, flag_ref, g1_ref, g2_ref, w_ref, diag_ref,
                acc_ref, extra_ref, out_ref, s_ref, lt_ref):
    k = pl.program_id(0)
    first_blocks = g1_ref.shape[0] // BLK
    row_blocks = first_blocks + g2_ref.shape[0] // BLK
    col_blocks = g1_ref.shape[1] // BLK

    def rows_of(rb, cols):
        if rb < first_blocks:
            return g1_ref[rb * BLK:(rb + 1) * BLK, cols]
        return g2_ref[(rb - first_blocks) * BLK:(rb - first_blocks + 1) * BLK, cols]

    @pl.when(k == 0)
    def _():
        def fill(j, carry):
            src = src_right[j]
            c0 = pl.multiple_of(src * BLK, BLK)
            d0 = pl.multiple_of(j * BLK, BLK)
            for rb in range(row_blocks):
                live = mask_ref[rb * col_blocks + src].astype(jnp.float32)
                vals = rows_of(rb, pl.ds(c0, BLK)).astype(jnp.float32)
                wts = w_ref[rb * BLK:(rb + 1) * BLK, :]
                s_ref[rb * BLK:(rb + 1) * BLK, pl.ds(d0, BLK)] = (wts * (vals * live)).astype(jnp.bfloat16)
            return carry
        lax.fori_loop(0, col_blocks, fill, 0)

    src = src_left[k]
    c0 = pl.multiple_of(src * BLK, BLK)
    for rb in range(row_blocks):
        live = mask_ref[rb * col_blocks + src].astype(jnp.float32)
        vals = rows_of(rb, pl.ds(c0, BLK)).astype(jnp.float32) * live
        lt_ref[:, rb * BLK:(rb + 1) * BLK] = vals.T.astype(jnp.bfloat16)
    term = jnp.dot(lt_ref[...], s_ref[...], preferred_element_type=jnp.float32)
    out_ref[...] = (acc_ref[...] + extra_ref[...]) + term


def pair_rows(slab_one, slab_two, weights, live_blocks, src_left, src_right, out_tiles, diagonal, flags,
              group, acc, extra):
    height = slab_one.shape[0] + slab_two.shape[0]
    col_blocks = L // BLK
    out_blocks = src_left.shape[0]
    out_spec = pl.BlockSpec((None, BLK, L), lambda k, *_: (k // group, k % group, 0))
    grid_spec = pltpu.PrefetchScalarGridSpec(
        num_scalar_prefetch=5,
        grid=(out_blocks,),
        in_specs=[
            pl.BlockSpec(slab_one.shape, lambda k, *_: (0, 0)),
            pl.BlockSpec(slab_two.shape, lambda k, *_: (0, 0)),
            pl.BlockSpec((height, BLK), lambda k, *_: (0, 0)),
            pl.BlockSpec((col_blocks, BLK), lambda k, *_: (0, 0)),
            out_spec,
            out_spec,
        ],
        out_specs=out_spec,
        scratch_shapes=[pltpu.VMEM((height, L), jnp.bfloat16), pltpu.VMEM((BLK, height), jnp.bfloat16)],
    )
    return pl.pallas_call(
        pair_kernel,
        grid_spec=grid_spec,
        out_shape=jax.ShapeDtypeStruct((out_blocks // group, group * BLK, L), jnp.float32),
        input_output_aliases={9: 0},
        compiler_params=pltpu.CompilerParams(vmem_limit_bytes=56 * 1024 * 1024),
    )(src_left, src_right, out_tiles, live_blocks.reshape(-1), flags, slab_one, slab_two,
      jnp.broadcast_to(weights.reshape(height, 1), (height, BLK)), diagonal.reshape(col_blocks, BLK),
      acc, extra)


HIGHEST = lax.Precision.HIGHEST


def join_segments(earlier_seg, later_seg):
    top_one, cross_one, bottom_one = earlier_seg
    top_two, cross_two, bottom_two = later_seg
    middle = bottom_one + top_two
    middle = 0.5 * (middle + middle.T)
    factor = jnp.linalg.cholesky(middle)
    half_width = top_one.shape[0]
    solved = lax.linalg.triangular_solve(
        factor, jnp.concatenate([cross_one.T, cross_two], axis=1), left_side=True, lower=True
    )
    solve_one = solved[:, :half_width]
    solve_two = solved[:, half_width:]
    top_new = top_one - jnp.dot(solve_one.T, solve_one, precision=HIGHEST)
    cross_new = -jnp.dot(solve_one.T, solve_two, precision=HIGHEST)
    bottom_new = bottom_two - jnp.dot(solve_two.T, solve_two, precision=HIGHEST)
    return (top_new, cross_new, bottom_new)


def contract_rows(left_cols, right_cols):
    return lax.dot_general(
        left_cols, right_cols, (((0,), (0,)), ((), ())), preferred_element_type=jnp.float32
    )


def local(coupling, row_scale, block_mask, link_map, tile_order, link_diag):
    local_slab = coupling[0]
    row_weights = row_scale[0]
    live_blocks = block_mask[0]
    block_map = link_map[0]
    diagonal = link_diag[0]
    slab_height = local_slab.shape[0]
    block_count = L // BLK
    my_index = lax.axis_index("row")
    block_ids = jnp.arange(block_count, dtype=jnp.int32)
    source = jnp.sum(
        block_ids[None, :] * (block_map[None, :] == block_ids[:, None]).astype(jnp.int32), axis=1
    )

    def edge_cols(global_block):
        local_block = source[global_block]
        cols = lax.dynamic_slice_in_dim(local_slab, local_block * BLK, BLK, axis=1)
        live = lax.dynamic_index_in_dim(live_blocks, local_block, 1, False)
        cols = (cols.reshape(slab_height // BLK, BLK, BLK) * live.astype(jnp.bfloat16)[:, None, None])
        cols = cols.reshape(slab_height, BLK)
        weighted = (row_weights[:, None] * cols.astype(jnp.float32)).astype(jnp.bfloat16)
        return cols, weighted

    first_cols, first_scaled = edge_cols(0)
    final_cols, final_scaled = edge_cols(block_count - 1)
    edge_gram = contract_rows(
        jnp.concatenate([first_cols, final_cols], axis=1),
        jnp.concatenate([first_scaled, final_scaled], axis=1),
    )
    part_pieces = jnp.stack(
        [edge_gram[:BLK, :BLK], edge_gram[:BLK, BLK:], edge_gram[BLK:, BLK:]]
    )
    owners = lax.axis_size("row")
    own_blocks = block_count // owners

    def exchange(value, step):
        return lax.ppermute(value, "row", [(src, src ^ step) for src in range(owners)])

    packed_side = jnp.concatenate([row_weights, live_blocks.reshape(-1).astype(jnp.float32)])
    side_slots = jnp.zeros((owners, packed_side.shape[0]), jnp.float32)
    side_slots = lax.dynamic_update_index_in_dim(side_slots, packed_side, my_index, 0)
    piece_count = part_pieces.size
    summed_all = jnp.concatenate([part_pieces.reshape(-1), side_slots.reshape(-1)])
    if owners == 4:
        summed_all = summed_all + exchange(summed_all, 1)
        summed_all = summed_all + exchange(summed_all, 2)
    else:
        summed_all = lax.psum(summed_all, "row")
    kernel_slab, summed_all = lax.optimization_barrier((local_slab, summed_all))
    summed = summed_all[:piece_count].reshape(part_pieces.shape)
    every_side = summed_all[piece_count:].reshape(side_slots.shape)
    eye = jnp.eye(BLK, dtype=jnp.float32)
    segment = jnp.stack([
        summed[0] + eye * diagonal[:BLK][None, :],
        summed[1],
        summed[2] + eye * diagonal[L - BLK :][None, :],
    ])

    if owners == 4:
        halves = 2
        half_rows = slab_height // halves
        across_halves = [
            exchange(lax.slice_in_dim(kernel_slab, h * half_rows, (h + 1) * half_rows), 2)
            for h in range(halves)
        ]
        across_side = lax.dynamic_index_in_dim(every_side, my_index ^ 2, 0, False)
        across_weights = across_side[:slab_height]
        across_live = across_side[slab_height:].reshape(live_blocks.shape).astype(jnp.int32)
        order = jnp.concatenate(
            [lax.dynamic_slice_in_dim(tile_order, (my_index ^ q) * own_blocks, own_blocks) for q in range(2)]
        )
        flags = (jnp.arange(2 * own_blocks) < own_blocks).astype(jnp.int32)
        left_src = jnp.take(source, order)

        def own_part(slab_in):
            return split_rows(
                slab_in, row_weights, live_blocks, left_src, source, order, diagonal, flags, own_blocks,
            )

        def across_part(slab_in, partial, half):
            rows = lax.slice_in_dim(across_weights, half * half_rows, (half + 1) * half_rows)
            live = lax.slice_in_dim(
                across_live, half * (half_rows // BLK), (half + 1) * (half_rows // BLK)
            )
            return split_rows(
                slab_in, rows, live, left_src, source, order, diagonal, flags, own_blocks, partial,
            )

        partner_side = lax.dynamic_index_in_dim(every_side, my_index ^ 3, 0, False)
        partner_weights = partner_side[:slab_height]
        partner_live = partner_side[slab_height:].reshape(live_blocks.shape).astype(jnp.int32)
        last_weights = jnp.concatenate([
            lax.slice_in_dim(across_weights, half_rows, slab_height),
            lax.slice_in_dim(partner_weights, half_rows, slab_height),
        ])
        last_live = jnp.concatenate([
            lax.slice_in_dim(across_live, half_rows // BLK, slab_height // BLK),
            lax.slice_in_dim(partner_live, half_rows // BLK, slab_height // BLK),
        ])
        mine_order = order[:own_blocks]

        def last_part(slab_one, slab_two, mine, received):
            total = pair_rows(
                slab_one, slab_two, last_weights, last_live, jnp.take(source, mine_order), source,
                mine_order, diagonal, flags[:own_blocks], own_blocks, mine[None], received[None],
            )
            return total[0]

        hooks = {2: ("across", across_halves[0]), 3: ("last", across_halves[1])}
        early_partial = own_part(local_slab)
    else:
        hooks = {}
        flags = jnp.full((block_count,), (my_index == 0).astype(jnp.int32))
        partial = gram_rows(
            kernel_slab, row_weights, live_blocks, jnp.take(source, tile_order), source,
            tile_order, diagonal, flags, own_blocks,
        )
        owned = lax.psum_scatter(
            partial.reshape(L, L), "row", scatter_dimension=0, tiled=True
        )

    times = lax.axis_size("tm")
    position = lax.axis_index("tm")
    running = (segment[0], segment[1], segment[2])
    shift = 1
    round_index = 0
    state = {}
    if owners == 4:
        state["partial"] = early_partial

    def run_hook(kind, slab_in, running):
        slab_in, running = lax.optimization_barrier((slab_in, running))
        if kind == "own":
            state["partial"] = own_part(slab_in)
        elif kind == "across":
            mine, partners = across_part(slab_in, state["partial"], 0)
            state["mine"] = mine
            state["received"] = exchange(partners, 1)
        else:
            state["owned"] = last_part(
                slab_in, exchange(slab_in, 1), state["mine"], state["received"]
            )
        return running

    while shift < times:
        if round_index in hooks:
            running = run_hook(*hooks.pop(round_index), running)
        round_index += 1
        pairs = [(src, src + shift) for src in range(times - shift)]
        moved = lax.ppermute(jnp.stack(running), "tm", pairs)
        earlier = (moved[0], moved[1], moved[2])
        joined = join_segments(earlier, running)
        take = position >= shift
        running = tuple(jnp.where(take, new, old) for new, old in zip(joined, running))
        shift *= 2
    for key in sorted(hooks):
        running = run_hook(*hooks[key], running)
    if "owned" in state:
        owned = state["owned"]
    chain_out = jnp.stack(running)[None]
    return (owned[None], chain_out)


def solution(mesh):
    placed = (
        P("tm", "row", None),
        P("tm", "row"),
        P("tm", "row", None),
        P("tm", None),
        P(),
        P("tm", None),
    )
    return jax.shard_map(
        local,
        mesh=mesh,
        in_specs=placed,
        out_specs=(P("tm", "row", None), P("tm", None, None, None)),
        check_vma=False,
    )
```

```python
import functools

import jax
import jax.numpy as jnp
from jax import lax
from jax.sharding import PartitionSpec as P
from jax.experimental import pallas as pl
from jax.experimental.pallas import tpu as pltpu

L = 2048
BLK = 128


def gram_kernel(src_left, src_right, tile_ref, mask_ref, flag_ref, g_ref, w_ref, diag_ref, *rest):
    extra_ref = None
    if len(rest) == 5:
        acc_ref, extra_ref, out_ref, s_ref, lt_ref = rest
    elif len(rest) == 4:
        acc_ref, out_ref, s_ref, lt_ref = rest
    else:
        acc_ref = None
        out_ref, s_ref, lt_ref = rest
    k = pl.program_id(0)
    row_blocks = g_ref.shape[0] // BLK
    col_blocks = g_ref.shape[1] // BLK

    @pl.when(k == 0)
    def _():
        def fill(j, carry):
            src = src_right[j]
            c0 = pl.multiple_of(src * BLK, BLK)
            d0 = pl.multiple_of(j * BLK, BLK)
            for rb in range(row_blocks):
                live = mask_ref[rb * col_blocks + src].astype(jnp.float32)
                vals = g_ref[rb * BLK:(rb + 1) * BLK, pl.ds(c0, BLK)].astype(jnp.float32)
                wts = w_ref[rb * BLK:(rb + 1) * BLK, :]
                s_ref[rb * BLK:(rb + 1) * BLK, pl.ds(d0, BLK)] = (wts * (vals * live)).astype(jnp.bfloat16)
            return carry
        lax.fori_loop(0, col_blocks, fill, 0)

    src = src_left[k]
    c0 = pl.multiple_of(src * BLK, BLK)
    for rb in range(row_blocks):
        live = mask_ref[rb * col_blocks + src].astype(jnp.float32)
        vals = g_ref[rb * BLK:(rb + 1) * BLK, pl.ds(c0, BLK)].astype(jnp.float32) * live
        lt_ref[:, rb * BLK:(rb + 1) * BLK] = vals.T.astype(jnp.bfloat16)
    term = jnp.dot(lt_ref[...], s_ref[...], preferred_element_type=jnp.float32)
    if acc_ref is None:
        out_ref[...] = term
        blk = tile_ref[k]
        e0 = pl.multiple_of(blk * BLK, BLK)
        rows = lax.broadcasted_iota(jnp.int32, (BLK, BLK), 0)
        cols = lax.broadcasted_iota(jnp.int32, (BLK, BLK), 1)
        dvals = diag_ref[pl.ds(blk, 1), :] * flag_ref[k].astype(jnp.float32)
        out_ref[:, pl.ds(e0, BLK)] += jnp.where(rows == cols, dvals, 0.0)
    elif extra_ref is None:
        out_ref[...] = acc_ref[...] + term
    else:
        out_ref[...] = (acc_ref[...] + extra_ref[...]) + term


def gram_rows(slab, weights, live_blocks, src_left, src_right, out_tiles, diagonal, flags, group, acc=None,
              extra=None):
    height = slab.shape[0]
    col_blocks = L // BLK
    out_blocks = src_left.shape[0]
    in_specs = [
        pl.BlockSpec((height, L), lambda k, *_: (0, 0)),
        pl.BlockSpec((height, BLK), lambda k, *_: (0, 0)),
        pl.BlockSpec((col_blocks, BLK), lambda k, *_: (0, 0)),
    ]
    operands = [slab, jnp.broadcast_to(weights.reshape(height, 1), (height, BLK)), diagonal.reshape(col_blocks, BLK)]
    aliases = {}
    out_spec = pl.BlockSpec((None, BLK, L), lambda k, *_: (k // group, k % group, 0))
    if acc is not None:
        in_specs.append(out_spec)
        operands.append(acc)
        aliases = {8: 0}
    if extra is not None:
        in_specs.append(out_spec)
        operands.append(extra)
    grid_spec = pltpu.PrefetchScalarGridSpec(
        num_scalar_prefetch=5,
        grid=(out_blocks,),
        in_specs=in_specs,
        out_specs=out_spec,
        scratch_shapes=[pltpu.VMEM((height, L), jnp.bfloat16), pltpu.VMEM((BLK, height), jnp.bfloat16)],
    )
    return pl.pallas_call(
        gram_kernel,
        grid_spec=grid_spec,
        out_shape=jax.ShapeDtypeStruct((out_blocks // group, group * BLK, L), jnp.float32),
        input_output_aliases=aliases,
        compiler_params=pltpu.CompilerParams(vmem_limit_bytes=56 * 1024 * 1024),
    )(src_left, src_right, out_tiles, live_blocks.reshape(-1), flags, *operands)


def split_kernel(src_left, src_right, tile_ref, mask_ref, flag_ref, g_ref, w_ref, diag_ref, *rest,
                 group, accumulate):
    if accumulate:
        acc_first, acc_second, out_first, out_second, s_ref, lt_ref = rest
    else:
        acc_first = acc_second = None
        out_first, out_second, s_ref, lt_ref = rest
    k = pl.program_id(0)
    row_blocks = g_ref.shape[0] // BLK
    col_blocks = g_ref.shape[1] // BLK

    @pl.when(k == 0)
    def _():
        def fill(j, carry):
            src = src_right[j]
            c0 = pl.multiple_of(src * BLK, BLK)
            d0 = pl.multiple_of(j * BLK, BLK)
            for rb in range(row_blocks):
                live = mask_ref[rb * col_blocks + src].astype(jnp.float32)
                vals = g_ref[rb * BLK:(rb + 1) * BLK, pl.ds(c0, BLK)].astype(jnp.float32)
                wts = w_ref[rb * BLK:(rb + 1) * BLK, :]
                s_ref[rb * BLK:(rb + 1) * BLK, pl.ds(d0, BLK)] = (wts * (vals * live)).astype(jnp.bfloat16)
            return carry
        lax.fori_loop(0, col_blocks, fill, 0)

    src = src_left[k]
    c0 = pl.multiple_of(src * BLK, BLK)
    for rb in range(row_blocks):
        live = mask_ref[rb * col_blocks + src].astype(jnp.float32)
        vals = g_ref[rb * BLK:(rb + 1) * BLK, pl.ds(c0, BLK)].astype(jnp.float32) * live
        lt_ref[:, rb * BLK:(rb + 1) * BLK] = vals.T.astype(jnp.bfloat16)
    term = jnp.dot(lt_ref[...], s_ref[...], preferred_element_type=jnp.float32)

    def store(out_ref, acc_ref):
        if acc_ref is None:
            out_ref[...] = term
            blk = tile_ref[k]
            e0 = pl.multiple_of(blk * BLK, BLK)
            rows = lax.broadcasted_iota(jnp.int32, (BLK, BLK), 0)
            cols = lax.broadcasted_iota(jnp.int32, (BLK, BLK), 1)
            dvals = diag_ref[pl.ds(blk, 1), :] * flag_ref[k].astype(jnp.float32)
            out_ref[:, pl.ds(e0, BLK)] += jnp.where(rows == cols, dvals, 0.0)
        else:
            out_ref[...] = acc_ref[...] + term

    @pl.when(k < group)
    def _():
        store(out_first, acc_first)

    @pl.when(k >= group)
    def _():
        store(out_second, acc_second)


def split_rows(slab, weights, live_blocks, src_left, src_right, out_tiles, diagonal, flags, group,
               acc=None):
    height = slab.shape[0]
    col_blocks = L // BLK
    in_specs = [
        pl.BlockSpec((height, L), lambda k, *_: (0, 0)),
        pl.BlockSpec((height, BLK), lambda k, *_: (0, 0)),
        pl.BlockSpec((col_blocks, BLK), lambda k, *_: (0, 0)),
    ]
    operands = [slab, jnp.broadcast_to(weights.reshape(height, 1), (height, BLK)), diagonal.reshape(col_blocks, BLK)]
    first_spec = pl.BlockSpec((BLK, L), lambda k, *_: (jnp.minimum(k, group - 1), 0))
    second_spec = pl.BlockSpec((BLK, L), lambda k, *_: (jnp.maximum(k - group, 0), 0))
    aliases = {}
    if acc is not None:
        in_specs += [first_spec, second_spec]
        operands += list(acc)
        aliases = {8: 0, 9: 1}
    grid_spec = pltpu.PrefetchScalarGridSpec(
        num_scalar_prefetch=5,
        grid=(2 * group,),
        in_specs=in_specs,
        out_specs=[first_spec, second_spec],
        scratch_shapes=[pltpu.VMEM((height, L), jnp.bfloat16), pltpu.VMEM((BLK, height), jnp.bfloat16)],
    )
    shape = jax.ShapeDtypeStruct((group * BLK, L), jnp.float32)
    return pl.pallas_call(
        functools.partial(split_kernel, group=group, accumulate=acc is not None),
        grid_spec=grid_spec,
        out_shape=(shape, shape),
        input_output_aliases=aliases,
        compiler_params=pltpu.CompilerParams(vmem_limit_bytes=56 * 1024 * 1024),
    )(src_left, src_right, out_tiles, live_blocks.reshape(-1), flags, *operands)


def pair_kernel(src_left, src_right, tile_ref, mask_ref, flag_ref, g1_ref, g2_ref, w_ref, diag_ref,
                acc_ref, extra_ref, out_ref, s_ref, lt_ref):
    k = pl.program_id(0)
    first_blocks = g1_ref.shape[0] // BLK
    row_blocks = first_blocks + g2_ref.shape[0] // BLK
    col_blocks = g1_ref.shape[1] // BLK

    def rows_of(rb, cols):
        if rb < first_blocks:
            return g1_ref[rb * BLK:(rb + 1) * BLK, cols]
        return g2_ref[(rb - first_blocks) * BLK:(rb - first_blocks + 1) * BLK, cols]

    @pl.when(k == 0)
    def _():
        def fill(j, carry):
            src = src_right[j]
            c0 = pl.multiple_of(src * BLK, BLK)
            d0 = pl.multiple_of(j * BLK, BLK)
            for rb in range(row_blocks):
                live = mask_ref[rb * col_blocks + src].astype(jnp.float32)
                vals = rows_of(rb, pl.ds(c0, BLK)).astype(jnp.float32)
                wts = w_ref[rb * BLK:(rb + 1) * BLK, :]
                s_ref[rb * BLK:(rb + 1) * BLK, pl.ds(d0, BLK)] = (wts * (vals * live)).astype(jnp.bfloat16)
            return carry
        lax.fori_loop(0, col_blocks, fill, 0)

    src = src_left[k]
    c0 = pl.multiple_of(src * BLK, BLK)
    for rb in range(row_blocks):
        live = mask_ref[rb * col_blocks + src].astype(jnp.float32)
        vals = rows_of(rb, pl.ds(c0, BLK)).astype(jnp.float32) * live
        lt_ref[:, rb * BLK:(rb + 1) * BLK] = vals.T.astype(jnp.bfloat16)
    term = jnp.dot(lt_ref[...], s_ref[...], preferred_element_type=jnp.float32)
    out_ref[...] = (acc_ref[...] + extra_ref[...]) + term


def pair_rows(slab_one, slab_two, weights, live_blocks, src_left, src_right, out_tiles, diagonal, flags,
              group, acc, extra):
    height = slab_one.shape[0] + slab_two.shape[0]
    col_blocks = L // BLK
    out_blocks = src_left.shape[0]
    out_spec = pl.BlockSpec((None, BLK, L), lambda k, *_: (k // group, k % group, 0))
    grid_spec = pltpu.PrefetchScalarGridSpec(
        num_scalar_prefetch=5,
        grid=(out_blocks,),
        in_specs=[
            pl.BlockSpec(slab_one.shape, lambda k, *_: (0, 0)),
            pl.BlockSpec(slab_two.shape, lambda k, *_: (0, 0)),
            pl.BlockSpec((height, BLK), lambda k, *_: (0, 0)),
            pl.BlockSpec((col_blocks, BLK), lambda k, *_: (0, 0)),
            out_spec,
            out_spec,
        ],
        out_specs=out_spec,
        scratch_shapes=[pltpu.VMEM((height, L), jnp.bfloat16), pltpu.VMEM((BLK, height), jnp.bfloat16)],
    )
    return pl.pallas_call(
        pair_kernel,
        grid_spec=grid_spec,
        out_shape=jax.ShapeDtypeStruct((out_blocks // group, group * BLK, L), jnp.float32),
        input_output_aliases={9: 0},
        compiler_params=pltpu.CompilerParams(vmem_limit_bytes=56 * 1024 * 1024),
    )(src_left, src_right, out_tiles, live_blocks.reshape(-1), flags, slab_one, slab_two,
      jnp.broadcast_to(weights.reshape(height, 1), (height, BLK)), diagonal.reshape(col_blocks, BLK),
      acc, extra)


HIGHEST = lax.Precision.HIGHEST


def join_segments(earlier_seg, later_seg):
    top_one, cross_one, bottom_one = earlier_seg
    top_two, cross_two, bottom_two = later_seg
    middle = bottom_one + top_two
    middle = 0.5 * (middle + middle.T)
    factor = jnp.linalg.cholesky(middle)
    half_width = top_one.shape[0]
    solved = lax.linalg.triangular_solve(
        factor, jnp.concatenate([cross_one.T, cross_two], axis=1), left_side=True, lower=True
    )
    solve_one = solved[:, :half_width]
    solve_two = solved[:, half_width:]
    top_new = top_one - jnp.dot(solve_one.T, solve_one, precision=HIGHEST)
    cross_new = -jnp.dot(solve_one.T, solve_two, precision=HIGHEST)
    bottom_new = bottom_two - jnp.dot(solve_two.T, solve_two, precision=HIGHEST)
    return (top_new, cross_new, bottom_new)


def contract_rows(left_cols, right_cols):
    return lax.dot_general(
        left_cols, right_cols, (((0,), (0,)), ((), ())), preferred_element_type=jnp.float32
    )


def local(coupling, row_scale, block_mask, link_map, tile_order, link_diag):
    local_slab = coupling[0]
    row_weights = row_scale[0]
    live_blocks = block_mask[0]
    block_map = link_map[0]
    diagonal = link_diag[0]
    slab_height = local_slab.shape[0]
    block_count = L // BLK
    my_index = lax.axis_index("row")
    block_ids = jnp.arange(block_count, dtype=jnp.int32)
    source = jnp.sum(
        block_ids[None, :] * (block_map[None, :] == block_ids[:, None]).astype(jnp.int32), axis=1
    )

    def edge_cols(global_block):
        local_block = source[global_block]
        cols = lax.dynamic_slice_in_dim(local_slab, local_block * BLK, BLK, axis=1)
        live = lax.dynamic_index_in_dim(live_blocks, local_block, 1, False)
        cols = (cols.reshape(slab_height // BLK, BLK, BLK) * live.astype(jnp.bfloat16)[:, None, None])
        cols = cols.reshape(slab_height, BLK)
        weighted = (row_weights[:, None] * cols.astype(jnp.float32)).astype(jnp.bfloat16)
        return cols, weighted

    first_cols, first_scaled = edge_cols(0)
    final_cols, final_scaled = edge_cols(block_count - 1)
    edge_gram = contract_rows(
        jnp.concatenate([first_cols, final_cols], axis=1),
        jnp.concatenate([first_scaled, final_scaled], axis=1),
    )
    part_pieces = jnp.stack(
        [edge_gram[:BLK, :BLK], edge_gram[:BLK, BLK:], edge_gram[BLK:, BLK:]]
    )
    owners = lax.axis_size("row")
    own_blocks = block_count // owners

    def exchange(value, step):
        return lax.ppermute(value, "row", [(src, src ^ step) for src in range(owners)])

    packed_side = jnp.concatenate([row_weights, live_blocks.reshape(-1).astype(jnp.float32)])
    side_slots = jnp.zeros((owners, packed_side.shape[0]), jnp.float32)
    side_slots = lax.dynamic_update_index_in_dim(side_slots, packed_side, my_index, 0)
    piece_count = part_pieces.size
    summed_all = jnp.concatenate([part_pieces.reshape(-1), side_slots.reshape(-1)])
    if owners == 4:
        summed_all = summed_all + exchange(summed_all, 2)
        summed_all = summed_all + exchange(summed_all, 1)
    else:
        summed_all = lax.psum(summed_all, "row")
    kernel_slab, summed_all = lax.optimization_barrier((local_slab, summed_all))
    summed = summed_all[:piece_count].reshape(part_pieces.shape)
    every_side = summed_all[piece_count:].reshape(side_slots.shape)
    eye = jnp.eye(BLK, dtype=jnp.float32)
    segment = jnp.stack([
        summed[0] + eye * diagonal[:BLK][None, :],
        summed[1],
        summed[2] + eye * diagonal[L - BLK :][None, :],
    ])

    if owners == 4:
        halves = 2
        half_rows = slab_height // halves
        across_halves = [
            exchange(lax.slice_in_dim(kernel_slab, h * half_rows, (h + 1) * half_rows), 2)
            for h in range(halves)
        ]
        across_side = lax.dynamic_index_in_dim(every_side, my_index ^ 2, 0, False)
        across_weights = across_side[:slab_height]
        across_live = across_side[slab_height:].reshape(live_blocks.shape).astype(jnp.int32)
        order = jnp.concatenate(
            [lax.dynamic_slice_in_dim(tile_order, (my_index ^ q) * own_blocks, own_blocks) for q in range(2)]
        )
        flags = (jnp.arange(2 * own_blocks) < own_blocks).astype(jnp.int32)
        left_src = jnp.take(source, order)

        def own_part(slab_in):
            return split_rows(
                slab_in, row_weights, live_blocks, left_src, source, order, diagonal, flags, own_blocks,
            )

        def across_part(slab_in, partial, half):
            rows = lax.slice_in_dim(across_weights, half * half_rows, (half + 1) * half_rows)
            live = lax.slice_in_dim(
                across_live, half * (half_rows // BLK), (half + 1) * (half_rows // BLK)
            )
            return split_rows(
                slab_in, rows, live, left_src, source, order, diagonal, flags, own_blocks, partial,
            )

        partner_side = lax.dynamic_index_in_dim(every_side, my_index ^ 3, 0, False)
        partner_weights = partner_side[:slab_height]
        partner_live = partner_side[slab_height:].reshape(live_blocks.shape).astype(jnp.int32)
        last_weights = jnp.concatenate([
            lax.slice_in_dim(across_weights, half_rows, slab_height),
            lax.slice_in_dim(partner_weights, half_rows, slab_height),
        ])
        last_live = jnp.concatenate([
            lax.slice_in_dim(across_live, half_rows // BLK, slab_height // BLK),
            lax.slice_in_dim(partner_live, half_rows // BLK, slab_height // BLK),
        ])
        mine_order = order[:own_blocks]

        def last_part(slab_one, slab_two, mine, received):
            total = pair_rows(
                slab_one, slab_two, last_weights, last_live, jnp.take(source, mine_order), source,
                mine_order, diagonal, flags[:own_blocks], own_blocks, mine[None], received[None],
            )
            return total[0]

        hooks = {2: ("across", across_halves[0]), 3: ("last", across_halves[1])}
        early_partial = own_part(local_slab)
    else:
        hooks = {}
        flags = jnp.full((block_count,), (my_index == 0).astype(jnp.int32))
        partial = gram_rows(
            kernel_slab, row_weights, live_blocks, jnp.take(source, tile_order), source,
            tile_order, diagonal, flags, own_blocks,
        )
        owned = lax.psum_scatter(
            partial.reshape(L, L), "row", scatter_dimension=0, tiled=True
        )

    times = lax.axis_size("tm")
    position = lax.axis_index("tm")
    running = (segment[0], segment[1], segment[2])
    shift = 1
    round_index = 0
    state = {}
    if owners == 4:
        state["partial"] = early_partial

    def run_hook(kind, slab_in, running):
        slab_in, running = lax.optimization_barrier((slab_in, running))
        if kind == "own":
            state["partial"] = own_part(slab_in)
        elif kind == "across":
            mine, partners = across_part(slab_in, state["partial"], 0)
            state["mine"] = mine
            state["received"] = exchange(partners, 1)
        else:
            state["owned"] = last_part(
                slab_in, exchange(slab_in, 1), state["mine"], state["received"]
            )
        return running

    while shift < times:
        if round_index in hooks:
            running = run_hook(*hooks.pop(round_index), running)
        round_index += 1
        pairs = [(src, src + shift) for src in range(times - shift)]
        moved = lax.ppermute(jnp.stack(running), "tm", pairs)
        earlier = (moved[0], moved[1], moved[2])
        joined = join_segments(earlier, running)
        take = position >= shift
        running = tuple(jnp.where(take, new, old) for new, old in zip(joined, running))
        shift *= 2
    for key in sorted(hooks):
        running = run_hook(*hooks[key], running)
    if "owned" in state:
        owned = state["owned"]
    chain_out = jnp.stack(running)[None]
    return (owned[None], chain_out)


def solution(mesh):
    placed = (
        P("tm", "row", None),
        P("tm", "row"),
        P("tm", "row", None),
        P("tm", None),
        P(),
        P("tm", None),
    )
    return jax.shard_map(
        local,
        mesh=mesh,
        in_specs=placed,
        out_specs=(P("tm", "row", None), P("tm", None, None, None)),
        check_vma=False,
    )
```

```python
import functools

import jax
import jax.numpy as jnp
from jax import lax
from jax.sharding import PartitionSpec as P
from jax.experimental import pallas as pl
from jax.experimental.pallas import tpu as pltpu

L = 2048
BLK = 128


def gram_kernel(src_left, src_right, tile_ref, mask_ref, flag_ref, g_ref, w_ref, diag_ref, *rest):
    extra_ref = None
    if len(rest) == 5:
        acc_ref, extra_ref, out_ref, s_ref, lt_ref = rest
    elif len(rest) == 4:
        acc_ref, out_ref, s_ref, lt_ref = rest
    else:
        acc_ref = None
        out_ref, s_ref, lt_ref = rest
    k = pl.program_id(0)
    row_blocks = g_ref.shape[0] // BLK
    col_blocks = g_ref.shape[1] // BLK

    @pl.when(k == 0)
    def _():
        def fill(j, carry):
            src = src_right[j]
            c0 = pl.multiple_of(src * BLK, BLK)
            d0 = pl.multiple_of(j * BLK, BLK)
            for rb in range(row_blocks):
                live = mask_ref[rb * col_blocks + src].astype(jnp.float32)
                vals = g_ref[rb * BLK:(rb + 1) * BLK, pl.ds(c0, BLK)].astype(jnp.float32)
                wts = w_ref[rb * BLK:(rb + 1) * BLK, :]
                s_ref[rb * BLK:(rb + 1) * BLK, pl.ds(d0, BLK)] = (wts * (vals * live)).astype(jnp.bfloat16)
            return carry
        lax.fori_loop(0, col_blocks, fill, 0)

    src = src_left[k]
    c0 = pl.multiple_of(src * BLK, BLK)
    for rb in range(row_blocks):
        live = mask_ref[rb * col_blocks + src].astype(jnp.float32)
        vals = g_ref[rb * BLK:(rb + 1) * BLK, pl.ds(c0, BLK)].astype(jnp.float32) * live
        lt_ref[:, rb * BLK:(rb + 1) * BLK] = vals.T.astype(jnp.bfloat16)
    term = jnp.dot(lt_ref[...], s_ref[...], preferred_element_type=jnp.float32)
    if acc_ref is None:
        out_ref[...] = term
        blk = tile_ref[k]
        e0 = pl.multiple_of(blk * BLK, BLK)
        rows = lax.broadcasted_iota(jnp.int32, (BLK, BLK), 0)
        cols = lax.broadcasted_iota(jnp.int32, (BLK, BLK), 1)
        dvals = diag_ref[pl.ds(blk, 1), :] * flag_ref[k].astype(jnp.float32)
        out_ref[:, pl.ds(e0, BLK)] += jnp.where(rows == cols, dvals, 0.0)
    elif extra_ref is None:
        out_ref[...] = acc_ref[...] + term
    else:
        out_ref[...] = (acc_ref[...] + extra_ref[...]) + term


def gram_rows(slab, weights, live_blocks, src_left, src_right, out_tiles, diagonal, flags, group, acc=None,
              extra=None):
    height = slab.shape[0]
    col_blocks = L // BLK
    out_blocks = src_left.shape[0]
    in_specs = [
        pl.BlockSpec((height, L), lambda k, *_: (0, 0)),
        pl.BlockSpec((height, BLK), lambda k, *_: (0, 0)),
        pl.BlockSpec((col_blocks, BLK), lambda k, *_: (0, 0)),
    ]
    operands = [slab, jnp.broadcast_to(weights.reshape(height, 1), (height, BLK)), diagonal.reshape(col_blocks, BLK)]
    aliases = {}
    out_spec = pl.BlockSpec((None, BLK, L), lambda k, *_: (k // group, k % group, 0))
    if acc is not None:
        in_specs.append(out_spec)
        operands.append(acc)
        aliases = {8: 0}
    if extra is not None:
        in_specs.append(out_spec)
        operands.append(extra)
    grid_spec = pltpu.PrefetchScalarGridSpec(
        num_scalar_prefetch=5,
        grid=(out_blocks,),
        in_specs=in_specs,
        out_specs=out_spec,
        scratch_shapes=[pltpu.VMEM((height, L), jnp.bfloat16), pltpu.VMEM((BLK, height), jnp.bfloat16)],
    )
    return pl.pallas_call(
        gram_kernel,
        grid_spec=grid_spec,
        out_shape=jax.ShapeDtypeStruct((out_blocks // group, group * BLK, L), jnp.float32),
        input_output_aliases=aliases,
        compiler_params=pltpu.CompilerParams(vmem_limit_bytes=56 * 1024 * 1024),
    )(src_left, src_right, out_tiles, live_blocks.reshape(-1), flags, *operands)


def split_kernel(src_left, src_right, tile_ref, mask_ref, flag_ref, g_ref, w_ref, diag_ref, *rest,
                 group, accumulate):
    if accumulate:
        acc_first, acc_second, out_first, out_second, s_ref, lt_ref = rest
    else:
        acc_first = acc_second = None
        out_first, out_second, s_ref, lt_ref = rest
    k = pl.program_id(0)
    row_blocks = g_ref.shape[0] // BLK
    col_blocks = g_ref.shape[1] // BLK

    @pl.when(k == 0)
    def _():
        def fill(j, carry):
            src = src_right[j]
            c0 = pl.multiple_of(src * BLK, BLK)
            d0 = pl.multiple_of(j * BLK, BLK)
            for rb in range(row_blocks):
                live = mask_ref[rb * col_blocks + src].astype(jnp.float32)
                vals = g_ref[rb * BLK:(rb + 1) * BLK, pl.ds(c0, BLK)].astype(jnp.float32)
                wts = w_ref[rb * BLK:(rb + 1) * BLK, :]
                s_ref[rb * BLK:(rb + 1) * BLK, pl.ds(d0, BLK)] = (wts * (vals * live)).astype(jnp.bfloat16)
            return carry
        lax.fori_loop(0, col_blocks, fill, 0)

    src = src_left[k]
    c0 = pl.multiple_of(src * BLK, BLK)
    for rb in range(row_blocks):
        live = mask_ref[rb * col_blocks + src].astype(jnp.float32)
        vals = g_ref[rb * BLK:(rb + 1) * BLK, pl.ds(c0, BLK)].astype(jnp.float32) * live
        lt_ref[:, rb * BLK:(rb + 1) * BLK] = vals.T.astype(jnp.bfloat16)
    term = jnp.dot(lt_ref[...], s_ref[...], preferred_element_type=jnp.float32)

    def store(out_ref, acc_ref):
        if acc_ref is None:
            out_ref[...] = term
            blk = tile_ref[k]
            e0 = pl.multiple_of(blk * BLK, BLK)
            rows = lax.broadcasted_iota(jnp.int32, (BLK, BLK), 0)
            cols = lax.broadcasted_iota(jnp.int32, (BLK, BLK), 1)
            dvals = diag_ref[pl.ds(blk, 1), :] * flag_ref[k].astype(jnp.float32)
            out_ref[:, pl.ds(e0, BLK)] += jnp.where(rows == cols, dvals, 0.0)
        else:
            out_ref[...] = acc_ref[...] + term

    @pl.when(k < group)
    def _():
        store(out_first, acc_first)

    @pl.when(k >= group)
    def _():
        store(out_second, acc_second)


def split_rows(slab, weights, live_blocks, src_left, src_right, out_tiles, diagonal, flags, group,
               acc=None):
    height = slab.shape[0]
    col_blocks = L // BLK
    in_specs = [
        pl.BlockSpec((height, L), lambda k, *_: (0, 0)),
        pl.BlockSpec((height, BLK), lambda k, *_: (0, 0)),
        pl.BlockSpec((col_blocks, BLK), lambda k, *_: (0, 0)),
    ]
    operands = [slab, jnp.broadcast_to(weights.reshape(height, 1), (height, BLK)), diagonal.reshape(col_blocks, BLK)]
    first_spec = pl.BlockSpec((BLK, L), lambda k, *_: (jnp.minimum(k, group - 1), 0))
    second_spec = pl.BlockSpec((BLK, L), lambda k, *_: (jnp.maximum(k - group, 0), 0))
    aliases = {}
    if acc is not None:
        in_specs += [first_spec, second_spec]
        operands += list(acc)
        aliases = {8: 0, 9: 1}
    grid_spec = pltpu.PrefetchScalarGridSpec(
        num_scalar_prefetch=5,
        grid=(2 * group,),
        in_specs=in_specs,
        out_specs=[first_spec, second_spec],
        scratch_shapes=[pltpu.VMEM((height, L), jnp.bfloat16), pltpu.VMEM((BLK, height), jnp.bfloat16)],
    )
    shape = jax.ShapeDtypeStruct((group * BLK, L), jnp.float32)
    return pl.pallas_call(
        functools.partial(split_kernel, group=group, accumulate=acc is not None),
        grid_spec=grid_spec,
        out_shape=(shape, shape),
        input_output_aliases=aliases,
        compiler_params=pltpu.CompilerParams(vmem_limit_bytes=56 * 1024 * 1024),
    )(src_left, src_right, out_tiles, live_blocks.reshape(-1), flags, *operands)


def pair_kernel(src_left, src_right, tile_ref, mask_ref, flag_ref, g1_ref, g2_ref, w_ref, diag_ref,
                acc_ref, extra_ref, out_ref, s_ref, lt_ref):
    k = pl.program_id(0)
    first_blocks = g1_ref.shape[0] // BLK
    row_blocks = first_blocks + g2_ref.shape[0] // BLK
    col_blocks = g1_ref.shape[1] // BLK

    def rows_of(rb, cols):
        if rb < first_blocks:
            return g1_ref[rb * BLK:(rb + 1) * BLK, cols]
        return g2_ref[(rb - first_blocks) * BLK:(rb - first_blocks + 1) * BLK, cols]

    @pl.when(k == 0)
    def _():
        def fill(j, carry):
            src = src_right[j]
            c0 = pl.multiple_of(src * BLK, BLK)
            d0 = pl.multiple_of(j * BLK, BLK)
            for rb in range(row_blocks):
                live = mask_ref[rb * col_blocks + src].astype(jnp.float32)
                vals = rows_of(rb, pl.ds(c0, BLK)).astype(jnp.float32)
                wts = w_ref[rb * BLK:(rb + 1) * BLK, :]
                s_ref[rb * BLK:(rb + 1) * BLK, pl.ds(d0, BLK)] = (wts * (vals * live)).astype(jnp.bfloat16)
            return carry
        lax.fori_loop(0, col_blocks, fill, 0)

    src = src_left[k]
    c0 = pl.multiple_of(src * BLK, BLK)
    for rb in range(row_blocks):
        live = mask_ref[rb * col_blocks + src].astype(jnp.float32)
        vals = rows_of(rb, pl.ds(c0, BLK)).astype(jnp.float32) * live
        lt_ref[:, rb * BLK:(rb + 1) * BLK] = vals.T.astype(jnp.bfloat16)
    term = jnp.dot(lt_ref[...], s_ref[...], preferred_element_type=jnp.float32)
    out_ref[...] = (acc_ref[...] + extra_ref[...]) + term


def pair_rows(slab_one, slab_two, weights, live_blocks, src_left, src_right, out_tiles, diagonal, flags,
              group, acc, extra):
    height = slab_one.shape[0] + slab_two.shape[0]
    col_blocks = L // BLK
    out_blocks = src_left.shape[0]
    out_spec = pl.BlockSpec((None, BLK, L), lambda k, *_: (k // group, k % group, 0))
    grid_spec = pltpu.PrefetchScalarGridSpec(
        num_scalar_prefetch=5,
        grid=(out_blocks,),
        in_specs=[
            pl.BlockSpec(slab_one.shape, lambda k, *_: (0, 0)),
            pl.BlockSpec(slab_two.shape, lambda k, *_: (0, 0)),
            pl.BlockSpec((height, BLK), lambda k, *_: (0, 0)),
            pl.BlockSpec((col_blocks, BLK), lambda k, *_: (0, 0)),
            out_spec,
            out_spec,
        ],
        out_specs=out_spec,
        scratch_shapes=[pltpu.VMEM((height, L), jnp.bfloat16), pltpu.VMEM((BLK, height), jnp.bfloat16)],
    )
    return pl.pallas_call(
        pair_kernel,
        grid_spec=grid_spec,
        out_shape=jax.ShapeDtypeStruct((out_blocks // group, group * BLK, L), jnp.float32),
        input_output_aliases={9: 0},
        compiler_params=pltpu.CompilerParams(vmem_limit_bytes=56 * 1024 * 1024),
    )(src_left, src_right, out_tiles, live_blocks.reshape(-1), flags, slab_one, slab_two,
      weights, diagonal.reshape(col_blocks, BLK), acc, extra)


HIGHEST = lax.Precision.HIGHEST


def join_segments(earlier_seg, later_seg):
    top_one, cross_one, bottom_one = earlier_seg
    top_two, cross_two, bottom_two = later_seg
    middle = bottom_one + top_two
    middle = 0.5 * (middle + middle.T)
    factor = jnp.linalg.cholesky(middle)
    half_width = top_one.shape[0]
    solved = lax.linalg.triangular_solve(
        factor, jnp.concatenate([cross_one.T, cross_two], axis=1), left_side=True, lower=True
    )
    solve_one = solved[:, :half_width]
    solve_two = solved[:, half_width:]
    top_new = top_one - jnp.dot(solve_one.T, solve_one, precision=HIGHEST)
    cross_new = -jnp.dot(solve_one.T, solve_two, precision=HIGHEST)
    bottom_new = bottom_two - jnp.dot(solve_two.T, solve_two, precision=HIGHEST)
    return (top_new, cross_new, bottom_new)


def contract_rows(left_cols, right_cols):
    return lax.dot_general(
        left_cols, right_cols, (((0,), (0,)), ((), ())), preferred_element_type=jnp.float32
    )


def local(coupling, row_scale, block_mask, link_map, tile_order, link_diag):
    local_slab = coupling[0]
    row_weights = row_scale[0]
    live_blocks = block_mask[0]
    block_map = link_map[0]
    diagonal = link_diag[0]
    slab_height = local_slab.shape[0]
    block_count = L // BLK
    my_index = lax.axis_index("row")
    block_ids = jnp.arange(block_count, dtype=jnp.int32)
    source = jnp.sum(
        block_ids[None, :] * (block_map[None, :] == block_ids[:, None]).astype(jnp.int32), axis=1
    )

    def edge_cols(global_block):
        local_block = source[global_block]
        cols = lax.dynamic_slice_in_dim(local_slab, local_block * BLK, BLK, axis=1)
        live = lax.dynamic_index_in_dim(live_blocks, local_block, 1, False)
        cols = (cols.reshape(slab_height // BLK, BLK, BLK) * live.astype(jnp.bfloat16)[:, None, None])
        cols = cols.reshape(slab_height, BLK)
        weighted = (row_weights[:, None] * cols.astype(jnp.float32)).astype(jnp.bfloat16)
        return cols, weighted

    first_cols, first_scaled = edge_cols(0)
    final_cols, final_scaled = edge_cols(block_count - 1)
    edge_gram = contract_rows(
        jnp.concatenate([first_cols, final_cols], axis=1),
        jnp.concatenate([first_scaled, final_scaled], axis=1),
    )
    part_pieces = jnp.stack(
        [edge_gram[:BLK, :BLK], edge_gram[:BLK, BLK:], edge_gram[BLK:, BLK:]]
    )
    owners = lax.axis_size("row")
    own_blocks = block_count // owners

    def exchange(value, step):
        return lax.ppermute(value, "row", [(src, src ^ step) for src in range(owners)])

    packed_side = jnp.concatenate([row_weights, live_blocks.reshape(-1).astype(jnp.float32)])
    side_slots = jnp.zeros((owners, packed_side.shape[0]), jnp.float32)
    side_slots = lax.dynamic_update_index_in_dim(side_slots, packed_side, my_index, 0)
    piece_count = part_pieces.size
    summed_all = jnp.concatenate([part_pieces.reshape(-1), side_slots.reshape(-1)])
    if owners == 4:
        summed_all = summed_all + exchange(summed_all, 2)
        summed_all = summed_all + exchange(summed_all, 1)
    else:
        summed_all = lax.psum(summed_all, "row")
    kernel_slab, summed_all = lax.optimization_barrier((local_slab, summed_all))
    summed = summed_all[:piece_count].reshape(part_pieces.shape)
    every_side = summed_all[piece_count:].reshape(side_slots.shape)
    eye = jnp.eye(BLK, dtype=jnp.float32)
    segment = jnp.stack([
        summed[0] + eye * diagonal[:BLK][None, :],
        summed[1],
        summed[2] + eye * diagonal[L - BLK :][None, :],
    ])

    if owners == 4:
        halves = 2
        half_rows = slab_height // halves
        across_halves = [
            exchange(lax.slice_in_dim(kernel_slab, h * half_rows, (h + 1) * half_rows), 2)
            for h in range(halves)
        ]
        across_side = lax.dynamic_index_in_dim(every_side, my_index ^ 2, 0, False)
        across_weights = across_side[:slab_height]
        across_live = across_side[slab_height:].reshape(live_blocks.shape).astype(jnp.int32)
        order = jnp.concatenate(
            [lax.dynamic_slice_in_dim(tile_order, (my_index ^ q) * own_blocks, own_blocks) for q in range(2)]
        )
        flags = (jnp.arange(2 * own_blocks) < own_blocks).astype(jnp.int32)
        left_src = jnp.take(source, order)

        def own_part(slab_in):
            return split_rows(
                slab_in, row_weights, live_blocks, left_src, source, order, diagonal, flags, own_blocks,
            )

        def across_part(slab_in, partial, half):
            rows = lax.slice_in_dim(across_weights, half * half_rows, (half + 1) * half_rows)
            live = lax.slice_in_dim(
                across_live, half * (half_rows // BLK), (half + 1) * (half_rows // BLK)
            )
            return split_rows(
                slab_in, rows, live, left_src, source, order, diagonal, flags, own_blocks, partial,
            )

        partner_side = lax.dynamic_index_in_dim(every_side, my_index ^ 3, 0, False)
        partner_weights = partner_side[:slab_height]
        partner_live = partner_side[slab_height:].reshape(live_blocks.shape).astype(jnp.int32)
        last_weights = jnp.concatenate([
            lax.slice_in_dim(across_weights, half_rows, slab_height),
            lax.slice_in_dim(partner_weights, half_rows, slab_height),
        ])
        last_live = jnp.concatenate([
            lax.slice_in_dim(across_live, half_rows // BLK, slab_height // BLK),
            lax.slice_in_dim(partner_live, half_rows // BLK, slab_height // BLK),
        ])
        mine_order = order[:own_blocks]

        def last_part(slab_one, slab_two, mine, received):
            total = pair_rows(
                slab_one, slab_two, state["wide"], last_live, jnp.take(source, mine_order), source,
                mine_order, diagonal, flags[:own_blocks], own_blocks, mine[None], received[None],
            )
            return total[0]

        hooks = {2: ("across", across_halves[0]), 3: ("last", across_halves[1])}
        early_partial = own_part(local_slab)
    else:
        hooks = {}
        flags = jnp.full((block_count,), (my_index == 0).astype(jnp.int32))
        partial = gram_rows(
            kernel_slab, row_weights, live_blocks, jnp.take(source, tile_order), source,
            tile_order, diagonal, flags, own_blocks,
        )
        owned = lax.psum_scatter(
            partial.reshape(L, L), "row", scatter_dimension=0, tiled=True
        )

    times = lax.axis_size("tm")
    position = lax.axis_index("tm")
    running = (segment[0], segment[1], segment[2])
    shift = 1
    round_index = 0
    state = {}
    if owners == 4:
        state["partial"] = early_partial

    def run_hook(kind, slab_in, running):
        slab_in, running = lax.optimization_barrier((slab_in, running))
        if kind == "own":
            state["partial"] = own_part(slab_in)
        elif kind == "across":
            mine, partners = across_part(slab_in, state["partial"], 0)
            wide = jnp.broadcast_to(last_weights.reshape(-1, 1), (last_weights.shape[0], BLK))
            state["wide"], mine = lax.optimization_barrier((wide, mine))
            state["mine"] = mine
            state["received"] = exchange(partners, 1)
        else:
            state["owned"] = last_part(
                slab_in, exchange(slab_in, 1), state["mine"], state["received"]
            )
        return running

    while shift < times:
        if round_index in hooks:
            running = run_hook(*hooks.pop(round_index), running)
        round_index += 1
        pairs = [(src, src + shift) for src in range(times - shift)]
        moved = lax.ppermute(jnp.stack(running), "tm", pairs)
        earlier = (moved[0], moved[1], moved[2])
        joined = join_segments(earlier, running)
        take = position >= shift
        running = tuple(jnp.where(take, new, old) for new, old in zip(joined, running))
        shift *= 2
    for key in sorted(hooks):
        running = run_hook(*hooks[key], running)
    if "owned" in state:
        owned = state["owned"]
    chain_out = jnp.stack(running)[None]
    return (owned[None], chain_out)


def solution(mesh):
    placed = (
        P("tm", "row", None),
        P("tm", "row"),
        P("tm", "row", None),
        P("tm", None),
        P(),
        P("tm", None),
    )
    return jax.shard_map(
        local,
        mesh=mesh,
        in_specs=placed,
        out_specs=(P("tm", "row", None), P("tm", None, None, None)),
        check_vma=False,
    )
```
